32 devices in a mesh: blk: 2 (over y), req: 16 (over z, x, core).
Axes of the slice: x: 2, y: 2, z: 4, core: 2. Of those that a mesh axis runs over, the one named last changes fastest.
Arguments:
- hidden: bfloat16 [6144, 8192], P('req', 'blk'), may hold values from -120 to 120
- input_norm_gain: float32 [8192], replicated, may hold values from 0.1 to 1.9
- query_weight: bfloat16 [8192, 2048], P('req', 'blk')
- keyvalue_weight: bfloat16 [8192, 512], P('req', 'blk')
- adapter_down: bfloat16 [16, 3, 16, 8192], P('req', None, None, 'blk'), may hold values from -0.0625 to 0.0625
- adapter_up_query: bfloat16 [16, 16, 2048], P('req', None, 'blk'), may hold values from -1.5 to 1.5
- adapter_up_keyvalue: bfloat16 [16, 16, 512], P('req', None, 'blk'), may hold values from -1.5 to 1.5
- packed_lengths: int32 [16, 4], P('req'), may hold values from 1 to 192, 384 in all within a row
- prompt_adapter: int32 [16, 4], P('req'), may hold values from 0 to 15
Outputs:
- context: bfloat16 [6144, 2048], P('req', 'blk')
- key_cache: bfloat16 [6144, 256], P('req', 'blk')
- value_cache: bfloat16 [6144, 256], P('req', 'blk')
The draws below stay inside these ranges and needn't reach their ends.
Inputs may be any that keep to these rules, and one draw needn't show every extreme that they name: `packed_lengths`: each row sums to 384; the longest prompt of the whole draw has 192 tokens.
All inputs are finite; a program needn't handle non-finite values.
Results may differ from the reference program's by a relative error of at most 0.012.
The reference program's roundings to bfloat16 on the way (of `normed`, `low_rank` and `attend`) count: a program that leaves them out, or rounds other values in their place, can miss the bound.
Values may be sent and summed in bfloat16 or wider, within the bound.
No kernel may reach another device: no remote copies, remote signals or barrier semaphores. Data moves between devices by JAX's collectives and lax.ppermute only.
A program may use at most 128 MiB of HBM per device.

```python
import math
import jax
import jax.numpy as jnp
import numpy as np
from jax import lax

MODEL_WIDTH = 8192
HEAD_WIDTH = 128
QUERY_LOCAL = 8
KEYVALUE_LOCAL = 1
ADAPTER_RANK = 16
PROMPTS_PER_REQ = 4
TOKEN_SLOTS = 384
LONGEST = 192
QUERY_HEADS = 16
KEYVALUE_HEADS = 2
ADAPTER_TOTAL = 16
TOKENS = 6144
N_BLK = 2
N_REQ = 16


def draw_hidden(key, part):
    streams = jax.random.split(key, 3)
    row_scale = jnp.exp(jax.random.uniform(streams[0], (TOKENS, 1), minval=0.0, maxval=math.log(10.0)))
    column_scale = jnp.exp(jax.random.uniform(streams[1], (1, MODEL_WIDTH), minval=0.0, maxval=math.log(10.0)))
    noise = jnp.clip(jax.random.normal(streams[2], (TOKENS, MODEL_WIDTH)), -4.0, 4.0)
    result = noise * row_scale * column_scale * 0.3
    return result.astype(jnp.bfloat16)


def draw_query_weight(key, part):
    base = jnp.clip(jax.random.normal(jax.random.fold_in(key, 11), (MODEL_WIDTH, QUERY_HEADS * HEAD_WIDTH)), -6.0, 6.0) * MODEL_WIDTH ** (-0.5)
    return base.astype(jnp.bfloat16)


def draw_keyvalue_weight(key, part):
    base = jnp.clip(jax.random.normal(jax.random.fold_in(key, 12), (MODEL_WIDTH, 2 * KEYVALUE_HEADS * HEAD_WIDTH)), -6.0, 6.0) * MODEL_WIDTH ** (-0.5)
    return base.astype(jnp.bfloat16)


def plant(values, rng, low, largest):
    shape = values.shape
    spot = [jax.random.randint(jax.random.fold_in(rng, axis), (), 0, shape[axis]) for axis in range(len(shape))]
    values = values.at[tuple(spot)].set(low)
    longest = shape.index(max(shape))
    spot[longest] = (spot[longest] + 1) % shape[longest]
    return values.at[tuple(spot)].set(largest)


def steps_of(rng, shape, pieces, smallest, largest):
    gain = 1.0
    for axis_at, parts in pieces:
        heights = jax.random.uniform(jax.random.fold_in(jax.random.fold_in(rng, 6), axis_at), (parts,), jnp.float32, smallest / len(pieces), largest / len(pieces))
        gain = gain * jnp.repeat(jnp.exp(heights), shape[axis_at] // parts).reshape((-1,) + (1,) * (len(shape) - 1 - axis_at))
    return gain


def profile(count, total, limit, slope):
    loads = [(1 << 20) // math.isqrt(standing ** slope) + 1 for standing in range(2, count + 1)]
    rest, counts = total - limit - (count - 1), [1] * (count - 1)
    while rest > 0:
        candidates = [i for i in range(count - 1) if counts[i] < limit]
        pool, remaining = sum([loads[i] for i in candidates]), rest
        for i in candidates:
            more = min(limit - counts[i], max(1, remaining * loads[i] // pool), rest)
            counts[i] = counts[i] + more
            rest = rest - more
    return np.array([limit] + counts)


def uneven_parts(stream_key, count, total, bound, slope):
    if count == 2:
        one = jax.random.randint(stream_key, (), max(1, total - bound), min(bound, total - 1) + 1)
        return jnp.stack([one, total - one])
    sizes = jnp.asarray(profile(count, total, bound, slope), jnp.int32)
    twos = (count - 1) // 2
    donor, receiver = sizes[1:1 + 2 * twos:2], sizes[2:2 + 2 * twos:2]
    slack = jnp.minimum(donor - 1, bound - receiver)
    passed = jax.random.randint(jax.random.fold_in(stream_key, 1), (twos,), 0, 1 << 20) % (slack + 1)
    sizes = sizes.at[1:1 + 2 * twos:2].set(donor - passed).at[2:2 + 2 * twos:2].set(receiver + passed)
    return sizes[jax.random.permutation(jax.random.fold_in(stream_key, 2), count)]


def gaussian(own_key, extent, deviation, limit, pieces=(), kind=jnp.bfloat16):
    values = jax.random.normal(own_key, extent, jnp.float32) * deviation
    if len(pieces) > 0:
        values = steps_of(own_key, extent, pieces, -0.22, 0.18) * values
    return jnp.clip(values, min=-limit, max=limit).astype(kind)


def setup_inputs(seed: int = 0) -> dict:
    seeds = jax.random.split(jax.random.key(seed), 10)
    return {
        "hidden": draw_hidden(jax.random.fold_in(seeds[9], 71), 0),
        "input_norm_gain": jnp.clip(1.0 + 0.18 * jax.random.normal(seeds[1], (MODEL_WIDTH,), jnp.float32), 0.1, 1.9),
        "query_weight": draw_query_weight(jax.random.fold_in(seeds[9], 71), 0),
        "keyvalue_weight": draw_keyvalue_weight(jax.random.fold_in(seeds[9], 71), 0),
        "adapter_down": gaussian(seeds[4], (ADAPTER_TOTAL, 3, ADAPTER_RANK, MODEL_WIDTH), MODEL_WIDTH ** -0.5, 0.0625, ((0, 16), (3, 2))),
        "adapter_up_query": gaussian(seeds[5], (ADAPTER_TOTAL, ADAPTER_RANK, QUERY_HEADS * HEAD_WIDTH), ADAPTER_RANK ** -0.5, 1.5, ((0, 16), (2, 2))),
        "adapter_up_keyvalue": gaussian(seeds[6], (ADAPTER_TOTAL, ADAPTER_RANK, 2 * KEYVALUE_HEADS * HEAD_WIDTH), ADAPTER_RANK ** -0.5, 1.5, ((0, 16), (2, 2))),
        "packed_lengths": jax.vmap(lambda own: uneven_parts(own, PROMPTS_PER_REQ, TOKEN_SLOTS, LONGEST, 2))(jax.random.split(seeds[7], N_REQ)).reshape((N_REQ, PROMPTS_PER_REQ)).astype(jnp.int32),
        "prompt_adapter": plant(jax.random.randint(seeds[8], (N_REQ, PROMPTS_PER_REQ), 0, ADAPTER_TOTAL), jax.random.fold_in(seeds[8], 1), 0, ADAPTER_TOTAL - 1).astype(jnp.int32),
    }


epsilon = 1e-05
adapter_scale = 2.0
rope_base = 10000.0

def apply_rotation(vectors, cosine_table, sine_table):
    half_size = vectors.shape[-1] // 2
    first_half = vectors[..., :half_size]
    second_half = vectors[..., half_size:]
    turned = jnp.concatenate([-second_half, first_half], axis=-1)
    return vectors * cosine_table + turned * sine_table

def layout(lengths, count):
    slot_index = jnp.arange(count, dtype=jnp.int32)
    prompt_ends = jnp.cumsum(lengths).astype(jnp.int32)
    prompt_starts = (prompt_ends - lengths).astype(jnp.int32)
    member = (slot_index[:, None] >= prompt_starts[None, :]) & (slot_index[:, None] < prompt_ends[None, :])
    position = lax.optimization_barrier(jnp.sum(jnp.where(member, slot_index[:, None] - prompt_starts[None, :], 0), axis=1)).astype(jnp.int32)
    owner = lax.optimization_barrier(jnp.sum((slot_index[:, None] >= prompt_ends[None, :]).astype(jnp.int32), axis=1)).astype(jnp.int32)
    return (member.astype(jnp.float32), position, owner, slot_index)

def rope_tables(position, head_size):
    frequency = rope_base ** (-(jnp.arange(head_size // 2, dtype=jnp.float32) * 2.0 / head_size))
    angles = position.astype(jnp.float32)[:, None] * frequency[None, :]
    cosine_table = jnp.cos(angles)
    sine_table = jnp.sin(angles)
    return (jnp.concatenate([cosine_table, cosine_table], 1)[:, None, :], jnp.concatenate([sine_table, sine_table], 1)[:, None, :])

def attention(query_states, key_vectors, value_vectors, owner, slot_index):
    scores = jnp.einsum('tkgc,skc->kgts', query_states.astype(jnp.float32), key_vectors.astype(jnp.float32))
    scores = scores / math.sqrt(HEAD_WIDTH)
    allowed = (owner[:, None] == owner[None, :]) & (slot_index[None, :] <= slot_index[:, None])
    scores = jnp.where(allowed[None, None], scores, -1e+30)
    row_max = lax.optimization_barrier(jnp.max(scores, axis=-1, keepdims=True))
    exponent = jnp.exp(scores - row_max)
    attend = (exponent / lax.optimization_barrier(jnp.sum(exponent, axis=-1, keepdims=True))).astype(jnp.bfloat16)
    return jnp.einsum('kgts,skc->tkgc', attend.astype(jnp.float32), value_vectors.astype(jnp.float32))

def reference(hidden, input_norm_gain, query_weight, keyvalue_weight, adapter_down, adapter_up_query, adapter_up_keyvalue, packed_lengths, prompt_adapter):
    keyvalue_heads = KEYVALUE_LOCAL * N_BLK
    query_head_rows = QUERY_LOCAL * N_BLK

    def one_group(group_data):
        row_block, lengths, picked_adapter = group_data
        member, position, owner, slot_index = layout(lengths, TOKEN_SLOTS)
        values = row_block.astype(jnp.float32)
        mean_square = lax.optimization_barrier(jnp.mean(values * values, axis=1, keepdims=True))
        normed = (values * lax.rsqrt(mean_square + epsilon) * input_norm_gain[None, :]).astype(jnp.bfloat16)
        query_plain = jnp.dot(normed, query_weight, preferred_element_type=jnp.float32)
        base_pair = jnp.dot(normed, keyvalue_weight, preferred_element_type=jnp.float32)
        down_selected = adapter_down[picked_adapter].astype(jnp.float32)
        rank_all = jnp.einsum('td,pjrd->tpjr', normed.astype(jnp.float32), down_selected)
        low_rank = lax.optimization_barrier(jnp.sum(rank_all * member[:, :, None, None], axis=1)).astype(jnp.bfloat16)
        low_rank = lax.optimization_barrier(low_rank).astype(jnp.float32)
        up_query_selected = adapter_up_query[picked_adapter].astype(jnp.float32)
        query_update = lax.optimization_barrier(jnp.sum(jnp.einsum('tr,prc->tpc', low_rank[:, 0], up_query_selected) * member[:, :, None], axis=1))
        up_keyvalue_selected = adapter_up_keyvalue[picked_adapter].astype(jnp.float32).reshape(PROMPTS_PER_REQ, ADAPTER_RANK, keyvalue_heads, 2, HEAD_WIDTH)
        key_update = lax.optimization_barrier(jnp.sum(jnp.einsum('tr,prhc->tphc', low_rank[:, 1], up_keyvalue_selected[:, :, :, 0]) * member[:, :, None, None], axis=1))
        value_update = lax.optimization_barrier(jnp.sum(jnp.einsum('tr,prhc->tphc', low_rank[:, 2], up_keyvalue_selected[:, :, :, 1]) * member[:, :, None, None], axis=1))
        cosine_table, sine_table = rope_tables(position, HEAD_WIDTH)
        query_complete = query_plain.reshape(TOKEN_SLOTS, query_head_rows, HEAD_WIDTH) + adapter_scale * query_update.reshape(TOKEN_SLOTS, query_head_rows, HEAD_WIDTH)
        query_states = apply_rotation(query_complete, cosine_table, sine_table).astype(jnp.bfloat16)
        keyvalue_plain = base_pair.reshape(TOKEN_SLOTS, keyvalue_heads, 2, HEAD_WIDTH)
        key_vectors = apply_rotation(keyvalue_plain[:, :, 0] + adapter_scale * key_update, cosine_table, sine_table).astype(jnp.bfloat16)
        value_vectors = (keyvalue_plain[:, :, 1] + adapter_scale * value_update).astype(jnp.bfloat16)
        grouped = query_states.reshape(TOKEN_SLOTS, keyvalue_heads, QUERY_LOCAL, HEAD_WIDTH)
        context = attention(grouped, key_vectors, value_vectors, owner, slot_index).astype(jnp.bfloat16)
        return (context.reshape(TOKEN_SLOTS, query_head_rows * HEAD_WIDTH), key_vectors.reshape(TOKEN_SLOTS, keyvalue_heads * HEAD_WIDTH), value_vectors.reshape(TOKEN_SLOTS, keyvalue_heads * HEAD_WIDTH))
    context, key_cache, value_cache = lax.map(one_group, (hidden.reshape(N_REQ, TOKEN_SLOTS, MODEL_WIDTH), packed_lengths, prompt_adapter))
    return (context.reshape(N_REQ * TOKEN_SLOTS, query_head_rows * HEAD_WIDTH), key_cache.reshape(N_REQ * TOKEN_SLOTS, keyvalue_heads * HEAD_WIDTH), value_cache.reshape(N_REQ * TOKEN_SLOTS, keyvalue_heads * HEAD_WIDTH))
```

```python
import math

import jax
import jax.numpy as jnp
from jax import lax
from jax.sharding import Mesh
from jax.sharding import PartitionSpec as P

HEAD_WIDTH = 128
QUERY_LOCAL = 8
KEYVALUE_LOCAL = 1


epsilon = 1e-05
adapter_scale = 2.0
rope_base = 10000.0


def apply_rotation(vectors, cosine_table, sine_table):
    half_size = vectors.shape[-1] // 2
    first_half = vectors[..., :half_size]
    second_half = vectors[..., half_size:]
    turned = jnp.concatenate([-second_half, first_half], axis=-1)
    return vectors * cosine_table + turned * sine_table


def layout(lengths, count):
    slot_index = jnp.arange(count, dtype=jnp.int32)
    prompt_ends = jnp.cumsum(lengths)
    prompt_starts = prompt_ends - lengths
    member = (slot_index[:, None] >= prompt_starts[None, :]) & (
        slot_index[:, None] < prompt_ends[None, :]
    )
    position = jnp.sum(jnp.where(member, slot_index[:, None] - prompt_starts[None, :], 0), axis=1)
    owner = jnp.sum((slot_index[:, None] >= prompt_ends[None, :]).astype(jnp.int32), axis=1)
    return (member.astype(jnp.float32), position, owner, slot_index)


def rope_tables(position, head_size):
    frequency = rope_base ** (-(jnp.arange(head_size // 2, dtype=jnp.float32) * 2.0 / head_size))
    angles = position.astype(jnp.float32)[:, None] * frequency[None, :]
    cosine_table = jnp.cos(angles)
    sine_table = jnp.sin(angles)
    return (
        jnp.concatenate([cosine_table, cosine_table], 1)[:, None, :],
        jnp.concatenate([sine_table, sine_table], 1)[:, None, :],
    )


def gather_blk(piece, n_blk):
    me = lax.axis_index("blk")
    received = [piece]
    for shift in range(1, n_blk):
        pairs = [(i, (i + shift) % n_blk) for i in range(n_blk)]
        received.append(lax.ppermute(piece, "blk", pairs))
    ordered = []
    for source in range(n_blk):
        pick = (me - source) % n_blk
        ordered.append(lax.switch(pick, [lambda s=s: received[s] for s in range(n_blk)]))
    return ordered


def sum_blk(piece, n_blk):
    if n_blk == 2:
        return piece + lax.ppermute(piece, "blk", [(0, 1), (1, 0)])
    return lax.psum(piece, "blk")


def gather_req(piece):
    stacked = lax.all_gather(piece, "chip", axis=0, tiled=False)
    return lax.all_gather(stacked, "core", axis=0, tiled=False)


def shards(
    hidden,
    input_norm_gain,
    query_weight,
    keyvalue_weight,
    adapter_down,
    adapter_up_query,
    adapter_up_keyvalue,
    packed_lengths,
    prompt_adapter,
):
    n_blk = lax.axis_size("blk")
    n_lo = lax.axis_size("core")
    n_chip = lax.axis_size("chip")
    row_number, feature_cols = hidden.shape
    full_width = feature_cols * n_blk
    me_blk = lax.axis_index("blk")

    if n_blk == 2:
        other = lax.ppermute(hidden, "blk", [(0, 1), (1, 0)])
        halves = [lax.select(me_blk == 0, hidden, other), lax.select(me_blk == 0, other, hidden)]
    else:
        halves = gather_blk(hidden, n_blk)
    full_hidden = jnp.concatenate(halves, axis=1)
    values = full_hidden.astype(jnp.float32)
    squares = jnp.sum(values * values, axis=1)
    factor = lax.rsqrt(squares / full_width + epsilon)
    normed = (values * factor[:, None] * input_norm_gain[None, :]).astype(jnp.bfloat16)
    normed_part = lax.dynamic_slice_in_dim(normed, me_blk * feature_cols, feature_cols, 1)

    weight_rows = query_weight.shape[0]
    query_cols = query_weight.shape[1]
    pair_cols = keyvalue_weight.shape[1]
    query_all = gather_req(query_weight)
    pair_all = gather_req(keyvalue_weight)
    normed_blocks = normed.reshape(row_number, n_chip, n_lo, weight_rows)

    def project(weight_all, cols):
        total = None
        for c in range(n_lo):
            lhs = normed_blocks[:, :, c, :].reshape(row_number, n_chip * weight_rows)
            rhs = weight_all[c].reshape(n_chip * weight_rows, cols)
            part = jnp.dot(lhs, rhs, preferred_element_type=jnp.float32)
            total = part if total is None else total + part
        return total

    down_size = adapter_down[0].size
    upq_size = adapter_up_query[0].size
    flat = jnp.concatenate(
        [
            adapter_down.reshape(-1),
            adapter_up_query.reshape(-1),
            adapter_up_keyvalue.reshape(-1),
        ]
    )
    adapters_all = gather_req(flat)
    picked = prompt_adapter[0]
    chosen = adapters_all[picked % n_lo, picked // n_lo]
    prompt_count = picked.shape[0]
    down_selected = chosen[:, :down_size].reshape((prompt_count,) + adapter_down.shape[1:])
    up_query_selected = chosen[:, down_size : down_size + upq_size].reshape(
        (prompt_count,) + adapter_up_query.shape[1:]
    )
    up_pair_selected = chosen[:, down_size + upq_size :].reshape(
        (prompt_count,) + adapter_up_keyvalue.shape[1:]
    )

    base_pair = project(pair_all, pair_cols)
    query_plain = project(query_all, query_cols)

    lengths = packed_lengths[0]
    member, position, owner, slot_index = layout(lengths, row_number)
    rank_size = down_selected.shape[2]
    partial_value = lax.dot_general(
        normed_part,
        down_selected.reshape(prompt_count * 3 * rank_size, feature_cols),
        (((1,), (1,)), ((), ())),
        preferred_element_type=jnp.float32,
    )
    partial_value = partial_value.reshape(row_number, prompt_count, 3, rank_size)
    masked = jnp.sum(partial_value * member[:, :, None, None], axis=1).reshape(
        row_number, 3 * rank_size
    )
    low_rank = sum_blk(masked, n_blk).reshape(row_number, 3, rank_size).astype(jnp.bfloat16)
    low_float = low_rank.astype(jnp.float32)

    def spread(column):
        return (
            (member[:, :, None] * low_float[:, None, column, :])
            .astype(jnp.bfloat16)
            .reshape(row_number, prompt_count * rank_size)
        )

    up_keyvalue_selected = up_pair_selected.reshape(
        prompt_count, rank_size, KEYVALUE_LOCAL, 2, HEAD_WIDTH
    )
    query_update = jnp.dot(
        spread(0),
        up_query_selected.reshape(prompt_count * rank_size, query_cols),
        preferred_element_type=jnp.float32,
    )
    key_update = jnp.dot(
        spread(1),
        up_keyvalue_selected[:, :, :, 0].reshape(
            prompt_count * rank_size, KEYVALUE_LOCAL * HEAD_WIDTH
        ),
        preferred_element_type=jnp.float32,
    )
    value_update = jnp.dot(
        spread(2),
        up_keyvalue_selected[:, :, :, 1].reshape(
            prompt_count * rank_size, KEYVALUE_LOCAL * HEAD_WIDTH
        ),
        preferred_element_type=jnp.float32,
    )
    cosine_table, sine_table = rope_tables(position, HEAD_WIDTH)
    query_complete = (query_plain + adapter_scale * query_update).reshape(
        row_number, QUERY_LOCAL * KEYVALUE_LOCAL, HEAD_WIDTH
    )
    query_states = apply_rotation(query_complete, cosine_table, sine_table).astype(jnp.bfloat16)
    keyvalue_plain = base_pair.reshape(row_number, KEYVALUE_LOCAL, 2, HEAD_WIDTH)
    key_vectors = apply_rotation(
        keyvalue_plain[:, :, 0]
        + adapter_scale * key_update.reshape(row_number, KEYVALUE_LOCAL, HEAD_WIDTH),
        cosine_table,
        sine_table,
    ).astype(jnp.bfloat16)
    value_vectors = (
        keyvalue_plain[:, :, 1]
        + adapter_scale * value_update.reshape(row_number, KEYVALUE_LOCAL, HEAD_WIDTH)
    ).astype(jnp.bfloat16)
    grouped = query_states.reshape(row_number, KEYVALUE_LOCAL, QUERY_LOCAL, HEAD_WIDTH)
    scores = jnp.einsum(
        "tkgc,skc->kgts", grouped, key_vectors, preferred_element_type=jnp.float32
    ) / math.sqrt(HEAD_WIDTH)
    allowed = (owner[:, None] == owner[None, :]) & (slot_index[None, :] <= slot_index[:, None])
    scores = jnp.where(allowed[None, None], scores, -1e30)
    row_max = jnp.max(scores, axis=-1, keepdims=True)
    exponent = jnp.exp(scores - row_max)
    attend = (exponent / jnp.sum(exponent, axis=-1, keepdims=True)).astype(jnp.bfloat16)
    context = jnp.einsum(
        "kgts,skc->tkgc", attend, value_vectors, preferred_element_type=jnp.float32
    ).astype(jnp.bfloat16)
    return (
        context.reshape(row_number, KEYVALUE_LOCAL * QUERY_LOCAL * HEAD_WIDTH),
        key_vectors.reshape(row_number, KEYVALUE_LOCAL * HEAD_WIDTH),
        value_vectors.reshape(row_number, KEYVALUE_LOCAL * HEAD_WIDTH),
    )


def solution(mesh):
    n_blk = mesh.shape["blk"]
    n_req = mesh.shape["req"]
    n_lo = 2 if n_req % 2 == 0 else 1
    devices = mesh.devices.reshape(n_blk, n_req // n_lo, n_lo)
    split_mesh = Mesh(devices, ("blk", "chip", "core"))
    req = ("chip", "core")
    in_specs = (
        P(req, "blk"),
        P(),
        P(req, "blk"),
        P(req, "blk"),
        P(req, None, None, "blk"),
        P(req, None, "blk"),
        P(req, None, "blk"),
        P(req, None),
        P(req, None),
    )
    out_specs = (P(req, "blk"), P(req, "blk"), P(req, "blk"))
    return jax.shard_map(
        shards, mesh=split_mesh, in_specs=in_specs, out_specs=out_specs, check_vma=False
    )
```

```python
import math

import jax
import jax.numpy as jnp
from jax import lax
from jax.sharding import Mesh
from jax.sharding import PartitionSpec as P

HEAD_WIDTH = 128
QUERY_LOCAL = 8
KEYVALUE_LOCAL = 1


epsilon = 1e-05
adapter_scale = 2.0
rope_base = 10000.0


def apply_rotation(vectors, cosine_table, sine_table):
    half_size = vectors.shape[-1] // 2
    first_half = vectors[..., :half_size]
    second_half = vectors[..., half_size:]
    turned = jnp.concatenate([-second_half, first_half], axis=-1)
    return vectors * cosine_table + turned * sine_table


def layout(lengths, count):
    slot_index = jnp.arange(count, dtype=jnp.int32)
    prompt_ends = jnp.cumsum(lengths)
    prompt_starts = prompt_ends - lengths
    member = (slot_index[:, None] >= prompt_starts[None, :]) & (
        slot_index[:, None] < prompt_ends[None, :]
    )
    position = jnp.sum(jnp.where(member, slot_index[:, None] - prompt_starts[None, :], 0), axis=1)
    owner = jnp.sum((slot_index[:, None] >= prompt_ends[None, :]).astype(jnp.int32), axis=1)
    return (member.astype(jnp.float32), position, owner, slot_index)


def rope_tables(position, head_size):
    frequency = rope_base ** (-(jnp.arange(head_size // 2, dtype=jnp.float32) * 2.0 / head_size))
    angles = position.astype(jnp.float32)[:, None] * frequency[None, :]
    cosine_table = jnp.cos(angles)
    sine_table = jnp.sin(angles)
    return (
        jnp.concatenate([cosine_table, cosine_table], 1)[:, None, :],
        jnp.concatenate([sine_table, sine_table], 1)[:, None, :],
    )


def gather_blk(piece, n_blk):
    me = lax.axis_index("blk")
    received = [piece]
    for shift in range(1, n_blk):
        pairs = [(i, (i + shift) % n_blk) for i in range(n_blk)]
        received.append(lax.ppermute(piece, "blk", pairs))
    ordered = []
    for source in range(n_blk):
        pick = (me - source) % n_blk
        ordered.append(lax.switch(pick, [lambda s=s: received[s] for s in range(n_blk)]))
    return ordered


def sum_blk(piece, n_blk):
    if n_blk == 2:
        return piece + lax.ppermute(piece, "blk", [(0, 1), (1, 0)])
    return lax.psum(piece, "blk")


def ring_order(count):
    if count % 2 == 0 and count > 2:
        return list(range(0, count, 2)) + list(range(count - 1, 0, -2))
    return list(range(count))


def ring_gather(piece, count, order, direction):
    pairs = [(order[i], order[(i + direction) % count]) for i in range(count)]
    received = [piece]
    current = piece
    for _ in range(count - 1):
        current = lax.ppermute(current, "chip", pairs)
        received.append(current)
    return received


def shards(
    hidden,
    input_norm_gain,
    query_weight,
    keyvalue_weight,
    adapter_down,
    adapter_up_query,
    adapter_up_keyvalue,
    packed_lengths,
    prompt_adapter,
):
    n_blk = lax.axis_size("blk")
    n_lo = lax.axis_size("core")
    n_chip = lax.axis_size("chip")
    row_number, feature_cols = hidden.shape
    full_width = feature_cols * n_blk
    me_blk = lax.axis_index("blk")
    me_core = lax.axis_index("core")
    me_chip = lax.axis_index("chip")

    if n_blk == 2:
        other = lax.ppermute(hidden, "blk", [(0, 1), (1, 0)])
        halves = [lax.select(me_blk == 0, hidden, other), lax.select(me_blk == 0, other, hidden)]
    else:
        halves = gather_blk(hidden, n_blk)
    full_hidden = jnp.concatenate(halves, axis=1)
    values = full_hidden.astype(jnp.float32)
    squares = jnp.sum(values * values, axis=1)
    factor = lax.rsqrt(squares / full_width + epsilon)
    normed = (values * factor[:, None] * input_norm_gain[None, :]).astype(jnp.bfloat16)
    normed_part = lax.dynamic_slice_in_dim(normed, me_blk * feature_cols, feature_cols, 1)

    weight_rows = query_weight.shape[0]
    query_cols = query_weight.shape[1]
    pair_cols = keyvalue_weight.shape[1]
    half_rows = weight_rows // 2

    weights = jnp.concatenate([query_weight, keyvalue_weight], axis=1)
    down_rows = adapter_down.size // query_cols
    upq_rows = adapter_up_query.size // query_cols
    upkv_rows = adapter_up_keyvalue.size // query_cols
    down_flat = adapter_down.reshape(down_rows, query_cols)
    upq_flat = adapter_up_query.reshape(upq_rows, query_cols)
    upkv_flat = adapter_up_keyvalue.reshape(upkv_rows, query_cols)
    dh, uh, vh = down_rows // 2, upq_rows // 2, upkv_rows // 2
    piece_rows = dh + uh + vh
    pad_rows = (-piece_rows) % 8

    def adapter_half(h):
        return jnp.concatenate(
            [
                down_flat[h * dh : (h + 1) * dh],
                upq_flat[h * uh : (h + 1) * uh],
                upkv_flat[h * vh : (h + 1) * vh],
                jnp.zeros((pad_rows, query_cols), jnp.bfloat16),
            ]
        )

    order = ring_order(n_chip)
    inverse = [0] * n_chip
    for i, c in enumerate(order):
        inverse[c] = i
    order_table = jnp.asarray(order, jnp.int32)
    inverse_table = jnp.asarray(inverse, jnp.int32)
    pos = inverse_table[me_chip]
    directions = (1, -1)

    def swap_core(x):
        if n_lo == 1:
            return [x]
        return [x, lax.ppermute(x, "core", [(0, 1), (1, 0)])]

    total = None
    adapter_pieces = []
    for h, direction in enumerate(directions):
        w_recv = ring_gather(weights[h * half_rows : (h + 1) * half_rows], n_chip, order, direction)
        a_recv = ring_gather(adapter_half(h), n_chip, order, direction)
        a_steps = []
        for s in range(n_chip):
            src_chip = order_table[(pos - s * direction) % n_chip]
            w_both = swap_core(w_recv[s])
            a_steps.append(jnp.stack(swap_core(a_recv[s])))
            for slot, w_piece in enumerate(w_both):
                src_core = me_core if slot == 0 else n_lo - 1 - me_core
                start = (src_chip * n_lo + src_core) * weight_rows + h * half_rows
                lhs = lax.dynamic_slice_in_dim(normed, start, half_rows, 1)
                part = jnp.dot(lhs, w_piece, preferred_element_type=jnp.float32)
                total = part if total is None else total + part
        adapter_pieces.append(jnp.stack(a_steps))

    picked = prompt_adapter[0]
    prompt_count = picked.shape[0]
    a_chip = picked // n_lo
    a_core = picked % n_lo
    a_slot = (a_core != me_core).astype(jnp.int32)
    per_half = []
    for h, direction in enumerate(directions):
        a_step = ((pos - inverse_table[a_chip]) * direction) % n_chip
        per_half.append(adapter_pieces[h][a_step, a_slot])
    down_selected = jnp.concatenate(
        [per_half[0][:, :dh], per_half[1][:, :dh]], axis=1
    ).reshape((prompt_count,) + adapter_down.shape[1:])
    up_query_selected = jnp.concatenate(
        [per_half[0][:, dh : dh + uh], per_half[1][:, dh : dh + uh]], axis=1
    ).reshape((prompt_count,) + adapter_up_query.shape[1:])
    up_pair_selected = jnp.concatenate(
        [per_half[0][:, dh + uh : piece_rows], per_half[1][:, dh + uh : piece_rows]], axis=1
    ).reshape((prompt_count,) + adapter_up_keyvalue.shape[1:])

    query_plain = total[:, :query_cols]
    base_pair = total[:, query_cols:]

    lengths = packed_lengths[0]
    member, position, owner, slot_index = layout(lengths, row_number)
    rank_size = down_selected.shape[2]
    partial_value = lax.dot_general(
        normed_part,
        down_selected.reshape(prompt_count * 3 * rank_size, feature_cols),
        (((1,), (1,)), ((), ())),
        preferred_element_type=jnp.float32,
    )
    partial_value = partial_value.reshape(row_number, prompt_count, 3, rank_size)
    masked = jnp.sum(partial_value * member[:, :, None, None], axis=1).reshape(
        row_number, 3 * rank_size
    )
    low_rank = sum_blk(masked, n_blk).reshape(row_number, 3, rank_size).astype(jnp.bfloat16)
    low_float = low_rank.astype(jnp.float32)

    def spread(column):
        return (
            (member[:, :, None] * low_float[:, None, column, :])
            .astype(jnp.bfloat16)
            .reshape(row_number, prompt_count * rank_size)
        )

    up_keyvalue_selected = up_pair_selected.reshape(
        prompt_count, rank_size, KEYVALUE_LOCAL, 2, HEAD_WIDTH
    )
    query_update = jnp.dot(
        spread(0),
        up_query_selected.reshape(prompt_count * rank_size, query_cols),
        preferred_element_type=jnp.float32,
    )
    key_update = jnp.dot(
        spread(1),
        up_keyvalue_selected[:, :, :, 0].reshape(
            prompt_count * rank_size, KEYVALUE_LOCAL * HEAD_WIDTH
        ),
        preferred_element_type=jnp.float32,
    )
    value_update = jnp.dot(
        spread(2),
        up_keyvalue_selected[:, :, :, 1].reshape(
            prompt_count * rank_size, KEYVALUE_LOCAL * HEAD_WIDTH
        ),
        preferred_element_type=jnp.float32,
    )
    cosine_table, sine_table = rope_tables(position, HEAD_WIDTH)
    query_complete = (query_plain + adapter_scale * query_update).reshape(
        row_number, QUERY_LOCAL * KEYVALUE_LOCAL, HEAD_WIDTH
    )
    query_states = apply_rotation(query_complete, cosine_table, sine_table).astype(jnp.bfloat16)
    keyvalue_plain = base_pair.reshape(row_number, KEYVALUE_LOCAL, 2, HEAD_WIDTH)
    key_vectors = apply_rotation(
        keyvalue_plain[:, :, 0]
        + adapter_scale * key_update.reshape(row_number, KEYVALUE_LOCAL, HEAD_WIDTH),
        cosine_table,
        sine_table,
    ).astype(jnp.bfloat16)
    value_vectors = (
        keyvalue_plain[:, :, 1]
        + adapter_scale * value_update.reshape(row_number, KEYVALUE_LOCAL, HEAD_WIDTH)
    ).astype(jnp.bfloat16)
    grouped = query_states.reshape(row_number, KEYVALUE_LOCAL, QUERY_LOCAL, HEAD_WIDTH)
    scores = jnp.einsum(
        "tkgc,skc->kgts", grouped, key_vectors, preferred_element_type=jnp.float32
    ) / math.sqrt(HEAD_WIDTH)
    allowed = (owner[:, None] == owner[None, :]) & (slot_index[None, :] <= slot_index[:, None])
    scores = jnp.where(allowed[None, None], scores, -1e30)
    row_max = jnp.max(scores, axis=-1, keepdims=True)
    exponent = jnp.exp(scores - row_max)
    attend = (exponent / jnp.sum(exponent, axis=-1, keepdims=True)).astype(jnp.bfloat16)
    context = jnp.einsum(
        "kgts,skc->tkgc", attend, value_vectors, preferred_element_type=jnp.float32
    ).astype(jnp.bfloat16)
    return (
        context.reshape(row_number, KEYVALUE_LOCAL * QUERY_LOCAL * HEAD_WIDTH),
        key_vectors.reshape(row_number, KEYVALUE_LOCAL * HEAD_WIDTH),
        value_vectors.reshape(row_number, KEYVALUE_LOCAL * HEAD_WIDTH),
    )


def solution(mesh):
    n_blk = mesh.shape["blk"]
    n_req = mesh.shape["req"]
    n_lo = 2 if n_req % 2 == 0 else 1
    devices = mesh.devices.reshape(n_blk, n_req // n_lo, n_lo)
    split_mesh = Mesh(devices, ("blk", "chip", "core"))
    req = ("chip", "core")
    in_specs = (
        P(req, "blk"),
        P(),
        P(req, "blk"),
        P(req, "blk"),
        P(req, None, None, "blk"),
        P(req, None, "blk"),
        P(req, None, "blk"),
        P(req, None),
        P(req, None),
    )
    out_specs = (P(req, "blk"), P(req, "blk"), P(req, "blk"))
    return jax.shard_map(
        shards, mesh=split_mesh, in_specs=in_specs, out_specs=out_specs, check_vma=False
    )
```

```python
import math

import jax
import jax.numpy as jnp
from jax import lax
from jax.sharding import Mesh
from jax.sharding import PartitionSpec as P

HEAD_WIDTH = 128
QUERY_LOCAL = 8
KEYVALUE_LOCAL = 1


epsilon = 1e-05
adapter_scale = 2.0
rope_base = 10000.0


def apply_rotation(vectors, cosine_table, sine_table):
    half_size = vectors.shape[-1] // 2
    first_half = vectors[..., :half_size]
    second_half = vectors[..., half_size:]
    turned = jnp.concatenate([-second_half, first_half], axis=-1)
    return vectors * cosine_table + turned * sine_table


def layout(lengths, count):
    slot_index = jnp.arange(count, dtype=jnp.int32)
    prompt_ends = jnp.cumsum(lengths)
    prompt_starts = prompt_ends - lengths
    member = (slot_index[:, None] >= prompt_starts[None, :]) & (
        slot_index[:, None] < prompt_ends[None, :]
    )
    position = jnp.sum(jnp.where(member, slot_index[:, None] - prompt_starts[None, :], 0), axis=1)
    owner = jnp.sum((slot_index[:, None] >= prompt_ends[None, :]).astype(jnp.int32), axis=1)
    return (member.astype(jnp.float32), position, owner, slot_index)


def rope_tables(position, head_size):
    frequency = rope_base ** (-(jnp.arange(head_size // 2, dtype=jnp.float32) * 2.0 / head_size))
    angles = position.astype(jnp.float32)[:, None] * frequency[None, :]
    cosine_table = jnp.cos(angles)
    sine_table = jnp.sin(angles)
    return (
        jnp.concatenate([cosine_table, cosine_table], 1)[:, None, :],
        jnp.concatenate([sine_table, sine_table], 1)[:, None, :],
    )


def gather_blk(piece, n_blk):
    me = lax.axis_index("blk")
    received = [piece]
    for shift in range(1, n_blk):
        pairs = [(i, (i + shift) % n_blk) for i in range(n_blk)]
        received.append(lax.ppermute(piece, "blk", pairs))
    ordered = []
    for source in range(n_blk):
        pick = (me - source) % n_blk
        ordered.append(lax.switch(pick, [lambda s=s: received[s] for s in range(n_blk)]))
    return ordered


def sum_blk(piece, n_blk):
    if n_blk == 2:
        return piece + lax.ppermute(piece, "blk", [(0, 1), (1, 0)])
    return lax.psum(piece, "blk")


def ring_order(count):
    if count % 2 == 0 and count > 2:
        return list(range(0, count, 2)) + list(range(count - 1, 0, -2))
    return list(range(count))


def ring_gather(piece, count, order, direction):
    pairs = [(order[i], order[(i + direction) % count]) for i in range(count)]
    received = [piece]
    current = piece
    for _ in range(count - 1):
        current = lax.ppermute(current, "chip", pairs)
        received.append(current)
    return received


def shards(
    hidden,
    input_norm_gain,
    query_weight,
    keyvalue_weight,
    adapter_down,
    adapter_up_query,
    adapter_up_keyvalue,
    packed_lengths,
    prompt_adapter,
):
    n_blk = lax.axis_size("blk")
    n_lo = lax.axis_size("core")
    n_chip = lax.axis_size("chip")
    row_number, feature_cols = hidden.shape
    full_width = feature_cols * n_blk
    me_blk = lax.axis_index("blk")
    me_core = lax.axis_index("core")
    me_chip = lax.axis_index("chip")

    if n_blk == 2:
        other = lax.ppermute(hidden, "blk", [(0, 1), (1, 0)])
        halves = [lax.select(me_blk == 0, hidden, other), lax.select(me_blk == 0, other, hidden)]
    else:
        halves = gather_blk(hidden, n_blk)
    full_hidden = jnp.concatenate(halves, axis=1)
    values = full_hidden.astype(jnp.float32)
    squares = jnp.sum(values * values, axis=1)
    factor = lax.rsqrt(squares / full_width + epsilon)
    normed = (values * factor[:, None] * input_norm_gain[None, :]).astype(jnp.bfloat16)
    normed_part = lax.dynamic_slice_in_dim(normed, me_blk * feature_cols, feature_cols, 1)

    weight_rows = query_weight.shape[0]
    query_cols = query_weight.shape[1]
    pair_cols = keyvalue_weight.shape[1]
    half_rows = weight_rows // 2

    weights = jnp.concatenate([query_weight, keyvalue_weight], axis=1)
    down_rows = adapter_down.size // query_cols
    upq_rows = adapter_up_query.size // query_cols
    upkv_rows = adapter_up_keyvalue.size // query_cols
    down_flat = adapter_down.reshape(down_rows, query_cols)
    upq_flat = adapter_up_query.reshape(upq_rows, query_cols)
    upkv_flat = adapter_up_keyvalue.reshape(upkv_rows, query_cols)
    dh, uh, vh = down_rows // 2, upq_rows // 2, upkv_rows // 2
    piece_rows = dh + uh + vh
    pad_rows = (-piece_rows) % 8

    def adapter_half(h):
        return jnp.concatenate(
            [
                down_flat[h * dh : (h + 1) * dh],
                upq_flat[h * uh : (h + 1) * uh],
                upkv_flat[h * vh : (h + 1) * vh],
                jnp.zeros((pad_rows, query_cols), jnp.bfloat16),
            ]
        )

    order = ring_order(n_chip)
    inverse = [0] * n_chip
    for i, c in enumerate(order):
        inverse[c] = i
    order_table = jnp.asarray(order, jnp.int32)
    inverse_table = jnp.asarray(inverse, jnp.int32)
    pos = inverse_table[me_chip]
    directions = (1, -1)

    def swap_core(x):
        if n_lo == 1:
            return [x]
        return [x, lax.ppermute(x, "core", [(0, 1), (1, 0)])]

    pair_width = query_cols + pair_cols
    recv = []
    for h, direction in enumerate(directions):
        adapters_padded = jnp.pad(adapter_half(h), ((0, 0), (0, pair_width - query_cols)))
        piece = jnp.concatenate(
            [weights[h * half_rows : (h + 1) * half_rows], adapters_padded], axis=0
        )
        recv.append(ring_gather(piece, n_chip, order, direction))

    total = None
    adapter_steps = [[], []]
    for s in range(n_chip):
        for h, direction in enumerate(directions):
            src_chip = order_table[(pos - s * direction) % n_chip]
            both = swap_core(recv[h][s])
            adapter_steps[h].append(jnp.stack([p[half_rows:, :query_cols] for p in both]))
            for slot, p in enumerate(both):
                src_core = me_core if slot == 0 else n_lo - 1 - me_core
                start = (src_chip * n_lo + src_core) * weight_rows + h * half_rows
                lhs = lax.dynamic_slice_in_dim(normed, start, half_rows, 1)
                part = jnp.dot(lhs, p[:half_rows], preferred_element_type=jnp.float32)
                total = part if total is None else total + part
    adapter_pieces = [jnp.stack(a) for a in adapter_steps]

    picked = prompt_adapter[0]
    prompt_count = picked.shape[0]
    a_chip = picked // n_lo
    a_core = picked % n_lo
    a_slot = (a_core != me_core).astype(jnp.int32)
    per_half = []
    for h, direction in enumerate(directions):
        a_step = ((pos - inverse_table[a_chip]) * direction) % n_chip
        per_half.append(adapter_pieces[h][a_step, a_slot])
    down_selected = jnp.concatenate(
        [per_half[0][:, :dh], per_half[1][:, :dh]], axis=1
    ).reshape((prompt_count,) + adapter_down.shape[1:])
    up_query_selected = jnp.concatenate(
        [per_half[0][:, dh : dh + uh], per_half[1][:, dh : dh + uh]], axis=1
    ).reshape((prompt_count,) + adapter_up_query.shape[1:])
    up_pair_selected = jnp.concatenate(
        [per_half[0][:, dh + uh : piece_rows], per_half[1][:, dh + uh : piece_rows]], axis=1
    ).reshape((prompt_count,) + adapter_up_keyvalue.shape[1:])

    query_plain = total[:, :query_cols]
    base_pair = total[:, query_cols:]

    lengths = packed_lengths[0]
    member, position, owner, slot_index = layout(lengths, row_number)
    rank_size = down_selected.shape[2]
    partial_value = lax.dot_general(
        normed_part,
        down_selected.reshape(prompt_count * 3 * rank_size, feature_cols),
        (((1,), (1,)), ((), ())),
        preferred_element_type=jnp.float32,
    )
    partial_value = partial_value.reshape(row_number, prompt_count, 3, rank_size)
    masked = jnp.sum(partial_value * member[:, :, None, None], axis=1).reshape(
        row_number, 3 * rank_size
    )
    low_rank = sum_blk(masked, n_blk).reshape(row_number, 3, rank_size).astype(jnp.bfloat16)
    low_float = low_rank.astype(jnp.float32)

    def spread(column):
        return (
            (member[:, :, None] * low_float[:, None, column, :])
            .astype(jnp.bfloat16)
            .reshape(row_number, prompt_count * rank_size)
        )

    up_keyvalue_selected = up_pair_selected.reshape(
        prompt_count, rank_size, KEYVALUE_LOCAL, 2, HEAD_WIDTH
    )
    query_update = jnp.dot(
        spread(0),
        up_query_selected.reshape(prompt_count * rank_size, query_cols),
        preferred_element_type=jnp.float32,
    )
    key_update = jnp.dot(
        spread(1),
        up_keyvalue_selected[:, :, :, 0].reshape(
            prompt_count * rank_size, KEYVALUE_LOCAL * HEAD_WIDTH
        ),
        preferred_element_type=jnp.float32,
    )
    value_update = jnp.dot(
        spread(2),
        up_keyvalue_selected[:, :, :, 1].reshape(
            prompt_count * rank_size, KEYVALUE_LOCAL * HEAD_WIDTH
        ),
        preferred_element_type=jnp.float32,
    )
    cosine_table, sine_table = rope_tables(position, HEAD_WIDTH)
    query_complete = (query_plain + adapter_scale * query_update).reshape(
        row_number, QUERY_LOCAL * KEYVALUE_LOCAL, HEAD_WIDTH
    )
    query_states = apply_rotation(query_complete, cosine_table, sine_table).astype(jnp.bfloat16)
    keyvalue_plain = base_pair.reshape(row_number, KEYVALUE_LOCAL, 2, HEAD_WIDTH)
    key_vectors = apply_rotation(
        keyvalue_plain[:, :, 0]
        + adapter_scale * key_update.reshape(row_number, KEYVALUE_LOCAL, HEAD_WIDTH),
        cosine_table,
        sine_table,
    ).astype(jnp.bfloat16)
    value_vectors = (
        keyvalue_plain[:, :, 1]
        + adapter_scale * value_update.reshape(row_number, KEYVALUE_LOCAL, HEAD_WIDTH)
    ).astype(jnp.bfloat16)
    grouped = query_states.reshape(row_number, KEYVALUE_LOCAL, QUERY_LOCAL, HEAD_WIDTH)
    scores = jnp.einsum(
        "tkgc,skc->kgts", grouped, key_vectors, preferred_element_type=jnp.float32
    ) / math.sqrt(HEAD_WIDTH)
    allowed = (owner[:, None] == owner[None, :]) & (slot_index[None, :] <= slot_index[:, None])
    scores = jnp.where(allowed[None, None], scores, -1e30)
    row_max = jnp.max(scores, axis=-1, keepdims=True)
    exponent = jnp.exp(scores - row_max)
    attend = (exponent / jnp.sum(exponent, axis=-1, keepdims=True)).astype(jnp.bfloat16)
    context = jnp.einsum(
        "kgts,skc->tkgc", attend, value_vectors, preferred_element_type=jnp.float32
    ).astype(jnp.bfloat16)
    return (
        context.reshape(row_number, KEYVALUE_LOCAL * QUERY_LOCAL * HEAD_WIDTH),
        key_vectors.reshape(row_number, KEYVALUE_LOCAL * HEAD_WIDTH),
        value_vectors.reshape(row_number, KEYVALUE_LOCAL * HEAD_WIDTH),
    )


def solution(mesh):
    n_blk = mesh.shape["blk"]
    n_req = mesh.shape["req"]
    n_lo = 2 if n_req % 2 == 0 else 1
    devices = mesh.devices.reshape(n_blk, n_req // n_lo, n_lo)
    split_mesh = Mesh(devices, ("blk", "chip", "core"))
    req = ("chip", "core")
    in_specs = (
        P(req, "blk"),
        P(),
        P(req, "blk"),
        P(req, "blk"),
        P(req, None, None, "blk"),
        P(req, None, "blk"),
        P(req, None, "blk"),
        P(req, None),
        P(req, None),
    )
    out_specs = (P(req, "blk"), P(req, "blk"), P(req, "blk"))
    return jax.shard_map(
        shards, mesh=split_mesh, in_specs=in_specs, out_specs=out_specs, check_vma=False
    )
```

```python
import math

import jax
import jax.numpy as jnp
from jax import lax
from jax.sharding import Mesh
from jax.sharding import PartitionSpec as P

HEAD_WIDTH = 128
QUERY_LOCAL = 8
KEYVALUE_LOCAL = 1


epsilon = 1e-05
adapter_scale = 2.0
rope_base = 10000.0


def apply_rotation(vectors, cosine_table, sine_table):
    half_size = vectors.shape[-1] // 2
    first_half = vectors[..., :half_size]
    second_half = vectors[..., half_size:]
    turned = jnp.concatenate([-second_half, first_half], axis=-1)
    return vectors * cosine_table + turned * sine_table


def layout(lengths, count):
    slot_index = jnp.arange(count, dtype=jnp.int32)
    prompt_ends = jnp.cumsum(lengths)
    prompt_starts = prompt_ends - lengths
    member = (slot_index[:, None] >= prompt_starts[None, :]) & (
        slot_index[:, None] < prompt_ends[None, :]
    )
    position = jnp.sum(jnp.where(member, slot_index[:, None] - prompt_starts[None, :], 0), axis=1)
    owner = jnp.sum((slot_index[:, None] >= prompt_ends[None, :]).astype(jnp.int32), axis=1)
    return (member.astype(jnp.float32), position, owner, slot_index)


def rope_tables(position, head_size):
    frequency = rope_base ** (-(jnp.arange(head_size // 2, dtype=jnp.float32) * 2.0 / head_size))
    angles = position.astype(jnp.float32)[:, None] * frequency[None, :]
    cosine_table = jnp.cos(angles)
    sine_table = jnp.sin(angles)
    return (
        jnp.concatenate([cosine_table, cosine_table], 1)[:, None, :],
        jnp.concatenate([sine_table, sine_table], 1)[:, None, :],
    )


def gather_blk(piece, n_blk):
    me = lax.axis_index("blk")
    received = [piece]
    for shift in range(1, n_blk):
        pairs = [(i, (i + shift) % n_blk) for i in range(n_blk)]
        received.append(lax.ppermute(piece, "blk", pairs))
    ordered = []
    for source in range(n_blk):
        pick = (me - source) % n_blk
        ordered.append(lax.switch(pick, [lambda s=s: received[s] for s in range(n_blk)]))
    return ordered


def sum_blk(piece, n_blk):
    if n_blk == 2:
        return piece + lax.ppermute(piece, "blk", [(0, 1), (1, 0)])
    return lax.psum(piece, "blk")


def ring_order(count):
    if count % 2 == 0 and count > 2:
        return list(range(0, count, 2)) + list(range(count - 1, 0, -2))
    return list(range(count))


def ring_gather(piece, count, order, direction):
    pairs = [(order[i], order[(i + direction) % count]) for i in range(count)]
    received = [piece]
    current = piece
    for _ in range(count - 1):
        current = lax.ppermute(current, "chip", pairs)
        received.append(current)
    return received


def shards(
    hidden,
    input_norm_gain,
    query_weight,
    keyvalue_weight,
    adapter_down,
    adapter_up_query,
    adapter_up_keyvalue,
    packed_lengths,
    prompt_adapter,
):
    n_blk = lax.axis_size("blk")
    n_lo = lax.axis_size("core")
    n_chip = lax.axis_size("chip")
    row_number, feature_cols = hidden.shape
    full_width = feature_cols * n_blk
    me_blk = lax.axis_index("blk")
    me_core = lax.axis_index("core")
    me_chip = lax.axis_index("chip")

    if n_blk == 2:
        other = lax.ppermute(hidden, "blk", [(0, 1), (1, 0)])
        halves = [lax.select(me_blk == 0, hidden, other), lax.select(me_blk == 0, other, hidden)]
    else:
        halves = gather_blk(hidden, n_blk)
    full_hidden = jnp.concatenate(halves, axis=1)
    values = full_hidden.astype(jnp.float32)
    squares = jnp.sum(values * values, axis=1)
    factor = lax.rsqrt(squares / full_width + epsilon)
    normed = (values * factor[:, None] * input_norm_gain[None, :]).astype(jnp.bfloat16)
    normed_part = lax.dynamic_slice_in_dim(normed, me_blk * feature_cols, feature_cols, 1)

    weight_rows = query_weight.shape[0]
    query_cols = query_weight.shape[1]
    pair_cols = keyvalue_weight.shape[1]
    half_rows = weight_rows // 2

    weights = jnp.concatenate([query_weight, keyvalue_weight], axis=1)
    down_rows = adapter_down.size // query_cols
    upq_rows = adapter_up_query.size // query_cols
    upkv_rows = adapter_up_keyvalue.size // query_cols
    down_flat = adapter_down.reshape(down_rows, query_cols)
    upq_flat = adapter_up_query.reshape(upq_rows, query_cols)
    upkv_flat = adapter_up_keyvalue.reshape(upkv_rows, query_cols)
    dh, uh, vh = down_rows // 2, upq_rows // 2, upkv_rows // 2
    piece_rows = dh + uh + vh
    pad_rows = (-piece_rows) % 8

    def adapter_half(h):
        return jnp.concatenate(
            [
                down_flat[h * dh : (h + 1) * dh],
                upq_flat[h * uh : (h + 1) * uh],
                upkv_flat[h * vh : (h + 1) * vh],
                jnp.zeros((pad_rows, query_cols), jnp.bfloat16),
            ]
        )

    order = ring_order(n_chip)
    inverse = [0] * n_chip
    for i, c in enumerate(order):
        inverse[c] = i
    order_table = jnp.asarray(order, jnp.int32)
    inverse_table = jnp.asarray(inverse, jnp.int32)
    pos = inverse_table[me_chip]
    directions = (1, -1)

    def swap_core(x):
        if n_lo == 1:
            return [x]
        return [x, lax.ppermute(x, "core", [(0, 1), (1, 0)])]

    w_recv, a_recv = [], []
    for h, direction in enumerate(directions):
        a_recv.append(ring_gather(adapter_half(h), n_chip, order, direction))
        w_recv.append(
            ring_gather(weights[h * half_rows : (h + 1) * half_rows], n_chip, order, direction)
        )
    adapter_pieces = [
        jnp.stack([jnp.stack(swap_core(a_recv[h][s])) for s in range(n_chip)])
        for h in range(len(directions))
    ]

    total = None
    for s in range(n_chip):
        for h, direction in enumerate(directions):
            src_chip = order_table[(pos - s * direction) % n_chip]
            for slot, p in enumerate(swap_core(w_recv[h][s])):
                src_core = me_core if slot == 0 else n_lo - 1 - me_core
                start = (src_chip * n_lo + src_core) * weight_rows + h * half_rows
                lhs = lax.dynamic_slice_in_dim(normed, start, half_rows, 1)
                part = jnp.dot(lhs, p, preferred_element_type=jnp.float32)
                total = part if total is None else total + part

    picked = prompt_adapter[0]
    prompt_count = picked.shape[0]
    a_chip = picked // n_lo
    a_core = picked % n_lo
    a_slot = (a_core != me_core).astype(jnp.int32)
    per_half = []
    for h, direction in enumerate(directions):
        a_step = ((pos - inverse_table[a_chip]) * direction) % n_chip
        per_half.append(adapter_pieces[h][a_step, a_slot])
    down_selected = jnp.concatenate(
        [per_half[0][:, :dh], per_half[1][:, :dh]], axis=1
    ).reshape((prompt_count,) + adapter_down.shape[1:])
    up_query_selected = jnp.concatenate(
        [per_half[0][:, dh : dh + uh], per_half[1][:, dh : dh + uh]], axis=1
    ).reshape((prompt_count,) + adapter_up_query.shape[1:])
    up_pair_selected = jnp.concatenate(
        [per_half[0][:, dh + uh : piece_rows], per_half[1][:, dh + uh : piece_rows]], axis=1
    ).reshape((prompt_count,) + adapter_up_keyvalue.shape[1:])

    query_plain = total[:, :query_cols]
    base_pair = total[:, query_cols:]

    lengths = packed_lengths[0]
    member, position, owner, slot_index = layout(lengths, row_number)
    rank_size = down_selected.shape[2]
    partial_value = lax.dot_general(
        normed_part,
        down_selected.reshape(prompt_count * 3 * rank_size, feature_cols),
        (((1,), (1,)), ((), ())),
        preferred_element_type=jnp.float32,
    )
    partial_value = partial_value.reshape(row_number, prompt_count, 3, rank_size)
    masked = jnp.sum(partial_value * member[:, :, None, None], axis=1).reshape(
        row_number, 3 * rank_size
    )
    low_rank = sum_blk(masked, n_blk).reshape(row_number, 3, rank_size).astype(jnp.bfloat16)
    low_float = low_rank.astype(jnp.float32)

    def spread(column):
        return (
            (member[:, :, None] * low_float[:, None, column, :])
            .astype(jnp.bfloat16)
            .reshape(row_number, prompt_count * rank_size)
        )

    up_keyvalue_selected = up_pair_selected.reshape(
        prompt_count, rank_size, KEYVALUE_LOCAL, 2, HEAD_WIDTH
    )
    query_update = jnp.dot(
        spread(0),
        up_query_selected.reshape(prompt_count * rank_size, query_cols),
        preferred_element_type=jnp.float32,
    )
    key_update = jnp.dot(
        spread(1),
        up_keyvalue_selected[:, :, :, 0].reshape(
            prompt_count * rank_size, KEYVALUE_LOCAL * HEAD_WIDTH
        ),
        preferred_element_type=jnp.float32,
    )
    value_update = jnp.dot(
        spread(2),
        up_keyvalue_selected[:, :, :, 1].reshape(
            prompt_count * rank_size, KEYVALUE_LOCAL * HEAD_WIDTH
        ),
        preferred_element_type=jnp.float32,
    )
    cosine_table, sine_table = rope_tables(position, HEAD_WIDTH)
    query_complete = (query_plain + adapter_scale * query_update).reshape(
        row_number, QUERY_LOCAL * KEYVALUE_LOCAL, HEAD_WIDTH
    )
    query_states = apply_rotation(query_complete, cosine_table, sine_table).astype(jnp.bfloat16)
    keyvalue_plain = base_pair.reshape(row_number, KEYVALUE_LOCAL, 2, HEAD_WIDTH)
    key_vectors = apply_rotation(
        keyvalue_plain[:, :, 0]
        + adapter_scale * key_update.reshape(row_number, KEYVALUE_LOCAL, HEAD_WIDTH),
        cosine_table,
        sine_table,
    ).astype(jnp.bfloat16)
    value_vectors = (
        keyvalue_plain[:, :, 1]
        + adapter_scale * value_update.reshape(row_number, KEYVALUE_LOCAL, HEAD_WIDTH)
    ).astype(jnp.bfloat16)
    grouped = query_states.reshape(row_number, KEYVALUE_LOCAL, QUERY_LOCAL, HEAD_WIDTH)
    scores = jnp.einsum(
        "tkgc,skc->kgts", grouped, key_vectors, preferred_element_type=jnp.float32
    ) / math.sqrt(HEAD_WIDTH)
    allowed = (owner[:, None] == owner[None, :]) & (slot_index[None, :] <= slot_index[:, None])
    scores = jnp.where(allowed[None, None], scores, -1e30)
    row_max = jnp.max(scores, axis=-1, keepdims=True)
    exponent = jnp.exp(scores - row_max)
    attend = (exponent / jnp.sum(exponent, axis=-1, keepdims=True)).astype(jnp.bfloat16)
    context = jnp.einsum(
        "kgts,skc->tkgc", attend, value_vectors, preferred_element_type=jnp.float32
    ).astype(jnp.bfloat16)
    return (
        context.reshape(row_number, KEYVALUE_LOCAL * QUERY_LOCAL * HEAD_WIDTH),
        key_vectors.reshape(row_number, KEYVALUE_LOCAL * HEAD_WIDTH),
        value_vectors.reshape(row_number, KEYVALUE_LOCAL * HEAD_WIDTH),
    )


def solution(mesh):
    n_blk = mesh.shape["blk"]
    n_req = mesh.shape["req"]
    n_lo = 2 if n_req % 2 == 0 else 1
    devices = mesh.devices.reshape(n_blk, n_req // n_lo, n_lo)
    split_mesh = Mesh(devices, ("blk", "chip", "core"))
    req = ("chip", "core")
    in_specs = (
        P(req, "blk"),
        P(),
        P(req, "blk"),
        P(req, "blk"),
        P(req, None, None, "blk"),
        P(req, None, "blk"),
        P(req, None, "blk"),
        P(req, None),
        P(req, None),
    )
    out_specs = (P(req, "blk"), P(req, "blk"), P(req, "blk"))
    return jax.shard_map(
        shards, mesh=split_mesh, in_specs=in_specs, out_specs=out_specs, check_vma=False
    )
```

```python
import math

import jax
import jax.numpy as jnp
from jax import lax
from jax.sharding import Mesh
from jax.sharding import PartitionSpec as P

HEAD_WIDTH = 128
QUERY_LOCAL = 8
KEYVALUE_LOCAL = 1


epsilon = 1e-05
adapter_scale = 2.0
rope_base = 10000.0


def apply_rotation(vectors, cosine_table, sine_table):
    half_size = vectors.shape[-1] // 2
    first_half = vectors[..., :half_size]
    second_half = vectors[..., half_size:]
    turned = jnp.concatenate([-second_half, first_half], axis=-1)
    return vectors * cosine_table + turned * sine_table


def layout(lengths, count):
    slot_index = jnp.arange(count, dtype=jnp.int32)
    prompt_ends = jnp.cumsum(lengths)
    prompt_starts = prompt_ends - lengths
    member = (slot_index[:, None] >= prompt_starts[None, :]) & (
        slot_index[:, None] < prompt_ends[None, :]
    )
    position = jnp.sum(jnp.where(member, slot_index[:, None] - prompt_starts[None, :], 0), axis=1)
    owner = jnp.sum((slot_index[:, None] >= prompt_ends[None, :]).astype(jnp.int32), axis=1)
    return (member.astype(jnp.float32), position, owner, slot_index)


def rope_tables(position, head_size):
    frequency = rope_base ** (-(jnp.arange(head_size // 2, dtype=jnp.float32) * 2.0 / head_size))
    angles = position.astype(jnp.float32)[:, None] * frequency[None, :]
    cosine_table = jnp.cos(angles)
    sine_table = jnp.sin(angles)
    return (
        jnp.concatenate([cosine_table, cosine_table], 1)[:, None, :],
        jnp.concatenate([sine_table, sine_table], 1)[:, None, :],
    )


def gather_blk(piece, n_blk):
    me = lax.axis_index("blk")
    received = [piece]
    for shift in range(1, n_blk):
        pairs = [(i, (i + shift) % n_blk) for i in range(n_blk)]
        received.append(lax.ppermute(piece, "blk", pairs))
    ordered = []
    for source in range(n_blk):
        pick = (me - source) % n_blk
        ordered.append(lax.switch(pick, [lambda s=s: received[s] for s in range(n_blk)]))
    return ordered


def sum_blk(piece, n_blk):
    if n_blk == 2:
        return piece + lax.ppermute(piece, "blk", [(0, 1), (1, 0)])
    return lax.psum(piece, "blk")


def ring_order(count):
    if count % 2 == 0 and count > 2:
        return list(range(0, count, 2)) + list(range(count - 1, 0, -2))
    return list(range(count))


def ring_gather(piece, count, order, direction):
    pairs = [(order[i], order[(i + direction) % count]) for i in range(count)]
    received = [piece]
    current = piece
    for _ in range(count - 1):
        current = lax.ppermute(current, "chip", pairs)
        received.append(current)
    return received


def shards(
    hidden,
    input_norm_gain,
    query_weight,
    keyvalue_weight,
    adapter_down,
    adapter_up_query,
    adapter_up_keyvalue,
    packed_lengths,
    prompt_adapter,
):
    n_blk = lax.axis_size("blk")
    n_lo = lax.axis_size("core")
    n_chip = lax.axis_size("chip")
    row_number, feature_cols = hidden.shape
    full_width = feature_cols * n_blk
    me_blk = lax.axis_index("blk")
    me_core = lax.axis_index("core")
    me_chip = lax.axis_index("chip")

    if n_blk == 2:
        other = lax.ppermute(hidden, "blk", [(0, 1), (1, 0)])
        halves = [lax.select(me_blk == 0, hidden, other), lax.select(me_blk == 0, other, hidden)]
    else:
        halves = gather_blk(hidden, n_blk)
    full_hidden = jnp.concatenate(halves, axis=1)
    values = full_hidden.astype(jnp.float32)
    squares = jnp.sum(values * values, axis=1)
    factor = lax.rsqrt(squares / full_width + epsilon)
    normed = (values * factor[:, None] * input_norm_gain[None, :]).astype(jnp.bfloat16)
    normed_part = lax.dynamic_slice_in_dim(normed, me_blk * feature_cols, feature_cols, 1)

    weight_rows = query_weight.shape[0]
    query_cols = query_weight.shape[1]
    pair_cols = keyvalue_weight.shape[1]
    half_rows = weight_rows // 2

    weights = jnp.concatenate([query_weight, keyvalue_weight], axis=1)
    width = query_cols + pair_cols
    down_size = adapter_down.size
    upq_size = adapter_up_query.size
    upkv_size = adapter_up_keyvalue.size
    adapter_size = down_size + upq_size + upkv_size
    adapter_rows = -(-adapter_size // (width * 8)) * 8
    adapter_own = jnp.pad(
        jnp.concatenate(
            [adapter_down.reshape(-1), adapter_up_query.reshape(-1), adapter_up_keyvalue.reshape(-1)]
        ),
        (0, adapter_rows * width - adapter_size),
    ).reshape(adapter_rows, width)

    order = ring_order(n_chip)
    inverse = [0] * n_chip
    for i, c in enumerate(order):
        inverse[c] = i
    order_table = jnp.asarray(order, jnp.int32)
    inverse_table = jnp.asarray(inverse, jnp.int32)
    pos = inverse_table[me_chip]
    directions = (1, -1)
    adapter_reach = (n_chip // 2, n_chip - 1 - n_chip // 2)

    def swap_core(x):
        if n_lo == 1:
            return [x]
        return [x, lax.ppermute(x, "core", [(0, 1), (1, 0)])]

    w_recv = [[weights[h * half_rows : (h + 1) * half_rows]] for h in range(2)]
    a_recv = [[], []]
    for h, direction in enumerate(directions):
        pairs = [(order[i], order[(i + direction) % n_chip]) for i in range(n_chip)]
        w_cur, a_cur = w_recv[h][0], adapter_own
        for s in range(1, n_chip):
            if s <= adapter_reach[h]:
                got = lax.ppermute(jnp.concatenate([w_cur, a_cur]), "chip", pairs)
                w_cur, a_cur = got[:half_rows], got[half_rows:]
                a_recv[h].append(a_cur)
            else:
                w_cur = lax.ppermute(w_cur, "chip", pairs)
            w_recv[h].append(w_cur)
    adapter_list = [adapter_own] + a_recv[0] + a_recv[1]
    adapter_pieces = jnp.stack([jnp.stack(swap_core(p)) for p in adapter_list])

    total = None
    for s in range(n_chip):
        for h, direction in enumerate(directions):
            src_chip = order_table[(pos - s * direction) % n_chip]
            for slot, p in enumerate(swap_core(w_recv[h][s])):
                src_core = me_core if slot == 0 else n_lo - 1 - me_core
                start = (src_chip * n_lo + src_core) * weight_rows + h * half_rows
                lhs = lax.dynamic_slice_in_dim(normed, start, half_rows, 1)
                part = jnp.dot(lhs, p, preferred_element_type=jnp.float32)
                total = part if total is None else total + part

    picked = prompt_adapter[0]
    prompt_count = picked.shape[0]
    a_chip = picked // n_lo
    a_core = picked % n_lo
    a_slot = (a_core != me_core).astype(jnp.int32)
    distance = (pos - inverse_table[a_chip]) % n_chip
    a_index = jnp.where(
        distance <= adapter_reach[0], distance, adapter_reach[0] + (n_chip - distance)
    )
    chosen = adapter_pieces[a_index, a_slot].reshape(prompt_count, adapter_rows * width)
    down_selected = chosen[:, :down_size].reshape((prompt_count,) + adapter_down.shape[1:])
    up_query_selected = chosen[:, down_size : down_size + upq_size].reshape(
        (prompt_count,) + adapter_up_query.shape[1:]
    )
    up_pair_selected = chosen[:, down_size + upq_size : adapter_size].reshape(
        (prompt_count,) + adapter_up_keyvalue.shape[1:]
    )

    query_plain = total[:, :query_cols]
    base_pair = total[:, query_cols:]

    lengths = packed_lengths[0]
    member, position, owner, slot_index = layout(lengths, row_number)
    rank_size = down_selected.shape[2]
    partial_value = lax.dot_general(
        normed_part,
        down_selected.reshape(prompt_count * 3 * rank_size, feature_cols),
        (((1,), (1,)), ((), ())),
        preferred_element_type=jnp.float32,
    )
    partial_value = partial_value.reshape(row_number, prompt_count, 3, rank_size)
    masked = jnp.sum(partial_value * member[:, :, None, None], axis=1).reshape(
        row_number, 3 * rank_size
    )
    low_rank = sum_blk(masked, n_blk).reshape(row_number, 3, rank_size).astype(jnp.bfloat16)
    low_float = low_rank.astype(jnp.float32)

    def spread(column):
        return (
            (member[:, :, None] * low_float[:, None, column, :])
            .astype(jnp.bfloat16)
            .reshape(row_number, prompt_count * rank_size)
        )

    up_keyvalue_selected = up_pair_selected.reshape(
        prompt_count, rank_size, KEYVALUE_LOCAL, 2, HEAD_WIDTH
    )
    query_update = jnp.dot(
        spread(0),
        up_query_selected.reshape(prompt_count * rank_size, query_cols),
        preferred_element_type=jnp.float32,
    )
    key_update = jnp.dot(
        spread(1),
        up_keyvalue_selected[:, :, :, 0].reshape(
            prompt_count * rank_size, KEYVALUE_LOCAL * HEAD_WIDTH
        ),
        preferred_element_type=jnp.float32,
    )
    value_update = jnp.dot(
        spread(2),
        up_keyvalue_selected[:, :, :, 1].reshape(
            prompt_count * rank_size, KEYVALUE_LOCAL * HEAD_WIDTH
        ),
        preferred_element_type=jnp.float32,
    )
    cosine_table, sine_table = rope_tables(position, HEAD_WIDTH)
    query_complete = (query_plain + adapter_scale * query_update).reshape(
        row_number, QUERY_LOCAL * KEYVALUE_LOCAL, HEAD_WIDTH
    )
    query_states = apply_rotation(query_complete, cosine_table, sine_table).astype(jnp.bfloat16)
    keyvalue_plain = base_pair.reshape(row_number, KEYVALUE_LOCAL, 2, HEAD_WIDTH)
    key_vectors = apply_rotation(
        keyvalue_plain[:, :, 0]
        + adapter_scale * key_update.reshape(row_number, KEYVALUE_LOCAL, HEAD_WIDTH),
        cosine_table,
        sine_table,
    ).astype(jnp.bfloat16)
    value_vectors = (
        keyvalue_plain[:, :, 1]
        + adapter_scale * value_update.reshape(row_number, KEYVALUE_LOCAL, HEAD_WIDTH)
    ).astype(jnp.bfloat16)
    grouped = query_states.reshape(row_number, KEYVALUE_LOCAL, QUERY_LOCAL, HEAD_WIDTH)
    scores = jnp.einsum(
        "tkgc,skc->kgts", grouped, key_vectors, preferred_element_type=jnp.float32
    ) / math.sqrt(HEAD_WIDTH)
    allowed = (owner[:, None] == owner[None, :]) & (slot_index[None, :] <= slot_index[:, None])
    scores = jnp.where(allowed[None, None], scores, -1e30)
    row_max = jnp.max(scores, axis=-1, keepdims=True)
    exponent = jnp.exp(scores - row_max)
    attend = (exponent / jnp.sum(exponent, axis=-1, keepdims=True)).astype(jnp.bfloat16)
    context = jnp.einsum(
        "kgts,skc->tkgc", attend, value_vectors, preferred_element_type=jnp.float32
    ).astype(jnp.bfloat16)
    return (
        context.reshape(row_number, KEYVALUE_LOCAL * QUERY_LOCAL * HEAD_WIDTH),
        key_vectors.reshape(row_number, KEYVALUE_LOCAL * HEAD_WIDTH),
        value_vectors.reshape(row_number, KEYVALUE_LOCAL * HEAD_WIDTH),
    )


def solution(mesh):
    n_blk = mesh.shape["blk"]
    n_req = mesh.shape["req"]
    n_lo = 2 if n_req % 2 == 0 else 1
    devices = mesh.devices.reshape(n_blk, n_req // n_lo, n_lo)
    split_mesh = Mesh(devices, ("blk", "chip", "core"))
    req = ("chip", "core")
    in_specs = (
        P(req, "blk"),
        P(),
        P(req, "blk"),
        P(req, "blk"),
        P(req, None, None, "blk"),
        P(req, None, "blk"),
        P(req, None, "blk"),
        P(req, None),
        P(req, None),
    )
    out_specs = (P(req, "blk"), P(req, "blk"), P(req, "blk"))
    return jax.shard_map(
        shards, mesh=split_mesh, in_specs=in_specs, out_specs=out_specs, check_vma=False
    )
```

```python
import math

import jax
import jax.numpy as jnp
from jax import lax
from jax.sharding import Mesh
from jax.sharding import PartitionSpec as P

HEAD_WIDTH = 128
QUERY_LOCAL = 8
KEYVALUE_LOCAL = 1


epsilon = 1e-05
adapter_scale = 2.0
rope_base = 10000.0


def apply_rotation(vectors, cosine_table, sine_table):
    half_size = vectors.shape[-1] // 2
    first_half = vectors[..., :half_size]
    second_half = vectors[..., half_size:]
    turned = jnp.concatenate([-second_half, first_half], axis=-1)
    return vectors * cosine_table + turned * sine_table


def layout(lengths, count):
    slot_index = jnp.arange(count, dtype=jnp.int32)
    prompt_ends = jnp.cumsum(lengths)
    prompt_starts = prompt_ends - lengths
    member = (slot_index[:, None] >= prompt_starts[None, :]) & (
        slot_index[:, None] < prompt_ends[None, :]
    )
    position = jnp.sum(jnp.where(member, slot_index[:, None] - prompt_starts[None, :], 0), axis=1)
    owner = jnp.sum((slot_index[:, None] >= prompt_ends[None, :]).astype(jnp.int32), axis=1)
    return (member.astype(jnp.float32), position, owner, slot_index)


def rope_tables(position, head_size):
    frequency = rope_base ** (-(jnp.arange(head_size // 2, dtype=jnp.float32) * 2.0 / head_size))
    angles = position.astype(jnp.float32)[:, None] * frequency[None, :]
    cosine_table = jnp.cos(angles)
    sine_table = jnp.sin(angles)
    return (
        jnp.concatenate([cosine_table, cosine_table], 1)[:, None, :],
        jnp.concatenate([sine_table, sine_table], 1)[:, None, :],
    )


def gather_blk(piece, n_blk):
    me = lax.axis_index("blk")
    received = [piece]
    for shift in range(1, n_blk):
        pairs = [(i, (i + shift) % n_blk) for i in range(n_blk)]
        received.append(lax.ppermute(piece, "blk", pairs))
    ordered = []
    for source in range(n_blk):
        pick = (me - source) % n_blk
        ordered.append(lax.switch(pick, [lambda s=s: received[s] for s in range(n_blk)]))
    return ordered


def sum_blk(piece, n_blk):
    if n_blk == 2:
        return piece + lax.ppermute(piece, "blk", [(0, 1), (1, 0)])
    return lax.psum(piece, "blk")


def ring_order(count):
    if count % 2 == 0 and count > 2:
        return list(range(0, count, 2)) + list(range(count - 1, 0, -2))
    return list(range(count))


def ring_gather(piece, count, order, direction):
    pairs = [(order[i], order[(i + direction) % count]) for i in range(count)]
    received = [piece]
    current = piece
    for _ in range(count - 1):
        current = lax.ppermute(current, "chip", pairs)
        received.append(current)
    return received


def shards(
    hidden,
    input_norm_gain,
    query_weight,
    keyvalue_weight,
    adapter_down,
    adapter_up_query,
    adapter_up_keyvalue,
    packed_lengths,
    prompt_adapter,
):
    n_blk = lax.axis_size("blk")
    n_lo = lax.axis_size("core")
    n_chip = lax.axis_size("chip")
    row_number, feature_cols = hidden.shape
    full_width = feature_cols * n_blk
    me_blk = lax.axis_index("blk")
    me_core = lax.axis_index("core")
    me_chip = lax.axis_index("chip")

    if n_blk == 2:
        other = lax.ppermute(hidden, "blk", [(0, 1), (1, 0)])
        halves = [lax.select(me_blk == 0, hidden, other), lax.select(me_blk == 0, other, hidden)]
    else:
        halves = gather_blk(hidden, n_blk)
    full_hidden = jnp.concatenate(halves, axis=1)
    values = full_hidden.astype(jnp.float32)
    squares = jnp.sum(values * values, axis=1)
    factor = lax.rsqrt(squares / full_width + epsilon)
    normed = (values * factor[:, None] * input_norm_gain[None, :]).astype(jnp.bfloat16)
    normed_part = lax.dynamic_slice_in_dim(normed, me_blk * feature_cols, feature_cols, 1)

    weight_rows = query_weight.shape[0]
    query_cols = query_weight.shape[1]
    pair_cols = keyvalue_weight.shape[1]
    half_rows = weight_rows // 2

    weights = jnp.concatenate([query_weight, keyvalue_weight], axis=1)
    width = query_cols + pair_cols
    down_half = adapter_down.size // 2
    upq_half = adapter_up_query.size // 2
    upkv_half = adapter_up_keyvalue.size // 2
    half_size = down_half + upq_half + upkv_half
    adapter_rows = -(-half_size // (width * 8)) * 8
    down_flat = adapter_down.reshape(-1)
    upq_flat = adapter_up_query.reshape(-1)
    upkv_flat = adapter_up_keyvalue.reshape(-1)

    def adapter_half(h):
        flat = jnp.concatenate(
            [
                down_flat[h * down_half : (h + 1) * down_half],
                upq_flat[h * upq_half : (h + 1) * upq_half],
                upkv_flat[h * upkv_half : (h + 1) * upkv_half],
            ]
        )
        return jnp.pad(flat, (0, adapter_rows * width - half_size)).reshape(adapter_rows, width)

    order = ring_order(n_chip)
    inverse = [0] * n_chip
    for i, c in enumerate(order):
        inverse[c] = i
    order_table = jnp.asarray(order, jnp.int32)
    inverse_table = jnp.asarray(inverse, jnp.int32)
    pos = inverse_table[me_chip]
    directions = (1, -1)

    def swap_core(x):
        if n_lo == 1:
            return [x]
        return [x, lax.ppermute(x, "core", [(0, 1), (1, 0)])]

    recv = []
    for h, direction in enumerate(directions):
        piece = jnp.concatenate(
            [weights[h * half_rows : (h + 1) * half_rows], adapter_half(h)], axis=0
        )
        recv.append(ring_gather(piece, n_chip, order, direction))

    total = None
    adapter_steps = [[], []]
    for s in range(n_chip):
        for h, direction in enumerate(directions):
            src_chip = order_table[(pos - s * direction) % n_chip]
            both = swap_core(recv[h][s])
            adapter_steps[h].append(jnp.stack([p[half_rows:] for p in both]))
            for slot, p in enumerate(both):
                src_core = me_core if slot == 0 else n_lo - 1 - me_core
                start = (src_chip * n_lo + src_core) * weight_rows + h * half_rows
                lhs = lax.dynamic_slice_in_dim(normed, start, half_rows, 1)
                part = jnp.dot(lhs, p[:half_rows], preferred_element_type=jnp.float32)
                total = part if total is None else total + part
    adapter_pieces = [jnp.stack(a) for a in adapter_steps]

    picked = prompt_adapter[0]
    prompt_count = picked.shape[0]
    a_chip = picked // n_lo
    a_core = picked % n_lo
    a_slot = (a_core != me_core).astype(jnp.int32)
    per_half = []
    for h, direction in enumerate(directions):
        a_step = ((pos - inverse_table[a_chip]) * direction) % n_chip
        per_half.append(adapter_pieces[h][a_step, a_slot])
    flat_half = [p.reshape(prompt_count, adapter_rows * width) for p in per_half]

    def joined(lo, hi, shape):
        return jnp.concatenate([f[:, lo:hi] for f in flat_half], axis=1).reshape(
            (prompt_count,) + shape[1:]
        )

    down_selected = joined(0, down_half, adapter_down.shape)
    up_query_selected = joined(down_half, down_half + upq_half, adapter_up_query.shape)
    up_pair_selected = joined(down_half + upq_half, half_size, adapter_up_keyvalue.shape)

    query_plain = total[:, :query_cols]
    base_pair = total[:, query_cols:]

    lengths = packed_lengths[0]
    member, position, owner, slot_index = layout(lengths, row_number)
    rank_size = down_selected.shape[2]
    partial_value = lax.dot_general(
        normed_part,
        down_selected.reshape(prompt_count * 3 * rank_size, feature_cols),
        (((1,), (1,)), ((), ())),
        preferred_element_type=jnp.float32,
    )
    partial_value = partial_value.reshape(row_number, prompt_count, 3, rank_size)
    masked = jnp.sum(partial_value * member[:, :, None, None], axis=1).reshape(
        row_number, 3 * rank_size
    )
    low_rank = sum_blk(masked, n_blk).reshape(row_number, 3, rank_size).astype(jnp.bfloat16)
    low_float = low_rank.astype(jnp.float32)

    def spread(column):
        return (
            (member[:, :, None] * low_float[:, None, column, :])
            .astype(jnp.bfloat16)
            .reshape(row_number, prompt_count * rank_size)
        )

    up_keyvalue_selected = up_pair_selected.reshape(
        prompt_count, rank_size, KEYVALUE_LOCAL, 2, HEAD_WIDTH
    )
    query_update = jnp.dot(
        spread(0),
        up_query_selected.reshape(prompt_count * rank_size, query_cols),
        preferred_element_type=jnp.float32,
    )
    key_update = jnp.dot(
        spread(1),
        up_keyvalue_selected[:, :, :, 0].reshape(
            prompt_count * rank_size, KEYVALUE_LOCAL * HEAD_WIDTH
        ),
        preferred_element_type=jnp.float32,
    )
    value_update = jnp.dot(
        spread(2),
        up_keyvalue_selected[:, :, :, 1].reshape(
            prompt_count * rank_size, KEYVALUE_LOCAL * HEAD_WIDTH
        ),
        preferred_element_type=jnp.float32,
    )
    cosine_table, sine_table = rope_tables(position, HEAD_WIDTH)
    query_complete = (query_plain + adapter_scale * query_update).reshape(
        row_number, QUERY_LOCAL * KEYVALUE_LOCAL, HEAD_WIDTH
    )
    query_states = apply_rotation(query_complete, cosine_table, sine_table).astype(jnp.bfloat16)
    keyvalue_plain = base_pair.reshape(row_number, KEYVALUE_LOCAL, 2, HEAD_WIDTH)
    key_vectors = apply_rotation(
        keyvalue_plain[:, :, 0]
        + adapter_scale * key_update.reshape(row_number, KEYVALUE_LOCAL, HEAD_WIDTH),
        cosine_table,
        sine_table,
    ).astype(jnp.bfloat16)
    value_vectors = (
        keyvalue_plain[:, :, 1]
        + adapter_scale * value_update.reshape(row_number, KEYVALUE_LOCAL, HEAD_WIDTH)
    ).astype(jnp.bfloat16)
    grouped = query_states.reshape(row_number, KEYVALUE_LOCAL, QUERY_LOCAL, HEAD_WIDTH)
    scores = jnp.einsum(
        "tkgc,skc->kgts", grouped, key_vectors, preferred_element_type=jnp.float32
    ) / math.sqrt(HEAD_WIDTH)
    allowed = (owner[:, None] == owner[None, :]) & (slot_index[None, :] <= slot_index[:, None])
    scores = jnp.where(allowed[None, None], scores, -1e30)
    row_max = jnp.max(scores, axis=-1, keepdims=True)
    exponent = jnp.exp(scores - row_max)
    attend = (exponent / jnp.sum(exponent, axis=-1, keepdims=True)).astype(jnp.bfloat16)
    context = jnp.einsum(
        "kgts,skc->tkgc", attend, value_vectors, preferred_element_type=jnp.float32
    ).astype(jnp.bfloat16)
    return (
        context.reshape(row_number, KEYVALUE_LOCAL * QUERY_LOCAL * HEAD_WIDTH),
        key_vectors.reshape(row_number, KEYVALUE_LOCAL * HEAD_WIDTH),
        value_vectors.reshape(row_number, KEYVALUE_LOCAL * HEAD_WIDTH),
    )


def solution(mesh):
    n_blk = mesh.shape["blk"]
    n_req = mesh.shape["req"]
    n_lo = 2 if n_req % 2 == 0 else 1
    devices = mesh.devices.reshape(n_blk, n_req // n_lo, n_lo)
    split_mesh = Mesh(devices, ("blk", "chip", "core"))
    req = ("chip", "core")
    in_specs = (
        P(req, "blk"),
        P(),
        P(req, "blk"),
        P(req, "blk"),
        P(req, None, None, "blk"),
        P(req, None, "blk"),
        P(req, None, "blk"),
        P(req, None),
        P(req, None),
    )
    out_specs = (P(req, "blk"), P(req, "blk"), P(req, "blk"))
    return jax.shard_map(
        shards, mesh=split_mesh, in_specs=in_specs, out_specs=out_specs, check_vma=False
    )
```

```python
import math

import jax
import jax.numpy as jnp
from jax import lax
from jax.sharding import Mesh
from jax.sharding import PartitionSpec as P

HEAD_WIDTH = 128
QUERY_LOCAL = 8
KEYVALUE_LOCAL = 1


epsilon = 1e-05
adapter_scale = 2.0
rope_base = 10000.0


def apply_rotation(vectors, cosine_table, sine_table):
    half_size = vectors.shape[-1] // 2
    first_half = vectors[..., :half_size]
    second_half = vectors[..., half_size:]
    turned = jnp.concatenate([-second_half, first_half], axis=-1)
    return vectors * cosine_table + turned * sine_table


def layout(lengths, count):
    slot_index = jnp.arange(count, dtype=jnp.int32)
    prompt_ends = jnp.cumsum(lengths)
    prompt_starts = prompt_ends - lengths
    member = (slot_index[:, None] >= prompt_starts[None, :]) & (
        slot_index[:, None] < prompt_ends[None, :]
    )
    position = jnp.sum(jnp.where(member, slot_index[:, None] - prompt_starts[None, :], 0), axis=1)
    owner = jnp.sum((slot_index[:, None] >= prompt_ends[None, :]).astype(jnp.int32), axis=1)
    return (member.astype(jnp.float32), position, owner, slot_index)


def rope_tables(position, head_size):
    frequency = rope_base ** (-(jnp.arange(head_size // 2, dtype=jnp.float32) * 2.0 / head_size))
    angles = position.astype(jnp.float32)[:, None] * frequency[None, :]
    cosine_table = jnp.cos(angles)
    sine_table = jnp.sin(angles)
    return (
        jnp.concatenate([cosine_table, cosine_table], 1)[:, None, :],
        jnp.concatenate([sine_table, sine_table], 1)[:, None, :],
    )


def gather_blk(piece, n_blk):
    me = lax.axis_index("blk")
    received = [piece]
    for shift in range(1, n_blk):
        pairs = [(i, (i + shift) % n_blk) for i in range(n_blk)]
        received.append(lax.ppermute(piece, "blk", pairs))
    ordered = []
    for source in range(n_blk):
        pick = (me - source) % n_blk
        ordered.append(lax.switch(pick, [lambda s=s: received[s] for s in range(n_blk)]))
    return ordered


def sum_blk(piece, n_blk):
    if n_blk == 2:
        return piece + lax.ppermute(piece, "blk", [(0, 1), (1, 0)])
    return lax.psum(piece, "blk")


def ring_order(count):
    if count % 2 == 0 and count > 2:
        return list(range(0, count, 2)) + list(range(count - 1, 0, -2))
    return list(range(count))


def ring_gather(piece, count, order, direction):
    pairs = [(order[i], order[(i + direction) % count]) for i in range(count)]
    received = [piece]
    current = piece
    for _ in range(count - 1):
        current = lax.ppermute(current, "chip", pairs)
        received.append(current)
    return received


def shards(
    hidden,
    input_norm_gain,
    query_weight,
    keyvalue_weight,
    adapter_down,
    adapter_up_query,
    adapter_up_keyvalue,
    packed_lengths,
    prompt_adapter,
):
    n_blk = lax.axis_size("blk")
    n_lo = lax.axis_size("core")
    n_chip = lax.axis_size("chip")
    row_number, feature_cols = hidden.shape
    full_width = feature_cols * n_blk
    me_blk = lax.axis_index("blk")
    me_core = lax.axis_index("core")
    me_chip = lax.axis_index("chip")

    if n_blk == 2:
        other = lax.ppermute(hidden, "blk", [(0, 1), (1, 0)])
        halves = [lax.select(me_blk == 0, hidden, other), lax.select(me_blk == 0, other, hidden)]
    else:
        halves = gather_blk(hidden, n_blk)
    full_hidden = jnp.concatenate(halves, axis=1)
    values = full_hidden.astype(jnp.float32)
    squares = jnp.sum(values * values, axis=1)
    factor = lax.rsqrt(squares / full_width + epsilon)
    normed = (values * factor[:, None] * input_norm_gain[None, :]).astype(jnp.bfloat16)
    normed_part = lax.dynamic_slice_in_dim(normed, me_blk * feature_cols, feature_cols, 1)

    weight_rows = query_weight.shape[0]
    query_cols = query_weight.shape[1]
    pair_cols = keyvalue_weight.shape[1]
    half_rows = weight_rows // 2

    weights = jnp.concatenate([query_weight, keyvalue_weight], axis=1)
    down_rows = adapter_down.size // query_cols
    upq_rows = adapter_up_query.size // query_cols
    upkv_rows = adapter_up_keyvalue.size // query_cols
    adapter_rows = down_rows + upq_rows + upkv_rows
    pad_rows = (-adapter_rows) % 8
    adapter_own = jnp.concatenate(
        [
            adapter_down.reshape(down_rows, query_cols),
            adapter_up_query.reshape(upq_rows, query_cols),
            adapter_up_keyvalue.reshape(upkv_rows, query_cols),
            jnp.zeros((pad_rows, query_cols), jnp.bfloat16),
        ]
    )

    order = ring_order(n_chip)
    inverse = [0] * n_chip
    for i, c in enumerate(order):
        inverse[c] = i
    order_table = jnp.asarray(order, jnp.int32)
    inverse_table = jnp.asarray(inverse, jnp.int32)
    pos = inverse_table[me_chip]
    directions = (1, -1)

    def swap_core(x):
        if n_lo == 1:
            return [x]
        return [x, lax.ppermute(x, "core", [(0, 1), (1, 0)])]

    adapters_chip = lax.all_gather(adapter_own, "chip", axis=0, tiled=False)
    adapter_pieces = jnp.stack(swap_core(adapters_chip))

    recv = [
        ring_gather(weights[h * half_rows : (h + 1) * half_rows], n_chip, order, direction)
        for h, direction in enumerate(directions)
    ]

    total = None
    for s in range(n_chip):
        for h, direction in enumerate(directions):
            src_chip = order_table[(pos - s * direction) % n_chip]
            for slot, p in enumerate(swap_core(recv[h][s])):
                src_core = me_core if slot == 0 else n_lo - 1 - me_core
                start = (src_chip * n_lo + src_core) * weight_rows + h * half_rows
                lhs = lax.dynamic_slice_in_dim(normed, start, half_rows, 1)
                part = jnp.dot(lhs, p, preferred_element_type=jnp.float32)
                total = part if total is None else total + part

    picked = prompt_adapter[0]
    prompt_count = picked.shape[0]
    a_slot = (picked % n_lo != me_core).astype(jnp.int32)
    chosen = adapter_pieces[a_slot, picked // n_lo]
    down_selected = chosen[:, :down_rows].reshape((prompt_count,) + adapter_down.shape[1:])
    up_query_selected = chosen[:, down_rows : down_rows + upq_rows].reshape(
        (prompt_count,) + adapter_up_query.shape[1:]
    )
    up_pair_selected = chosen[:, down_rows + upq_rows : adapter_rows].reshape(
        (prompt_count,) + adapter_up_keyvalue.shape[1:]
    )

    query_plain = total[:, :query_cols]
    base_pair = total[:, query_cols:]

    lengths = packed_lengths[0]
    member, position, owner, slot_index = layout(lengths, row_number)
    rank_size = down_selected.shape[2]
    partial_value = lax.dot_general(
        normed_part,
        down_selected.reshape(prompt_count * 3 * rank_size, feature_cols),
        (((1,), (1,)), ((), ())),
        preferred_element_type=jnp.float32,
    )
    partial_value = partial_value.reshape(row_number, prompt_count, 3, rank_size)
    masked = jnp.sum(partial_value * member[:, :, None, None], axis=1).reshape(
        row_number, 3 * rank_size
    )
    low_rank = sum_blk(masked, n_blk).reshape(row_number, 3, rank_size).astype(jnp.bfloat16)
    low_float = low_rank.astype(jnp.float32)

    def spread(column):
        return (
            (member[:, :, None] * low_float[:, None, column, :])
            .astype(jnp.bfloat16)
            .reshape(row_number, prompt_count * rank_size)
        )

    up_keyvalue_selected = up_pair_selected.reshape(
        prompt_count, rank_size, KEYVALUE_LOCAL, 2, HEAD_WIDTH
    )
    query_update = jnp.dot(
        spread(0),
        up_query_selected.reshape(prompt_count * rank_size, query_cols),
        preferred_element_type=jnp.float32,
    )
    key_update = jnp.dot(
        spread(1),
        up_keyvalue_selected[:, :, :, 0].reshape(
            prompt_count * rank_size, KEYVALUE_LOCAL * HEAD_WIDTH
        ),
        preferred_element_type=jnp.float32,
    )
    value_update = jnp.dot(
        spread(2),
        up_keyvalue_selected[:, :, :, 1].reshape(
            prompt_count * rank_size, KEYVALUE_LOCAL * HEAD_WIDTH
        ),
        preferred_element_type=jnp.float32,
    )
    cosine_table, sine_table = rope_tables(position, HEAD_WIDTH)
    query_complete = (query_plain + adapter_scale * query_update).reshape(
        row_number, QUERY_LOCAL * KEYVALUE_LOCAL, HEAD_WIDTH
    )
    query_states = apply_rotation(query_complete, cosine_table, sine_table).astype(jnp.bfloat16)
    keyvalue_plain = base_pair.reshape(row_number, KEYVALUE_LOCAL, 2, HEAD_WIDTH)
    key_vectors = apply_rotation(
        keyvalue_plain[:, :, 0]
        + adapter_scale * key_update.reshape(row_number, KEYVALUE_LOCAL, HEAD_WIDTH),
        cosine_table,
        sine_table,
    ).astype(jnp.bfloat16)
    value_vectors = (
        keyvalue_plain[:, :, 1]
        + adapter_scale * value_update.reshape(row_number, KEYVALUE_LOCAL, HEAD_WIDTH)
    ).astype(jnp.bfloat16)
    grouped = query_states.reshape(row_number, KEYVALUE_LOCAL, QUERY_LOCAL, HEAD_WIDTH)
    scores = jnp.einsum(
        "tkgc,skc->kgts", grouped, key_vectors, preferred_element_type=jnp.float32
    ) / math.sqrt(HEAD_WIDTH)
    allowed = (owner[:, None] == owner[None, :]) & (slot_index[None, :] <= slot_index[:, None])
    scores = jnp.where(allowed[None, None], scores, -1e30)
    row_max = jnp.max(scores, axis=-1, keepdims=True)
    exponent = jnp.exp(scores - row_max)
    attend = (exponent / jnp.sum(exponent, axis=-1, keepdims=True)).astype(jnp.bfloat16)
    context = jnp.einsum(
        "kgts,skc->tkgc", attend, value_vectors, preferred_element_type=jnp.float32
    ).astype(jnp.bfloat16)
    return (
        context.reshape(row_number, KEYVALUE_LOCAL * QUERY_LOCAL * HEAD_WIDTH),
        key_vectors.reshape(row_number, KEYVALUE_LOCAL * HEAD_WIDTH),
        value_vectors.reshape(row_number, KEYVALUE_LOCAL * HEAD_WIDTH),
    )


def solution(mesh):
    n_blk = mesh.shape["blk"]
    n_req = mesh.shape["req"]
    n_lo = 2 if n_req % 2 == 0 else 1
    devices = mesh.devices.reshape(n_blk, n_req // n_lo, n_lo)
    split_mesh = Mesh(devices, ("blk", "chip", "core"))
    req = ("chip", "core")
    in_specs = (
        P(req, "blk"),
        P(),
        P(req, "blk"),
        P(req, "blk"),
        P(req, None, None, "blk"),
        P(req, None, "blk"),
        P(req, None, "blk"),
        P(req, None),
        P(req, None),
    )
    out_specs = (P(req, "blk"), P(req, "blk"), P(req, "blk"))
    return jax.shard_map(
        shards, mesh=split_mesh, in_specs=in_specs, out_specs=out_specs, check_vma=False
    )
```

```python
import math

import jax
import jax.numpy as jnp
from jax import lax
from jax.sharding import Mesh
from jax.sharding import PartitionSpec as P

HEAD_WIDTH = 128
QUERY_LOCAL = 8
KEYVALUE_LOCAL = 1


epsilon = 1e-05
adapter_scale = 2.0
rope_base = 10000.0


def apply_rotation(vectors, cosine_table, sine_table):
    half_size = vectors.shape[-1] // 2
    first_half = vectors[..., :half_size]
    second_half = vectors[..., half_size:]
    turned = jnp.concatenate([-second_half, first_half], axis=-1)
    return vectors * cosine_table + turned * sine_table


def layout(lengths, count):
    slot_index = jnp.arange(count, dtype=jnp.int32)
    prompt_ends = jnp.cumsum(lengths)
    prompt_starts = prompt_ends - lengths
    member = (slot_index[:, None] >= prompt_starts[None, :]) & (
        slot_index[:, None] < prompt_ends[None, :]
    )
    position = jnp.sum(jnp.where(member, slot_index[:, None] - prompt_starts[None, :], 0), axis=1)
    owner = jnp.sum((slot_index[:, None] >= prompt_ends[None, :]).astype(jnp.int32), axis=1)
    return (member.astype(jnp.float32), position, owner, slot_index)


def rope_tables(position, head_size):
    frequency = rope_base ** (-(jnp.arange(head_size // 2, dtype=jnp.float32) * 2.0 / head_size))
    angles = position.astype(jnp.float32)[:, None] * frequency[None, :]
    cosine_table = jnp.cos(angles)
    sine_table = jnp.sin(angles)
    return (
        jnp.concatenate([cosine_table, cosine_table], 1)[:, None, :],
        jnp.concatenate([sine_table, sine_table], 1)[:, None, :],
    )


def gather_blk(piece, n_blk):
    me = lax.axis_index("blk")
    received = [piece]
    for shift in range(1, n_blk):
        pairs = [(i, (i + shift) % n_blk) for i in range(n_blk)]
        received.append(lax.ppermute(piece, "blk", pairs))
    ordered = []
    for source in range(n_blk):
        pick = (me - source) % n_blk
        ordered.append(lax.switch(pick, [lambda s=s: received[s] for s in range(n_blk)]))
    return ordered


def sum_blk(piece, n_blk):
    if n_blk == 2:
        return piece + lax.ppermute(piece, "blk", [(0, 1), (1, 0)])
    return lax.psum(piece, "blk")


def ring_order(count):
    if count % 2 == 0 and count > 2:
        return list(range(0, count, 2)) + list(range(count - 1, 0, -2))
    return list(range(count))


def ring_gather(piece, count, order, direction):
    pairs = [(order[i], order[(i + direction) % count]) for i in range(count)]
    received = [piece]
    current = piece
    for _ in range(count - 1):
        current = lax.ppermute(current, "chip", pairs)
        received.append(current)
    return received


def shards(
    hidden,
    input_norm_gain,
    query_weight,
    keyvalue_weight,
    adapter_down,
    adapter_up_query,
    adapter_up_keyvalue,
    packed_lengths,
    prompt_adapter,
):
    n_blk = lax.axis_size("blk")
    n_lo = lax.axis_size("core")
    n_chip = lax.axis_size("chip")
    row_number, feature_cols = hidden.shape
    full_width = feature_cols * n_blk
    me_blk = lax.axis_index("blk")
    me_core = lax.axis_index("core")
    me_chip = lax.axis_index("chip")

    if n_blk == 2:
        other = lax.ppermute(hidden, "blk", [(0, 1), (1, 0)])
        halves = [lax.select(me_blk == 0, hidden, other), lax.select(me_blk == 0, other, hidden)]
    else:
        halves = gather_blk(hidden, n_blk)
    full_hidden = jnp.concatenate(halves, axis=1)
    values = full_hidden.astype(jnp.float32)
    squares = jnp.sum(values * values, axis=1)
    factor = lax.rsqrt(squares / full_width + epsilon)
    normed = (values * factor[:, None] * input_norm_gain[None, :]).astype(jnp.bfloat16)
    normed_part = lax.dynamic_slice_in_dim(normed, me_blk * feature_cols, feature_cols, 1)

    weight_rows = query_weight.shape[0]
    query_cols = query_weight.shape[1]
    pair_cols = keyvalue_weight.shape[1]
    half_rows = weight_rows // 2

    weights = jnp.concatenate([query_weight, keyvalue_weight], axis=1)
    down_rows = adapter_down.size // query_cols
    upq_rows = adapter_up_query.size // query_cols
    upkv_rows = adapter_up_keyvalue.size // query_cols
    adapter_rows = down_rows + upq_rows + upkv_rows
    pad_rows = (-adapter_rows) % 8
    adapter_own = jnp.concatenate(
        [
            adapter_down.reshape(down_rows, query_cols),
            adapter_up_query.reshape(upq_rows, query_cols),
            adapter_up_keyvalue.reshape(upkv_rows, query_cols),
            jnp.zeros((pad_rows, query_cols), jnp.bfloat16),
        ]
    )

    order = ring_order(n_chip)
    inverse = [0] * n_chip
    for i, c in enumerate(order):
        inverse[c] = i
    order_table = jnp.asarray(order, jnp.int32)
    inverse_table = jnp.asarray(inverse, jnp.int32)
    pos = inverse_table[me_chip]
    directions = (1, -1)

    def swap_core(x):
        if n_lo == 1:
            return [x]
        return [x, lax.ppermute(x, "core", [(0, 1), (1, 0)])]

    adapters_chip = lax.all_gather(adapter_own, "chip", axis=0, tiled=False)
    adapter_pieces = jnp.stack(swap_core(adapters_chip))

    picked = prompt_adapter[0]
    prompt_count = picked.shape[0]
    a_slot = (picked % n_lo != me_core).astype(jnp.int32)
    chosen = adapter_pieces[a_slot, picked // n_lo]
    down_selected = chosen[:, :down_rows].reshape((prompt_count,) + adapter_down.shape[1:])
    up_query_selected = chosen[:, down_rows : down_rows + upq_rows].reshape(
        (prompt_count,) + adapter_up_query.shape[1:]
    )
    up_pair_selected = chosen[:, down_rows + upq_rows : adapter_rows].reshape(
        (prompt_count,) + adapter_up_keyvalue.shape[1:]
    )

    lengths = packed_lengths[0]
    member, position, owner, slot_index = layout(lengths, row_number)
    rank_size = down_selected.shape[2]
    partial_value = lax.dot_general(
        normed_part,
        down_selected.reshape(prompt_count * 3 * rank_size, feature_cols),
        (((1,), (1,)), ((), ())),
        preferred_element_type=jnp.float32,
    )
    partial_value = partial_value.reshape(row_number, prompt_count, 3, rank_size)
    masked = jnp.sum(partial_value * member[:, :, None, None], axis=1).reshape(
        row_number, 3 * rank_size
    )
    low_rank = sum_blk(masked, n_blk).reshape(row_number, 3, rank_size).astype(jnp.bfloat16)
    low_float = low_rank.astype(jnp.float32)

    def spread(column):
        return (
            (member[:, :, None] * low_float[:, None, column, :])
            .astype(jnp.bfloat16)
            .reshape(row_number, prompt_count * rank_size)
        )

    up_keyvalue_selected = up_pair_selected.reshape(
        prompt_count, rank_size, KEYVALUE_LOCAL, 2, HEAD_WIDTH
    )
    query_update = jnp.dot(
        spread(0),
        up_query_selected.reshape(prompt_count * rank_size, query_cols),
        preferred_element_type=jnp.float32,
    )
    key_update = jnp.dot(
        spread(1),
        up_keyvalue_selected[:, :, :, 0].reshape(
            prompt_count * rank_size, KEYVALUE_LOCAL * HEAD_WIDTH
        ),
        preferred_element_type=jnp.float32,
    )
    value_update = jnp.dot(
        spread(2),
        up_keyvalue_selected[:, :, :, 1].reshape(
            prompt_count * rank_size, KEYVALUE_LOCAL * HEAD_WIDTH
        ),
        preferred_element_type=jnp.float32,
    )
    cosine_table, sine_table = rope_tables(position, HEAD_WIDTH)

    early = (query_update, key_update, value_update, cosine_table, sine_table)
    tie_step = min(n_chip - 1, n_chip // 2 + 1)
    recv = []
    for h, direction in enumerate(directions):
        pairs = [(order[i], order[(i + direction) % n_chip]) for i in range(n_chip)]
        current = weights[h * half_rows : (h + 1) * half_rows]
        got = [current]
        for s in range(1, n_chip):
            if s == tie_step:
                current, early = lax.optimization_barrier((current, early))
            current = lax.ppermute(current, "chip", pairs)
            got.append(current)
        recv.append(got)
    query_update, key_update, value_update, cosine_table, sine_table = early

    total = None
    for s in range(n_chip):
        for h, direction in enumerate(directions):
            src_chip = order_table[(pos - s * direction) % n_chip]
            for slot, p in enumerate(swap_core(recv[h][s])):
                src_core = me_core if slot == 0 else n_lo - 1 - me_core
                start = (src_chip * n_lo + src_core) * weight_rows + h * half_rows
                lhs = lax.dynamic_slice_in_dim(normed, start, half_rows, 1)
                part = jnp.dot(lhs, p, preferred_element_type=jnp.float32)
                total = part if total is None else total + part


    query_plain = total[:, :query_cols]
    base_pair = total[:, query_cols:]

    query_complete = (query_plain + adapter_scale * query_update).reshape(
        row_number, QUERY_LOCAL * KEYVALUE_LOCAL, HEAD_WIDTH
    )
    query_states = apply_rotation(query_complete, cosine_table, sine_table).astype(jnp.bfloat16)
    keyvalue_plain = base_pair.reshape(row_number, KEYVALUE_LOCAL, 2, HEAD_WIDTH)
    key_vectors = apply_rotation(
        keyvalue_plain[:, :, 0]
        + adapter_scale * key_update.reshape(row_number, KEYVALUE_LOCAL, HEAD_WIDTH),
        cosine_table,
        sine_table,
    ).astype(jnp.bfloat16)
    value_vectors = (
        keyvalue_plain[:, :, 1]
        + adapter_scale * value_update.reshape(row_number, KEYVALUE_LOCAL, HEAD_WIDTH)
    ).astype(jnp.bfloat16)
    grouped = query_states.reshape(row_number, KEYVALUE_LOCAL, QUERY_LOCAL, HEAD_WIDTH)
    scores = jnp.einsum(
        "tkgc,skc->kgts", grouped, key_vectors, preferred_element_type=jnp.float32
    ) / math.sqrt(HEAD_WIDTH)
    allowed = (owner[:, None] == owner[None, :]) & (slot_index[None, :] <= slot_index[:, None])
    scores = jnp.where(allowed[None, None], scores, -1e30)
    row_max = jnp.max(scores, axis=-1, keepdims=True)
    exponent = jnp.exp(scores - row_max)
    attend = (exponent / jnp.sum(exponent, axis=-1, keepdims=True)).astype(jnp.bfloat16)
    context = jnp.einsum(
        "kgts,skc->tkgc", attend, value_vectors, preferred_element_type=jnp.float32
    ).astype(jnp.bfloat16)
    return (
        context.reshape(row_number, KEYVALUE_LOCAL * QUERY_LOCAL * HEAD_WIDTH),
        key_vectors.reshape(row_number, KEYVALUE_LOCAL * HEAD_WIDTH),
        value_vectors.reshape(row_number, KEYVALUE_LOCAL * HEAD_WIDTH),
    )


def solution(mesh):
    n_blk = mesh.shape["blk"]
    n_req = mesh.shape["req"]
    n_lo = 2 if n_req % 2 == 0 else 1
    devices = mesh.devices.reshape(n_blk, n_req // n_lo, n_lo)
    split_mesh = Mesh(devices, ("blk", "chip", "core"))
    req = ("chip", "core")
    in_specs = (
        P(req, "blk"),
        P(),
        P(req, "blk"),
        P(req, "blk"),
        P(req, None, None, "blk"),
        P(req, None, "blk"),
        P(req, None, "blk"),
        P(req, None),
        P(req, None),
    )
    out_specs = (P(req, "blk"), P(req, "blk"), P(req, "blk"))
    return jax.shard_map(
        shards, mesh=split_mesh, in_specs=in_specs, out_specs=out_specs, check_vma=False
    )
```

```python
import math

import jax
import jax.numpy as jnp
from jax import lax
from jax.sharding import Mesh
from jax.sharding import PartitionSpec as P

HEAD_WIDTH = 128
QUERY_LOCAL = 8
KEYVALUE_LOCAL = 1


epsilon = 1e-05
adapter_scale = 2.0
rope_base = 10000.0


def apply_rotation(vectors, cosine_table, sine_table):
    half_size = vectors.shape[-1] // 2
    first_half = vectors[..., :half_size]
    second_half = vectors[..., half_size:]
    turned = jnp.concatenate([-second_half, first_half], axis=-1)
    return vectors * cosine_table + turned * sine_table


def layout(lengths, count):
    slot_index = jnp.arange(count, dtype=jnp.int32)
    prompt_ends = jnp.cumsum(lengths)
    prompt_starts = prompt_ends - lengths
    member = (slot_index[:, None] >= prompt_starts[None, :]) & (
        slot_index[:, None] < prompt_ends[None, :]
    )
    position = jnp.sum(jnp.where(member, slot_index[:, None] - prompt_starts[None, :], 0), axis=1)
    owner = jnp.sum((slot_index[:, None] >= prompt_ends[None, :]).astype(jnp.int32), axis=1)
    return (member.astype(jnp.float32), position, owner, slot_index)


def rope_tables(position, head_size):
    frequency = rope_base ** (-(jnp.arange(head_size // 2, dtype=jnp.float32) * 2.0 / head_size))
    angles = position.astype(jnp.float32)[:, None] * frequency[None, :]
    cosine_table = jnp.cos(angles)
    sine_table = jnp.sin(angles)
    return (
        jnp.concatenate([cosine_table, cosine_table], 1)[:, None, :],
        jnp.concatenate([sine_table, sine_table], 1)[:, None, :],
    )


def gather_blk(piece, n_blk):
    me = lax.axis_index("blk")
    received = [piece]
    for shift in range(1, n_blk):
        pairs = [(i, (i + shift) % n_blk) for i in range(n_blk)]
        received.append(lax.ppermute(piece, "blk", pairs))
    ordered = []
    for source in range(n_blk):
        pick = (me - source) % n_blk
        ordered.append(lax.switch(pick, [lambda s=s: received[s] for s in range(n_blk)]))
    return ordered


def sum_blk(piece, n_blk):
    if n_blk == 2:
        return piece + lax.ppermute(piece, "blk", [(0, 1), (1, 0)])
    return lax.psum(piece, "blk")


def ring_order(count):
    if count % 2 == 0 and count > 2:
        return list(range(0, count, 2)) + list(range(count - 1, 0, -2))
    return list(range(count))


def ring_gather(piece, count, order, direction):
    pairs = [(order[i], order[(i + direction) % count]) for i in range(count)]
    received = [piece]
    current = piece
    for _ in range(count - 1):
        current = lax.ppermute(current, "chip", pairs)
        received.append(current)
    return received


def shards(
    hidden,
    input_norm_gain,
    query_weight,
    keyvalue_weight,
    adapter_down,
    adapter_up_query,
    adapter_up_keyvalue,
    packed_lengths,
    prompt_adapter,
):
    n_blk = lax.axis_size("blk")
    n_lo = lax.axis_size("core")
    n_chip = lax.axis_size("chip")
    row_number, feature_cols = hidden.shape
    full_width = feature_cols * n_blk
    me_blk = lax.axis_index("blk")
    me_core = lax.axis_index("core")
    me_chip = lax.axis_index("chip")

    if n_blk == 2:
        other = lax.ppermute(hidden, "blk", [(0, 1), (1, 0)])
        halves = [lax.select(me_blk == 0, hidden, other), lax.select(me_blk == 0, other, hidden)]
    else:
        halves = gather_blk(hidden, n_blk)
    full_hidden = jnp.concatenate(halves, axis=1)
    values = full_hidden.astype(jnp.float32)
    squares = jnp.sum(values * values, axis=1)
    factor = lax.rsqrt(squares / full_width + epsilon)
    normed = (values * factor[:, None] * input_norm_gain[None, :]).astype(jnp.bfloat16)
    normed_part = lax.dynamic_slice_in_dim(normed, me_blk * feature_cols, feature_cols, 1)

    weight_rows = query_weight.shape[0]
    query_cols = query_weight.shape[1]
    pair_cols = keyvalue_weight.shape[1]
    half_rows = weight_rows // 2

    down_rows = adapter_down.size // query_cols
    upq_rows = adapter_up_query.size // query_cols
    upkv_rows = adapter_up_keyvalue.size // query_cols
    down_flat = adapter_down.reshape(down_rows, query_cols)
    upq_flat = adapter_up_query.reshape(upq_rows, query_cols)
    upkv_flat = adapter_up_keyvalue.reshape(upkv_rows, query_cols)
    dh, uh, vh = down_rows // 2, upq_rows // 2, upkv_rows // 2
    piece_rows = dh + uh + vh
    pad_rows = (-piece_rows) % 8

    def adapter_half(h):
        return jnp.concatenate(
            [
                down_flat[h * dh : (h + 1) * dh],
                upq_flat[h * uh : (h + 1) * uh],
                upkv_flat[h * vh : (h + 1) * vh],
                jnp.zeros((pad_rows, query_cols), jnp.bfloat16),
            ]
        )

    order = ring_order(n_chip)
    inverse = [0] * n_chip
    for i, c in enumerate(order):
        inverse[c] = i
    order_table = jnp.asarray(order, jnp.int32)
    inverse_table = jnp.asarray(inverse, jnp.int32)
    pos = inverse_table[me_chip]
    directions = (1, -1)

    def swap_core(x):
        if n_lo == 1:
            return [x]
        return [x, lax.ppermute(x, "core", [(0, 1), (1, 0)])]

    pair_rows = half_rows * pair_cols // query_cols
    recv = []
    for h, direction in enumerate(directions):
        rows = slice(h * half_rows, (h + 1) * half_rows)
        piece = jnp.concatenate(
            [
                query_weight[rows],
                keyvalue_weight[rows].reshape(pair_rows, query_cols),
                adapter_half(h),
            ],
            axis=0,
        )
        recv.append(ring_gather(piece, n_chip, order, direction))

    total = None
    adapter_steps = [[], []]
    for s in range(n_chip):
        for h, direction in enumerate(directions):
            src_chip = order_table[(pos - s * direction) % n_chip]
            both = swap_core(recv[h][s])
            adapter_steps[h].append(jnp.stack([p[half_rows + pair_rows :] for p in both]))
            for slot, p in enumerate(both):
                src_core = me_core if slot == 0 else n_lo - 1 - me_core
                start = (src_chip * n_lo + src_core) * weight_rows + h * half_rows
                lhs = lax.dynamic_slice_in_dim(normed, start, half_rows, 1)
                rhs = jnp.concatenate(
                    [p[:half_rows], p[half_rows : half_rows + pair_rows].reshape(half_rows, pair_cols)],
                    axis=1,
                )
                part = jnp.dot(lhs, rhs, preferred_element_type=jnp.float32)
                total = part if total is None else total + part
    adapter_pieces = [jnp.stack(a) for a in adapter_steps]

    picked = prompt_adapter[0]
    prompt_count = picked.shape[0]
    a_chip = picked // n_lo
    a_core = picked % n_lo
    a_slot = (a_core != me_core).astype(jnp.int32)
    per_half = []
    for h, direction in enumerate(directions):
        a_step = ((pos - inverse_table[a_chip]) * direction) % n_chip
        per_half.append(adapter_pieces[h][a_step, a_slot])
    down_selected = jnp.concatenate(
        [per_half[0][:, :dh], per_half[1][:, :dh]], axis=1
    ).reshape((prompt_count,) + adapter_down.shape[1:])
    up_query_selected = jnp.concatenate(
        [per_half[0][:, dh : dh + uh], per_half[1][:, dh : dh + uh]], axis=1
    ).reshape((prompt_count,) + adapter_up_query.shape[1:])
    up_pair_selected = jnp.concatenate(
        [per_half[0][:, dh + uh : piece_rows], per_half[1][:, dh + uh : piece_rows]], axis=1
    ).reshape((prompt_count,) + adapter_up_keyvalue.shape[1:])

    query_plain = total[:, :query_cols]
    base_pair = total[:, query_cols:]

    lengths = packed_lengths[0]
    member, position, owner, slot_index = layout(lengths, row_number)
    rank_size = down_selected.shape[2]
    partial_value = lax.dot_general(
        normed_part,
        down_selected.reshape(prompt_count * 3 * rank_size, feature_cols),
        (((1,), (1,)), ((), ())),
        preferred_element_type=jnp.float32,
    )
    partial_value = partial_value.reshape(row_number, prompt_count, 3, rank_size)
    masked = jnp.sum(partial_value * member[:, :, None, None], axis=1).reshape(
        row_number, 3 * rank_size
    )
    low_rank = sum_blk(masked, n_blk).reshape(row_number, 3, rank_size).astype(jnp.bfloat16)
    low_float = low_rank.astype(jnp.float32)

    def spread(column):
        return (
            (member[:, :, None] * low_float[:, None, column, :])
            .astype(jnp.bfloat16)
            .reshape(row_number, prompt_count * rank_size)
        )

    up_keyvalue_selected = up_pair_selected.reshape(
        prompt_count, rank_size, KEYVALUE_LOCAL, 2, HEAD_WIDTH
    )
    query_update = jnp.dot(
        spread(0),
        up_query_selected.reshape(prompt_count * rank_size, query_cols),
        preferred_element_type=jnp.float32,
    )
    key_update = jnp.dot(
        spread(1),
        up_keyvalue_selected[:, :, :, 0].reshape(
            prompt_count * rank_size, KEYVALUE_LOCAL * HEAD_WIDTH
        ),
        preferred_element_type=jnp.float32,
    )
    value_update = jnp.dot(
        spread(2),
        up_keyvalue_selected[:, :, :, 1].reshape(
            prompt_count * rank_size, KEYVALUE_LOCAL * HEAD_WIDTH
        ),
        preferred_element_type=jnp.float32,
    )
    cosine_table, sine_table = rope_tables(position, HEAD_WIDTH)
    query_complete = (query_plain + adapter_scale * query_update).reshape(
        row_number, QUERY_LOCAL * KEYVALUE_LOCAL, HEAD_WIDTH
    )
    query_states = apply_rotation(query_complete, cosine_table, sine_table).astype(jnp.bfloat16)
    keyvalue_plain = base_pair.reshape(row_number, KEYVALUE_LOCAL, 2, HEAD_WIDTH)
    key_vectors = apply_rotation(
        keyvalue_plain[:, :, 0]
        + adapter_scale * key_update.reshape(row_number, KEYVALUE_LOCAL, HEAD_WIDTH),
        cosine_table,
        sine_table,
    ).astype(jnp.bfloat16)
    value_vectors = (
        keyvalue_plain[:, :, 1]
        + adapter_scale * value_update.reshape(row_number, KEYVALUE_LOCAL, HEAD_WIDTH)
    ).astype(jnp.bfloat16)
    grouped = query_states.reshape(row_number, KEYVALUE_LOCAL, QUERY_LOCAL, HEAD_WIDTH)
    scores = jnp.einsum(
        "tkgc,skc->kgts", grouped, key_vectors, preferred_element_type=jnp.float32
    ) / math.sqrt(HEAD_WIDTH)
    allowed = (owner[:, None] == owner[None, :]) & (slot_index[None, :] <= slot_index[:, None])
    scores = jnp.where(allowed[None, None], scores, -1e30)
    row_max = jnp.max(scores, axis=-1, keepdims=True)
    exponent = jnp.exp(scores - row_max)
    attend = (exponent / jnp.sum(exponent, axis=-1, keepdims=True)).astype(jnp.bfloat16)
    context = jnp.einsum(
        "kgts,skc->tkgc", attend, value_vectors, preferred_element_type=jnp.float32
    ).astype(jnp.bfloat16)
    return (
        context.reshape(row_number, KEYVALUE_LOCAL * QUERY_LOCAL * HEAD_WIDTH),
        key_vectors.reshape(row_number, KEYVALUE_LOCAL * HEAD_WIDTH),
        value_vectors.reshape(row_number, KEYVALUE_LOCAL * HEAD_WIDTH),
    )


def solution(mesh):
    n_blk = mesh.shape["blk"]
    n_req = mesh.shape["req"]
    n_lo = 2 if n_req % 2 == 0 else 1
    devices = mesh.devices.reshape(n_blk, n_req // n_lo, n_lo)
    split_mesh = Mesh(devices, ("blk", "chip", "core"))
    req = ("chip", "core")
    in_specs = (
        P(req, "blk"),
        P(),
        P(req, "blk"),
        P(req, "blk"),
        P(req, None, None, "blk"),
        P(req, None, "blk"),
        P(req, None, "blk"),
        P(req, None),
        P(req, None),
    )
    out_specs = (P(req, "blk"), P(req, "blk"), P(req, "blk"))
    return jax.shard_map(
        shards, mesh=split_mesh, in_specs=in_specs, out_specs=out_specs, check_vma=False
    )
```

```python
import math

import jax
import jax.numpy as jnp
from jax import lax
from jax.sharding import Mesh
from jax.sharding import PartitionSpec as P

HEAD_WIDTH = 128
QUERY_LOCAL = 8
KEYVALUE_LOCAL = 1


epsilon = 1e-05
adapter_scale = 2.0
rope_base = 10000.0


def apply_rotation(vectors, cosine_table, sine_table):
    half_size = vectors.shape[-1] // 2
    first_half = vectors[..., :half_size]
    second_half = vectors[..., half_size:]
    turned = jnp.concatenate([-second_half, first_half], axis=-1)
    return vectors * cosine_table + turned * sine_table


def layout(lengths, count):
    slot_index = jnp.arange(count, dtype=jnp.int32)
    prompt_ends = jnp.cumsum(lengths)
    prompt_starts = prompt_ends - lengths
    member = (slot_index[:, None] >= prompt_starts[None, :]) & (
        slot_index[:, None] < prompt_ends[None, :]
    )
    position = jnp.sum(jnp.where(member, slot_index[:, None] - prompt_starts[None, :], 0), axis=1)
    owner = jnp.sum((slot_index[:, None] >= prompt_ends[None, :]).astype(jnp.int32), axis=1)
    return (member.astype(jnp.float32), position, owner, slot_index)


def rope_tables(position, head_size):
    frequency = rope_base ** (-(jnp.arange(head_size // 2, dtype=jnp.float32) * 2.0 / head_size))
    angles = position.astype(jnp.float32)[:, None] * frequency[None, :]
    cosine_table = jnp.cos(angles)
    sine_table = jnp.sin(angles)
    return (
        jnp.concatenate([cosine_table, cosine_table], 1)[:, None, :],
        jnp.concatenate([sine_table, sine_table], 1)[:, None, :],
    )


def gather_blk(piece, n_blk):
    me = lax.axis_index("blk")
    received = [piece]
    for shift in range(1, n_blk):
        pairs = [(i, (i + shift) % n_blk) for i in range(n_blk)]
        received.append(lax.ppermute(piece, "blk", pairs))
    ordered = []
    for source in range(n_blk):
        pick = (me - source) % n_blk
        ordered.append(lax.switch(pick, [lambda s=s: received[s] for s in range(n_blk)]))
    return ordered


def sum_blk(piece, n_blk):
    if n_blk == 2:
        return piece + lax.ppermute(piece, "blk", [(0, 1), (1, 0)])
    return lax.psum(piece, "blk")


def ring_order(count):
    if count % 2 == 0 and count > 2:
        return list(range(0, count, 2)) + list(range(count - 1, 0, -2))
    return list(range(count))


def ring_gather(piece, count, order, direction):
    pairs = [(order[i], order[(i + direction) % count]) for i in range(count)]
    received = [piece]
    current = piece
    for _ in range(count - 1):
        current = lax.ppermute(current, "chip", pairs)
        received.append(current)
    return received


def shards(
    hidden,
    input_norm_gain,
    query_weight,
    keyvalue_weight,
    adapter_down,
    adapter_up_query,
    adapter_up_keyvalue,
    packed_lengths,
    prompt_adapter,
):
    n_blk = lax.axis_size("blk")
    n_lo = lax.axis_size("core")
    n_chip = lax.axis_size("chip")
    row_number, feature_cols = hidden.shape
    full_width = feature_cols * n_blk
    me_blk = lax.axis_index("blk")
    me_core = lax.axis_index("core")
    me_chip = lax.axis_index("chip")

    own_values = hidden.astype(jnp.float32)
    squares = sum_blk(jnp.sum(own_values * own_values, axis=1), n_blk)
    factor = lax.rsqrt(squares / full_width + epsilon)
    gain_part = lax.dynamic_slice_in_dim(input_norm_gain, me_blk * feature_cols, feature_cols, 0)
    normed_part = (own_values * factor[:, None] * gain_part[None, :]).astype(jnp.bfloat16)

    if n_blk == 2:
        other = lax.ppermute(hidden, "blk", [(0, 1), (1, 0)])
        halves = [lax.select(me_blk == 0, hidden, other), lax.select(me_blk == 0, other, hidden)]
    else:
        halves = gather_blk(hidden, n_blk)
    full_hidden = jnp.concatenate(halves, axis=1)
    values = full_hidden.astype(jnp.float32)
    normed = (values * factor[:, None] * input_norm_gain[None, :]).astype(jnp.bfloat16)

    weight_rows = query_weight.shape[0]
    query_cols = query_weight.shape[1]
    pair_cols = keyvalue_weight.shape[1]
    half_rows = weight_rows // 2

    weights = jnp.concatenate([query_weight, keyvalue_weight], axis=1)
    down_rows = adapter_down.size // query_cols
    upq_rows = adapter_up_query.size // query_cols
    upkv_rows = adapter_up_keyvalue.size // query_cols
    adapter_rows = down_rows + upq_rows + upkv_rows
    pad_rows = (-adapter_rows) % 8
    adapter_own = jnp.concatenate(
        [
            adapter_down.reshape(down_rows, query_cols),
            adapter_up_query.reshape(upq_rows, query_cols),
            adapter_up_keyvalue.reshape(upkv_rows, query_cols),
            jnp.zeros((pad_rows, query_cols), jnp.bfloat16),
        ]
    )

    order = ring_order(n_chip)
    inverse = [0] * n_chip
    for i, c in enumerate(order):
        inverse[c] = i
    order_table = jnp.asarray(order, jnp.int32)
    inverse_table = jnp.asarray(inverse, jnp.int32)
    pos = inverse_table[me_chip]
    directions = (1, -1)

    def swap_core(x):
        if n_lo == 1:
            return [x]
        return [x, lax.ppermute(x, "core", [(0, 1), (1, 0)])]

    adapters_chip = lax.all_gather(adapter_own, "chip", axis=0, tiled=False)
    adapter_pieces = jnp.stack(swap_core(adapters_chip))

    picked = prompt_adapter[0]
    prompt_count = picked.shape[0]
    a_slot = (picked % n_lo != me_core).astype(jnp.int32)
    chosen = adapter_pieces[a_slot, picked // n_lo]
    down_selected = chosen[:, :down_rows].reshape((prompt_count,) + adapter_down.shape[1:])
    up_query_selected = chosen[:, down_rows : down_rows + upq_rows].reshape(
        (prompt_count,) + adapter_up_query.shape[1:]
    )
    up_pair_selected = chosen[:, down_rows + upq_rows : adapter_rows].reshape(
        (prompt_count,) + adapter_up_keyvalue.shape[1:]
    )

    lengths = packed_lengths[0]
    member, position, owner, slot_index = layout(lengths, row_number)
    rank_size = down_selected.shape[2]
    partial_value = lax.dot_general(
        normed_part,
        down_selected.reshape(prompt_count * 3 * rank_size, feature_cols),
        (((1,), (1,)), ((), ())),
        preferred_element_type=jnp.float32,
    )
    partial_value = partial_value.reshape(row_number, prompt_count, 3, rank_size)
    masked = jnp.sum(partial_value * member[:, :, None, None], axis=1).reshape(
        row_number, 3 * rank_size
    )
    low_rank = sum_blk(masked, n_blk).reshape(row_number, 3, rank_size).astype(jnp.bfloat16)
    low_float = low_rank.astype(jnp.float32)

    def spread(column):
        return (
            (member[:, :, None] * low_float[:, None, column, :])
            .astype(jnp.bfloat16)
            .reshape(row_number, prompt_count * rank_size)
        )

    up_keyvalue_selected = up_pair_selected.reshape(
        prompt_count, rank_size, KEYVALUE_LOCAL, 2, HEAD_WIDTH
    )
    query_update = jnp.dot(
        spread(0),
        up_query_selected.reshape(prompt_count * rank_size, query_cols),
        preferred_element_type=jnp.float32,
    )
    key_update = jnp.dot(
        spread(1),
        up_keyvalue_selected[:, :, :, 0].reshape(
            prompt_count * rank_size, KEYVALUE_LOCAL * HEAD_WIDTH
        ),
        preferred_element_type=jnp.float32,
    )
    value_update = jnp.dot(
        spread(2),
        up_keyvalue_selected[:, :, :, 1].reshape(
            prompt_count * rank_size, KEYVALUE_LOCAL * HEAD_WIDTH
        ),
        preferred_element_type=jnp.float32,
    )
    cosine_table, sine_table = rope_tables(position, HEAD_WIDTH)

    early = (query_update, key_update, value_update, cosine_table, sine_table)
    tie_step = min(n_chip - 1, n_chip // 2 + 1)
    recv = []
    for h, direction in enumerate(directions):
        pairs = [(order[i], order[(i + direction) % n_chip]) for i in range(n_chip)]
        current = weights[h * half_rows : (h + 1) * half_rows]
        got = [current]
        for s in range(1, n_chip):
            if s == tie_step:
                current, early = lax.optimization_barrier((current, early))
            current = lax.ppermute(current, "chip", pairs)
            got.append(current)
        recv.append(got)
    query_update, key_update, value_update, cosine_table, sine_table = early

    total = None
    for s in range(n_chip):
        for h, direction in enumerate(directions):
            src_chip = order_table[(pos - s * direction) % n_chip]
            for slot, p in enumerate(swap_core(recv[h][s])):
                src_core = me_core if slot == 0 else n_lo - 1 - me_core
                start = (src_chip * n_lo + src_core) * weight_rows + h * half_rows
                lhs = lax.dynamic_slice_in_dim(normed, start, half_rows, 1)
                part = jnp.dot(lhs, p, preferred_element_type=jnp.float32)
                total = part if total is None else total + part


    query_plain = total[:, :query_cols]
    base_pair = total[:, query_cols:]

    query_complete = (query_plain + adapter_scale * query_update).reshape(
        row_number, QUERY_LOCAL * KEYVALUE_LOCAL, HEAD_WIDTH
    )
    query_states = apply_rotation(query_complete, cosine_table, sine_table).astype(jnp.bfloat16)
    keyvalue_plain = base_pair.reshape(row_number, KEYVALUE_LOCAL, 2, HEAD_WIDTH)
    key_vectors = apply_rotation(
        keyvalue_plain[:, :, 0]
        + adapter_scale * key_update.reshape(row_number, KEYVALUE_LOCAL, HEAD_WIDTH),
        cosine_table,
        sine_table,
    ).astype(jnp.bfloat16)
    value_vectors = (
        keyvalue_plain[:, :, 1]
        + adapter_scale * value_update.reshape(row_number, KEYVALUE_LOCAL, HEAD_WIDTH)
    ).astype(jnp.bfloat16)
    grouped = query_states.reshape(row_number, KEYVALUE_LOCAL, QUERY_LOCAL, HEAD_WIDTH)
    scores = jnp.einsum(
        "tkgc,skc->kgts", grouped, key_vectors, preferred_element_type=jnp.float32
    ) / math.sqrt(HEAD_WIDTH)
    allowed = (owner[:, None] == owner[None, :]) & (slot_index[None, :] <= slot_index[:, None])
    scores = jnp.where(allowed[None, None], scores, -1e30)
    row_max = jnp.max(scores, axis=-1, keepdims=True)
    exponent = jnp.exp(scores - row_max)
    attend = (exponent / jnp.sum(exponent, axis=-1, keepdims=True)).astype(jnp.bfloat16)
    context = jnp.einsum(
        "kgts,skc->tkgc", attend, value_vectors, preferred_element_type=jnp.float32
    ).astype(jnp.bfloat16)
    return (
        context.reshape(row_number, KEYVALUE_LOCAL * QUERY_LOCAL * HEAD_WIDTH),
        key_vectors.reshape(row_number, KEYVALUE_LOCAL * HEAD_WIDTH),
        value_vectors.reshape(row_number, KEYVALUE_LOCAL * HEAD_WIDTH),
    )


def solution(mesh):
    n_blk = mesh.shape["blk"]
    n_req = mesh.shape["req"]
    n_lo = 2 if n_req % 2 == 0 else 1
    devices = mesh.devices.reshape(n_blk, n_req // n_lo, n_lo)
    split_mesh = Mesh(devices, ("blk", "chip", "core"))
    req = ("chip", "core")
    in_specs = (
        P(req, "blk"),
        P(),
        P(req, "blk"),
        P(req, "blk"),
        P(req, None, None, "blk"),
        P(req, None, "blk"),
        P(req, None, "blk"),
        P(req, None),
        P(req, None),
    )
    out_specs = (P(req, "blk"), P(req, "blk"), P(req, "blk"))
    return jax.shard_map(
        shards, mesh=split_mesh, in_specs=in_specs, out_specs=out_specs, check_vma=False
    )
```

```python
import math

import jax
import jax.numpy as jnp
from jax import lax
from jax.sharding import Mesh
from jax.sharding import PartitionSpec as P

HEAD_WIDTH = 128
QUERY_LOCAL = 8
KEYVALUE_LOCAL = 1


epsilon = 1e-05
adapter_scale = 2.0
rope_base = 10000.0


def apply_rotation(vectors, cosine_table, sine_table):
    half_size = vectors.shape[-1] // 2
    first_half = vectors[..., :half_size]
    second_half = vectors[..., half_size:]
    turned = jnp.concatenate([-second_half, first_half], axis=-1)
    return vectors * cosine_table + turned * sine_table


def layout(lengths, count):
    slot_index = jnp.arange(count, dtype=jnp.int32)
    prompt_ends = jnp.cumsum(lengths)
    prompt_starts = prompt_ends - lengths
    member = (slot_index[:, None] >= prompt_starts[None, :]) & (
        slot_index[:, None] < prompt_ends[None, :]
    )
    position = jnp.sum(jnp.where(member, slot_index[:, None] - prompt_starts[None, :], 0), axis=1)
    owner = jnp.sum((slot_index[:, None] >= prompt_ends[None, :]).astype(jnp.int32), axis=1)
    return (member.astype(jnp.float32), position, owner, slot_index)


def rope_tables(position, head_size):
    frequency = rope_base ** (-(jnp.arange(head_size // 2, dtype=jnp.float32) * 2.0 / head_size))
    angles = position.astype(jnp.float32)[:, None] * frequency[None, :]
    cosine_table = jnp.cos(angles)
    sine_table = jnp.sin(angles)
    return (
        jnp.concatenate([cosine_table, cosine_table], 1)[:, None, :],
        jnp.concatenate([sine_table, sine_table], 1)[:, None, :],
    )


def gather_blk(piece, n_blk):
    me = lax.axis_index("blk")
    received = [piece]
    for shift in range(1, n_blk):
        pairs = [(i, (i + shift) % n_blk) for i in range(n_blk)]
        received.append(lax.ppermute(piece, "blk", pairs))
    ordered = []
    for source in range(n_blk):
        pick = (me - source) % n_blk
        ordered.append(lax.switch(pick, [lambda s=s: received[s] for s in range(n_blk)]))
    return ordered


def sum_blk(piece, n_blk):
    if n_blk == 2:
        return piece + lax.ppermute(piece, "blk", [(0, 1), (1, 0)])
    return lax.psum(piece, "blk")


def ring_order(count):
    if count % 2 == 0 and count > 2:
        return list(range(0, count, 2)) + list(range(count - 1, 0, -2))
    return list(range(count))


def ring_gather(piece, count, order, direction):
    pairs = [(order[i], order[(i + direction) % count]) for i in range(count)]
    received = [piece]
    current = piece
    for _ in range(count - 1):
        current = lax.ppermute(current, "chip", pairs)
        received.append(current)
    return received


def shards(
    hidden,
    input_norm_gain,
    query_weight,
    keyvalue_weight,
    adapter_down,
    adapter_up_query,
    adapter_up_keyvalue,
    packed_lengths,
    prompt_adapter,
):
    n_blk = lax.axis_size("blk")
    n_lo = lax.axis_size("core")
    n_chip = lax.axis_size("chip")
    row_number, feature_cols = hidden.shape
    full_width = feature_cols * n_blk
    me_blk = lax.axis_index("blk")
    me_core = lax.axis_index("core")
    me_chip = lax.axis_index("chip")

    full_hidden = lax.all_gather(hidden, "blk", axis=1, tiled=True)
    values = full_hidden.astype(jnp.float32)
    squares = jnp.sum(values * values, axis=1)
    factor = lax.rsqrt(squares / full_width + epsilon)
    normed = (values * factor[:, None] * input_norm_gain[None, :]).astype(jnp.bfloat16)
    normed_part = lax.dynamic_slice_in_dim(normed, me_blk * feature_cols, feature_cols, 1)

    weight_rows = query_weight.shape[0]
    query_cols = query_weight.shape[1]
    pair_cols = keyvalue_weight.shape[1]
    half_rows = weight_rows // 2

    weights = jnp.concatenate([query_weight, keyvalue_weight], axis=1)
    down_rows = adapter_down.size // query_cols
    upq_rows = adapter_up_query.size // query_cols
    upkv_rows = adapter_up_keyvalue.size // query_cols
    down_flat = adapter_down.reshape(down_rows, query_cols)
    upq_flat = adapter_up_query.reshape(upq_rows, query_cols)
    upkv_flat = adapter_up_keyvalue.reshape(upkv_rows, query_cols)
    dh, uh, vh = down_rows // 2, upq_rows // 2, upkv_rows // 2
    piece_rows = dh + uh + vh
    pad_rows = (-piece_rows) % 8

    def adapter_half(h):
        return jnp.concatenate(
            [
                down_flat[h * dh : (h + 1) * dh],
                upq_flat[h * uh : (h + 1) * uh],
                upkv_flat[h * vh : (h + 1) * vh],
                jnp.zeros((pad_rows, query_cols), jnp.bfloat16),
            ]
        )

    order = ring_order(n_chip)
    inverse = [0] * n_chip
    for i, c in enumerate(order):
        inverse[c] = i
    order_table = jnp.asarray(order, jnp.int32)
    inverse_table = jnp.asarray(inverse, jnp.int32)
    pos = inverse_table[me_chip]
    directions = (1, -1)

    def swap_core(x):
        if n_lo == 1:
            return [x]
        return [x, lax.ppermute(x, "core", [(0, 1), (1, 0)])]

    pair_width = query_cols + pair_cols
    recv = []
    for h, direction in enumerate(directions):
        adapters_padded = jnp.pad(adapter_half(h), ((0, 0), (0, pair_width - query_cols)))
        piece = jnp.concatenate(
            [weights[h * half_rows : (h + 1) * half_rows], adapters_padded], axis=0
        )
        recv.append(ring_gather(piece, n_chip, order, direction))

    total = None
    adapter_steps = [[], []]
    for s in range(n_chip):
        for h, direction in enumerate(directions):
            src_chip = order_table[(pos - s * direction) % n_chip]
            both = swap_core(recv[h][s])
            adapter_steps[h].append(jnp.stack([p[half_rows:, :query_cols] for p in both]))
            for slot, p in enumerate(both):
                src_core = me_core if slot == 0 else n_lo - 1 - me_core
                start = (src_chip * n_lo + src_core) * weight_rows + h * half_rows
                lhs = lax.dynamic_slice_in_dim(normed, start, half_rows, 1)
                part = jnp.dot(lhs, p[:half_rows], preferred_element_type=jnp.float32)
                total = part if total is None else total + part
    adapter_pieces = [jnp.stack(a) for a in adapter_steps]

    picked = prompt_adapter[0]
    prompt_count = picked.shape[0]
    a_chip = picked // n_lo
    a_core = picked % n_lo
    a_slot = (a_core != me_core).astype(jnp.int32)
    per_half = []
    for h, direction in enumerate(directions):
        a_step = ((pos - inverse_table[a_chip]) * direction) % n_chip
        per_half.append(adapter_pieces[h][a_step, a_slot])
    down_selected = jnp.concatenate(
        [per_half[0][:, :dh], per_half[1][:, :dh]], axis=1
    ).reshape((prompt_count,) + adapter_down.shape[1:])
    up_query_selected = jnp.concatenate(
        [per_half[0][:, dh : dh + uh], per_half[1][:, dh : dh + uh]], axis=1
    ).reshape((prompt_count,) + adapter_up_query.shape[1:])
    up_pair_selected = jnp.concatenate(
        [per_half[0][:, dh + uh : piece_rows], per_half[1][:, dh + uh : piece_rows]], axis=1
    ).reshape((prompt_count,) + adapter_up_keyvalue.shape[1:])

    query_plain = total[:, :query_cols]
    base_pair = total[:, query_cols:]

    lengths = packed_lengths[0]
    member, position, owner, slot_index = layout(lengths, row_number)
    rank_size = down_selected.shape[2]
    partial_value = lax.dot_general(
        normed_part,
        down_selected.reshape(prompt_count * 3 * rank_size, feature_cols),
        (((1,), (1,)), ((), ())),
        preferred_element_type=jnp.float32,
    )
    partial_value = partial_value.reshape(row_number, prompt_count, 3, rank_size)
    masked = jnp.sum(partial_value * member[:, :, None, None], axis=1).reshape(
        row_number, 3 * rank_size
    )
    low_rank = sum_blk(masked, n_blk).reshape(row_number, 3, rank_size).astype(jnp.bfloat16)
    low_float = low_rank.astype(jnp.float32)

    def spread(column):
        return (
            (member[:, :, None] * low_float[:, None, column, :])
            .astype(jnp.bfloat16)
            .reshape(row_number, prompt_count * rank_size)
        )

    up_keyvalue_selected = up_pair_selected.reshape(
        prompt_count, rank_size, KEYVALUE_LOCAL, 2, HEAD_WIDTH
    )
    query_update = jnp.dot(
        spread(0),
        up_query_selected.reshape(prompt_count * rank_size, query_cols),
        preferred_element_type=jnp.float32,
    )
    key_update = jnp.dot(
        spread(1),
        up_keyvalue_selected[:, :, :, 0].reshape(
            prompt_count * rank_size, KEYVALUE_LOCAL * HEAD_WIDTH
        ),
        preferred_element_type=jnp.float32,
    )
    value_update = jnp.dot(
        spread(2),
        up_keyvalue_selected[:, :, :, 1].reshape(
            prompt_count * rank_size, KEYVALUE_LOCAL * HEAD_WIDTH
        ),
        preferred_element_type=jnp.float32,
    )
    cosine_table, sine_table = rope_tables(position, HEAD_WIDTH)
    query_complete = (query_plain + adapter_scale * query_update).reshape(
        row_number, QUERY_LOCAL * KEYVALUE_LOCAL, HEAD_WIDTH
    )
    query_states = apply_rotation(query_complete, cosine_table, sine_table).astype(jnp.bfloat16)
    keyvalue_plain = base_pair.reshape(row_number, KEYVALUE_LOCAL, 2, HEAD_WIDTH)
    key_vectors = apply_rotation(
        keyvalue_plain[:, :, 0]
        + adapter_scale * key_update.reshape(row_number, KEYVALUE_LOCAL, HEAD_WIDTH),
        cosine_table,
        sine_table,
    ).astype(jnp.bfloat16)
    value_vectors = (
        keyvalue_plain[:, :, 1]
        + adapter_scale * value_update.reshape(row_number, KEYVALUE_LOCAL, HEAD_WIDTH)
    ).astype(jnp.bfloat16)
    grouped = query_states.reshape(row_number, KEYVALUE_LOCAL, QUERY_LOCAL, HEAD_WIDTH)
    scores = jnp.einsum(
        "tkgc,skc->kgts", grouped, key_vectors, preferred_element_type=jnp.float32
    ) / math.sqrt(HEAD_WIDTH)
    allowed = (owner[:, None] == owner[None, :]) & (slot_index[None, :] <= slot_index[:, None])
    scores = jnp.where(allowed[None, None], scores, -1e30)
    row_max = jnp.max(scores, axis=-1, keepdims=True)
    exponent = jnp.exp(scores - row_max)
    attend = (exponent / jnp.sum(exponent, axis=-1, keepdims=True)).astype(jnp.bfloat16)
    context = jnp.einsum(
        "kgts,skc->tkgc", attend, value_vectors, preferred_element_type=jnp.float32
    ).astype(jnp.bfloat16)
    return (
        context.reshape(row_number, KEYVALUE_LOCAL * QUERY_LOCAL * HEAD_WIDTH),
        key_vectors.reshape(row_number, KEYVALUE_LOCAL * HEAD_WIDTH),
        value_vectors.reshape(row_number, KEYVALUE_LOCAL * HEAD_WIDTH),
    )


def solution(mesh):
    n_blk = mesh.shape["blk"]
    n_req = mesh.shape["req"]
    n_lo = 2 if n_req % 2 == 0 else 1
    devices = mesh.devices.reshape(n_blk, n_req // n_lo, n_lo)
    split_mesh = Mesh(devices, ("blk", "chip", "core"))
    req = ("chip", "core")
    in_specs = (
        P(req, "blk"),
        P(),
        P(req, "blk"),
        P(req, "blk"),
        P(req, None, None, "blk"),
        P(req, None, "blk"),
        P(req, None, "blk"),
        P(req, None),
        P(req, None),
    )
    out_specs = (P(req, "blk"), P(req, "blk"), P(req, "blk"))
    return jax.shard_map(
        shards, mesh=split_mesh, in_specs=in_specs, out_specs=out_specs, check_vma=False
    )
```

```python
import math

import jax
import jax.numpy as jnp
from jax import lax
from jax.sharding import Mesh
from jax.sharding import PartitionSpec as P

HEAD_WIDTH = 128
QUERY_LOCAL = 8
KEYVALUE_LOCAL = 1


epsilon = 1e-05
adapter_scale = 2.0
rope_base = 10000.0


def apply_rotation(vectors, cosine_table, sine_table):
    half_size = vectors.shape[-1] // 2
    first_half = vectors[..., :half_size]
    second_half = vectors[..., half_size:]
    turned = jnp.concatenate([-second_half, first_half], axis=-1)
    return vectors * cosine_table + turned * sine_table


def layout(lengths, count):
    slot_index = jnp.arange(count, dtype=jnp.int32)
    prompt_ends = jnp.cumsum(lengths)
    prompt_starts = prompt_ends - lengths
    member = (slot_index[:, None] >= prompt_starts[None, :]) & (
        slot_index[:, None] < prompt_ends[None, :]
    )
    position = jnp.sum(jnp.where(member, slot_index[:, None] - prompt_starts[None, :], 0), axis=1)
    owner = jnp.sum((slot_index[:, None] >= prompt_ends[None, :]).astype(jnp.int32), axis=1)
    return (member.astype(jnp.float32), position, owner, slot_index)


def rope_tables(position, head_size):
    frequency = rope_base ** (-(jnp.arange(head_size // 2, dtype=jnp.float32) * 2.0 / head_size))
    angles = position.astype(jnp.float32)[:, None] * frequency[None, :]
    cosine_table = jnp.cos(angles)
    sine_table = jnp.sin(angles)
    return (
        jnp.concatenate([cosine_table, cosine_table], 1)[:, None, :],
        jnp.concatenate([sine_table, sine_table], 1)[:, None, :],
    )


def gather_blk(piece, n_blk):
    me = lax.axis_index("blk")
    received = [piece]
    for shift in range(1, n_blk):
        pairs = [(i, (i + shift) % n_blk) for i in range(n_blk)]
        received.append(lax.ppermute(piece, "blk", pairs))
    ordered = []
    for source in range(n_blk):
        pick = (me - source) % n_blk
        ordered.append(lax.switch(pick, [lambda s=s: received[s] for s in range(n_blk)]))
    return ordered


def sum_blk(piece, n_blk):
    if n_blk == 2:
        return piece + lax.ppermute(piece, "blk", [(0, 1), (1, 0)])
    return lax.psum(piece, "blk")


def ring_order(count):
    if count % 2 == 0 and count > 2:
        return list(range(0, count, 2)) + list(range(count - 1, 0, -2))
    return list(range(count))


def ring_gather(piece, count, order, direction):
    pairs = [(order[i], order[(i + direction) % count]) for i in range(count)]
    received = [piece]
    current = piece
    for _ in range(count - 1):
        current = lax.ppermute(current, "chip", pairs)
        received.append(current)
    return received


def shards(
    hidden,
    input_norm_gain,
    query_weight,
    keyvalue_weight,
    adapter_down,
    adapter_up_query,
    adapter_up_keyvalue,
    packed_lengths,
    prompt_adapter,
):
    n_blk = lax.axis_size("blk")
    n_lo = lax.axis_size("core")
    n_chip = lax.axis_size("chip")
    row_number, feature_cols = hidden.shape
    full_width = feature_cols * n_blk
    me_blk = lax.axis_index("blk")
    me_core = lax.axis_index("core")
    me_chip = lax.axis_index("chip")

    own_values = hidden.astype(jnp.float32)
    squares = sum_blk(jnp.sum(own_values * own_values, axis=1), n_blk)
    factor = lax.rsqrt(squares / full_width + epsilon)
    gain_part = lax.dynamic_slice_in_dim(input_norm_gain, me_blk * feature_cols, feature_cols, 0)
    normed_part = (own_values * factor[:, None] * gain_part[None, :]).astype(jnp.bfloat16)

    if n_blk == 2:
        other = lax.ppermute(hidden, "blk", [(0, 1), (1, 0)])
        halves = [lax.select(me_blk == 0, hidden, other), lax.select(me_blk == 0, other, hidden)]
    else:
        halves = gather_blk(hidden, n_blk)
    full_hidden = jnp.concatenate(halves, axis=1)
    values = full_hidden.astype(jnp.float32)
    normed = (values * factor[:, None] * input_norm_gain[None, :]).astype(jnp.bfloat16)

    weight_rows = query_weight.shape[0]
    query_cols = query_weight.shape[1]
    pair_cols = keyvalue_weight.shape[1]
    half_rows = weight_rows // 2

    weights = jnp.concatenate([query_weight, keyvalue_weight], axis=1)
    down_rows = adapter_down.size // query_cols
    upq_rows = adapter_up_query.size // query_cols
    upkv_rows = adapter_up_keyvalue.size // query_cols
    adapter_rows = down_rows + upq_rows + upkv_rows
    pad_rows = (-adapter_rows) % 8
    adapter_own = jnp.concatenate(
        [
            adapter_down.reshape(down_rows, query_cols),
            adapter_up_query.reshape(upq_rows, query_cols),
            adapter_up_keyvalue.reshape(upkv_rows, query_cols),
            jnp.zeros((pad_rows, query_cols), jnp.bfloat16),
        ]
    )

    order = ring_order(n_chip)
    inverse = [0] * n_chip
    for i, c in enumerate(order):
        inverse[c] = i
    order_table = jnp.asarray(order, jnp.int32)
    inverse_table = jnp.asarray(inverse, jnp.int32)
    pos = inverse_table[me_chip]
    directions = (1, -1)

    def swap_core(x):
        if n_lo == 1:
            return [x]
        return [x, lax.ppermute(x, "core", [(0, 1), (1, 0)])]

    adapters_chip = lax.all_gather(adapter_own, "chip", axis=0, tiled=False)
    adapter_pieces = jnp.stack(swap_core(adapters_chip))

    picked = prompt_adapter[0]
    prompt_count = picked.shape[0]
    a_slot = (picked % n_lo != me_core).astype(jnp.int32)
    chosen = adapter_pieces[a_slot, picked // n_lo]
    down_selected = chosen[:, :down_rows].reshape((prompt_count,) + adapter_down.shape[1:])
    up_query_selected = chosen[:, down_rows : down_rows + upq_rows].reshape(
        (prompt_count,) + adapter_up_query.shape[1:]
    )
    up_pair_selected = chosen[:, down_rows + upq_rows : adapter_rows].reshape(
        (prompt_count,) + adapter_up_keyvalue.shape[1:]
    )

    lengths = packed_lengths[0]
    member, position, owner, slot_index = layout(lengths, row_number)
    rank_size = down_selected.shape[2]
    partial_value = lax.dot_general(
        normed_part,
        down_selected.reshape(prompt_count * 3 * rank_size, feature_cols),
        (((1,), (1,)), ((), ())),
        preferred_element_type=jnp.float32,
    )
    partial_value = partial_value.reshape(row_number, prompt_count, 3, rank_size)
    masked = jnp.sum(partial_value * member[:, :, None, None], axis=1).reshape(
        row_number, 3 * rank_size
    )
    low_rank = sum_blk(masked, n_blk).reshape(row_number, 3, rank_size).astype(jnp.bfloat16)
    low_float = low_rank.astype(jnp.float32)

    def spread(column):
        return (
            (member[:, :, None] * low_float[:, None, column, :])
            .astype(jnp.bfloat16)
            .reshape(row_number, prompt_count * rank_size)
        )

    up_keyvalue_selected = up_pair_selected.reshape(
        prompt_count, rank_size, KEYVALUE_LOCAL, 2, HEAD_WIDTH
    )
    query_update = jnp.dot(
        spread(0),
        up_query_selected.reshape(prompt_count * rank_size, query_cols),
        preferred_element_type=jnp.float32,
    )
    key_update = jnp.dot(
        spread(1),
        up_keyvalue_selected[:, :, :, 0].reshape(
            prompt_count * rank_size, KEYVALUE_LOCAL * HEAD_WIDTH
        ),
        preferred_element_type=jnp.float32,
    )
    value_update = jnp.dot(
        spread(2),
        up_keyvalue_selected[:, :, :, 1].reshape(
            prompt_count * rank_size, KEYVALUE_LOCAL * HEAD_WIDTH
        ),
        preferred_element_type=jnp.float32,
    )
    cosine_table, sine_table = rope_tables(position, HEAD_WIDTH)

    recv = [
        ring_gather(weights[h * half_rows : (h + 1) * half_rows], n_chip, order, direction)
        for h, direction in enumerate(directions)
    ]

    total = adapter_scale * jnp.concatenate([query_update, key_update, value_update], axis=1)
    for s in range(n_chip):
        for h, direction in enumerate(directions):
            src_chip = order_table[(pos - s * direction) % n_chip]
            for slot, p in enumerate(swap_core(recv[h][s])):
                src_core = me_core if slot == 0 else n_lo - 1 - me_core
                start = (src_chip * n_lo + src_core) * weight_rows + h * half_rows
                lhs = lax.dynamic_slice_in_dim(normed, start, half_rows, 1)
                part = jnp.dot(lhs, p, preferred_element_type=jnp.float32)
                total = total + part


    query_plain = total[:, :query_cols]
    base_pair = total[:, query_cols:]

    query_complete = query_plain.reshape(row_number, QUERY_LOCAL * KEYVALUE_LOCAL, HEAD_WIDTH)
    query_states = apply_rotation(query_complete, cosine_table, sine_table).astype(jnp.bfloat16)
    keyvalue_plain = base_pair.reshape(row_number, KEYVALUE_LOCAL, 2, HEAD_WIDTH)
    key_vectors = apply_rotation(keyvalue_plain[:, :, 0], cosine_table, sine_table).astype(
        jnp.bfloat16
    )
    value_vectors = keyvalue_plain[:, :, 1].astype(jnp.bfloat16)
    grouped = query_states.reshape(row_number, KEYVALUE_LOCAL, QUERY_LOCAL, HEAD_WIDTH)
    scores = jnp.einsum(
        "tkgc,skc->kgts", grouped, key_vectors, preferred_element_type=jnp.float32
    ) / math.sqrt(HEAD_WIDTH)
    allowed = (owner[:, None] == owner[None, :]) & (slot_index[None, :] <= slot_index[:, None])
    scores = jnp.where(allowed[None, None], scores, -1e30)
    row_max = jnp.max(scores, axis=-1, keepdims=True)
    exponent = jnp.exp(scores - row_max)
    attend = (exponent / jnp.sum(exponent, axis=-1, keepdims=True)).astype(jnp.bfloat16)
    context = jnp.einsum(
        "kgts,skc->tkgc", attend, value_vectors, preferred_element_type=jnp.float32
    ).astype(jnp.bfloat16)
    return (
        context.reshape(row_number, KEYVALUE_LOCAL * QUERY_LOCAL * HEAD_WIDTH),
        key_vectors.reshape(row_number, KEYVALUE_LOCAL * HEAD_WIDTH),
        value_vectors.reshape(row_number, KEYVALUE_LOCAL * HEAD_WIDTH),
    )


def solution(mesh):
    n_blk = mesh.shape["blk"]
    n_req = mesh.shape["req"]
    n_lo = 2 if n_req % 2 == 0 else 1
    devices = mesh.devices.reshape(n_blk, n_req // n_lo, n_lo)
    split_mesh = Mesh(devices, ("blk", "chip", "core"))
    req = ("chip", "core")
    in_specs = (
        P(req, "blk"),
        P(),
        P(req, "blk"),
        P(req, "blk"),
        P(req, None, None, "blk"),
        P(req, None, "blk"),
        P(req, None, "blk"),
        P(req, None),
        P(req, None),
    )
    out_specs = (P(req, "blk"), P(req, "blk"), P(req, "blk"))
    return jax.shard_map(
        shards, mesh=split_mesh, in_specs=in_specs, out_specs=out_specs, check_vma=False
    )
```

```python
import math

import jax
import jax.numpy as jnp
from jax import lax
from jax.sharding import Mesh
from jax.sharding import PartitionSpec as P

HEAD_WIDTH = 128
QUERY_LOCAL = 8
KEYVALUE_LOCAL = 1


epsilon = 1e-05
adapter_scale = 2.0
rope_base = 10000.0


def apply_rotation(vectors, cosine_table, sine_table):
    half_size = vectors.shape[-1] // 2
    first_half = vectors[..., :half_size]
    second_half = vectors[..., half_size:]
    turned = jnp.concatenate([-second_half, first_half], axis=-1)
    return vectors * cosine_table + turned * sine_table


def layout(lengths, count):
    slot_index = jnp.arange(count, dtype=jnp.int32)
    prompt_ends = jnp.cumsum(lengths)
    prompt_starts = prompt_ends - lengths
    member = (slot_index[:, None] >= prompt_starts[None, :]) & (
        slot_index[:, None] < prompt_ends[None, :]
    )
    position = jnp.sum(jnp.where(member, slot_index[:, None] - prompt_starts[None, :], 0), axis=1)
    owner = jnp.sum((slot_index[:, None] >= prompt_ends[None, :]).astype(jnp.int32), axis=1)
    return (member.astype(jnp.float32), position, owner, slot_index)


def rope_tables(position, head_size):
    frequency = rope_base ** (-(jnp.arange(head_size // 2, dtype=jnp.float32) * 2.0 / head_size))
    angles = position.astype(jnp.float32)[:, None] * frequency[None, :]
    cosine_table = jnp.cos(angles)
    sine_table = jnp.sin(angles)
    return (
        jnp.concatenate([cosine_table, cosine_table], 1)[:, None, :],
        jnp.concatenate([sine_table, sine_table], 1)[:, None, :],
    )


def gather_blk(piece, n_blk):
    me = lax.axis_index("blk")
    received = [piece]
    for shift in range(1, n_blk):
        pairs = [(i, (i + shift) % n_blk) for i in range(n_blk)]
        received.append(lax.ppermute(piece, "blk", pairs))
    ordered = []
    for source in range(n_blk):
        pick = (me - source) % n_blk
        ordered.append(lax.switch(pick, [lambda s=s: received[s] for s in range(n_blk)]))
    return ordered


def sum_blk(piece, n_blk):
    if n_blk == 2:
        return piece + lax.ppermute(piece, "blk", [(0, 1), (1, 0)])
    return lax.psum(piece, "blk")


def ring_order(count):
    if count % 2 == 0 and count > 2:
        return list(range(0, count, 2)) + list(range(count - 1, 0, -2))
    return list(range(count))


def ring_gather(piece, count, order, direction):
    pairs = [(order[i], order[(i + direction) % count]) for i in range(count)]
    received = [piece]
    current = piece
    for _ in range(count - 1):
        current = lax.ppermute(current, "chip", pairs)
        received.append(current)
    return received


def shards(
    hidden,
    input_norm_gain,
    query_weight,
    keyvalue_weight,
    adapter_down,
    adapter_up_query,
    adapter_up_keyvalue,
    packed_lengths,
    prompt_adapter,
):
    n_blk = lax.axis_size("blk")
    n_lo = lax.axis_size("core")
    n_chip = lax.axis_size("chip")
    row_number, feature_cols = hidden.shape
    full_width = feature_cols * n_blk
    me_blk = lax.axis_index("blk")
    me_core = lax.axis_index("core")
    me_chip = lax.axis_index("chip")

    if n_blk == 2:
        other = lax.ppermute(hidden, "blk", [(0, 1), (1, 0)])
        halves = [lax.select(me_blk == 0, hidden, other), lax.select(me_blk == 0, other, hidden)]
    else:
        halves = gather_blk(hidden, n_blk)
    full_hidden = jnp.concatenate(halves, axis=1)
    values = full_hidden.astype(jnp.float32)
    squares = jnp.sum(values * values, axis=1)
    factor = lax.rsqrt(squares / full_width + epsilon)
    normed = (values * factor[:, None] * input_norm_gain[None, :]).astype(jnp.bfloat16)
    normed_part = lax.dynamic_slice_in_dim(normed, me_blk * feature_cols, feature_cols, 1)

    weight_rows = query_weight.shape[0]
    query_cols = query_weight.shape[1]
    pair_cols = keyvalue_weight.shape[1]
    half_rows = weight_rows // 2

    weights = jnp.concatenate([query_weight, keyvalue_weight], axis=1)
    down_rows = adapter_down.size // query_cols
    upq_rows = adapter_up_query.size // query_cols
    upkv_rows = adapter_up_keyvalue.size // query_cols
    down_flat = adapter_down.reshape(down_rows, query_cols)
    upq_flat = adapter_up_query.reshape(upq_rows, query_cols)
    upkv_flat = adapter_up_keyvalue.reshape(upkv_rows, query_cols)
    dh, uh, vh = down_rows // 2, upq_rows // 2, upkv_rows // 2
    piece_rows = dh + uh + vh
    pad_rows = (-piece_rows) % 8

    def adapter_half(h):
        return jnp.concatenate(
            [
                down_flat[h * dh : (h + 1) * dh],
                upq_flat[h * uh : (h + 1) * uh],
                upkv_flat[h * vh : (h + 1) * vh],
                jnp.zeros((pad_rows, query_cols), jnp.bfloat16),
            ]
        )

    order = ring_order(n_chip)
    inverse = [0] * n_chip
    for i, c in enumerate(order):
        inverse[c] = i
    order_table = jnp.asarray(order, jnp.int32)
    inverse_table = jnp.asarray(inverse, jnp.int32)
    pos = inverse_table[me_chip]
    directions = (1, -1)

    def swap_core(x):
        if n_lo == 1:
            return [x]
        return [x, lax.ppermute(x, "core", [(0, 1), (1, 0)])]

    pair_width = query_cols + pair_cols
    recv = []
    for h, direction in enumerate(directions):
        adapters_padded = jnp.pad(adapter_half(h), ((0, 0), (0, pair_width - query_cols)))
        piece = jnp.concatenate(
            [weights[h * half_rows : (h + 1) * half_rows], adapters_padded], axis=0
        )
        recv.append(ring_gather(piece, n_chip, order, direction))

    total = None
    adapter_steps = [[], []]
    for s in range(n_chip):
        for h, direction in enumerate(directions):
            src_chip = order_table[(pos - s * direction) % n_chip]
            both = swap_core(recv[h][s])
            adapter_steps[h].append(jnp.stack([p[half_rows:, :query_cols] for p in both]))
            for slot, p in enumerate(both):
                src_core = me_core if slot == 0 else n_lo - 1 - me_core
                start = (src_chip * n_lo + src_core) * weight_rows + h * half_rows
                lhs = lax.dynamic_slice_in_dim(normed, start, half_rows, 1)
                part = jnp.dot(lhs, p[:half_rows], preferred_element_type=jnp.float32)
                total = part if total is None else total + part
    adapter_pieces = [jnp.stack(a) for a in adapter_steps]

    picked = prompt_adapter[0]
    prompt_count = picked.shape[0]
    a_chip = picked // n_lo
    a_core = picked % n_lo
    a_slot = (a_core != me_core).astype(jnp.int32)
    per_half = []
    piece_ids = jnp.arange(n_chip * n_lo, dtype=jnp.int32)
    for h, direction in enumerate(directions):
        a_step = ((pos - inverse_table[a_chip]) * direction) % n_chip
        one_hot = (a_step[:, None] * n_lo + a_slot[:, None] == piece_ids[None, :]).astype(
            jnp.bfloat16
        )
        stacked = adapter_pieces[h].reshape((n_chip * n_lo,) + adapter_pieces[h].shape[2:])
        per_half.append(
            jnp.einsum("pk,krc->prc", one_hot, stacked, preferred_element_type=jnp.float32).astype(
                jnp.bfloat16
            )
        )
    down_selected = jnp.concatenate(
        [per_half[0][:, :dh], per_half[1][:, :dh]], axis=1
    ).reshape((prompt_count,) + adapter_down.shape[1:])
    up_query_selected = jnp.concatenate(
        [per_half[0][:, dh : dh + uh], per_half[1][:, dh : dh + uh]], axis=1
    ).reshape((prompt_count,) + adapter_up_query.shape[1:])
    up_pair_selected = jnp.concatenate(
        [per_half[0][:, dh + uh : piece_rows], per_half[1][:, dh + uh : piece_rows]], axis=1
    ).reshape((prompt_count,) + adapter_up_keyvalue.shape[1:])

    query_plain = total[:, :query_cols]
    base_pair = total[:, query_cols:]

    lengths = packed_lengths[0]
    member, position, owner, slot_index = layout(lengths, row_number)
    rank_size = down_selected.shape[2]
    partial_value = lax.dot_general(
        normed_part,
        down_selected.reshape(prompt_count * 3 * rank_size, feature_cols),
        (((1,), (1,)), ((), ())),
        preferred_element_type=jnp.float32,
    )
    partial_value = partial_value.reshape(row_number, prompt_count, 3, rank_size)
    masked = jnp.sum(partial_value * member[:, :, None, None], axis=1).reshape(
        row_number, 3 * rank_size
    )
    low_rank = sum_blk(masked, n_blk).reshape(row_number, 3, rank_size).astype(jnp.bfloat16)
    low_float = low_rank.astype(jnp.float32)

    def spread(column):
        return (
            (member[:, :, None] * low_float[:, None, column, :])
            .astype(jnp.bfloat16)
            .reshape(row_number, prompt_count * rank_size)
        )

    up_keyvalue_selected = up_pair_selected.reshape(
        prompt_count, rank_size, KEYVALUE_LOCAL, 2, HEAD_WIDTH
    )
    query_update = jnp.dot(
        spread(0),
        up_query_selected.reshape(prompt_count * rank_size, query_cols),
        preferred_element_type=jnp.float32,
    )
    key_update = jnp.dot(
        spread(1),
        up_keyvalue_selected[:, :, :, 0].reshape(
            prompt_count * rank_size, KEYVALUE_LOCAL * HEAD_WIDTH
        ),
        preferred_element_type=jnp.float32,
    )
    value_update = jnp.dot(
        spread(2),
        up_keyvalue_selected[:, :, :, 1].reshape(
            prompt_count * rank_size, KEYVALUE_LOCAL * HEAD_WIDTH
        ),
        preferred_element_type=jnp.float32,
    )
    cosine_table, sine_table = rope_tables(position, HEAD_WIDTH)
    query_complete = (query_plain + adapter_scale * query_update).reshape(
        row_number, QUERY_LOCAL * KEYVALUE_LOCAL, HEAD_WIDTH
    )
    query_states = apply_rotation(query_complete, cosine_table, sine_table).astype(jnp.bfloat16)
    keyvalue_plain = base_pair.reshape(row_number, KEYVALUE_LOCAL, 2, HEAD_WIDTH)
    key_vectors = apply_rotation(
        keyvalue_plain[:, :, 0]
        + adapter_scale * key_update.reshape(row_number, KEYVALUE_LOCAL, HEAD_WIDTH),
        cosine_table,
        sine_table,
    ).astype(jnp.bfloat16)
    value_vectors = (
        keyvalue_plain[:, :, 1]
        + adapter_scale * value_update.reshape(row_number, KEYVALUE_LOCAL, HEAD_WIDTH)
    ).astype(jnp.bfloat16)
    grouped = query_states.reshape(row_number, KEYVALUE_LOCAL, QUERY_LOCAL, HEAD_WIDTH)
    scores = jnp.einsum(
        "tkgc,skc->kgts", grouped, key_vectors, preferred_element_type=jnp.float32
    ) / math.sqrt(HEAD_WIDTH)
    allowed = (owner[:, None] == owner[None, :]) & (slot_index[None, :] <= slot_index[:, None])
    scores = jnp.where(allowed[None, None], scores, -1e30)
    row_max = jnp.max(scores, axis=-1, keepdims=True)
    exponent = jnp.exp(scores - row_max)
    attend = (exponent / jnp.sum(exponent, axis=-1, keepdims=True)).astype(jnp.bfloat16)
    context = jnp.einsum(
        "kgts,skc->tkgc", attend, value_vectors, preferred_element_type=jnp.float32
    ).astype(jnp.bfloat16)
    return (
        context.reshape(row_number, KEYVALUE_LOCAL * QUERY_LOCAL * HEAD_WIDTH),
        key_vectors.reshape(row_number, KEYVALUE_LOCAL * HEAD_WIDTH),
        value_vectors.reshape(row_number, KEYVALUE_LOCAL * HEAD_WIDTH),
    )


def solution(mesh):
    n_blk = mesh.shape["blk"]
    n_req = mesh.shape["req"]
    n_lo = 2 if n_req % 2 == 0 else 1
    devices = mesh.devices.reshape(n_blk, n_req // n_lo, n_lo)
    split_mesh = Mesh(devices, ("blk", "chip", "core"))
    req = ("chip", "core")
    in_specs = (
        P(req, "blk"),
        P(),
        P(req, "blk"),
        P(req, "blk"),
        P(req, None, None, "blk"),
        P(req, None, "blk"),
        P(req, None, "blk"),
        P(req, None),
        P(req, None),
    )
    out_specs = (P(req, "blk"), P(req, "blk"), P(req, "blk"))
    return jax.shard_map(
        shards, mesh=split_mesh, in_specs=in_specs, out_specs=out_specs, check_vma=False
    )
```

```python
import math

import jax
import jax.numpy as jnp
from jax import lax
from jax.sharding import Mesh
from jax.sharding import PartitionSpec as P

HEAD_WIDTH = 128
QUERY_LOCAL = 8
KEYVALUE_LOCAL = 1


epsilon = 1e-05
adapter_scale = 2.0
rope_base = 10000.0


def apply_rotation(vectors, cosine_table, sine_table):
    half_size = vectors.shape[-1] // 2
    first_half = vectors[..., :half_size]
    second_half = vectors[..., half_size:]
    turned = jnp.concatenate([-second_half, first_half], axis=-1)
    return vectors * cosine_table + turned * sine_table


def layout(lengths, count):
    slot_index = jnp.arange(count, dtype=jnp.int32)
    prompt_ends = jnp.cumsum(lengths)
    prompt_starts = prompt_ends - lengths
    member = (slot_index[:, None] >= prompt_starts[None, :]) & (
        slot_index[:, None] < prompt_ends[None, :]
    )
    position = jnp.sum(jnp.where(member, slot_index[:, None] - prompt_starts[None, :], 0), axis=1)
    owner = jnp.sum((slot_index[:, None] >= prompt_ends[None, :]).astype(jnp.int32), axis=1)
    return (member.astype(jnp.float32), position, owner, slot_index)


def rope_tables(position, head_size):
    frequency = rope_base ** (-(jnp.arange(head_size // 2, dtype=jnp.float32) * 2.0 / head_size))
    angles = position.astype(jnp.float32)[:, None] * frequency[None, :]
    cosine_table = jnp.cos(angles)
    sine_table = jnp.sin(angles)
    return (
        jnp.concatenate([cosine_table, cosine_table], 1)[:, None, :],
        jnp.concatenate([sine_table, sine_table], 1)[:, None, :],
    )


def gather_blk(piece, n_blk):
    me = lax.axis_index("blk")
    received = [piece]
    for shift in range(1, n_blk):
        pairs = [(i, (i + shift) % n_blk) for i in range(n_blk)]
        received.append(lax.ppermute(piece, "blk", pairs))
    ordered = []
    for source in range(n_blk):
        pick = (me - source) % n_blk
        ordered.append(lax.switch(pick, [lambda s=s: received[s] for s in range(n_blk)]))
    return ordered


def sum_blk(piece, n_blk):
    if n_blk == 2:
        return piece + lax.ppermute(piece, "blk", [(0, 1), (1, 0)])
    return lax.psum(piece, "blk")


def ring_order(count):
    if count % 2 == 0 and count > 2:
        return list(range(0, count, 2)) + list(range(count - 1, 0, -2))
    return list(range(count))


def ring_gather(piece, count, order, direction):
    pairs = [(order[i], order[(i + direction) % count]) for i in range(count)]
    received = [piece]
    current = piece
    for _ in range(count - 1):
        current = lax.ppermute(current, "chip", pairs)
        received.append(current)
    return received


def shards(
    hidden,
    input_norm_gain,
    query_weight,
    keyvalue_weight,
    adapter_down,
    adapter_up_query,
    adapter_up_keyvalue,
    packed_lengths,
    prompt_adapter,
):
    n_blk = lax.axis_size("blk")
    n_lo = lax.axis_size("core")
    n_chip = lax.axis_size("chip")
    row_number, feature_cols = hidden.shape
    full_width = feature_cols * n_blk
    me_blk = lax.axis_index("blk")
    me_core = lax.axis_index("core")
    me_chip = lax.axis_index("chip")

    if n_blk == 2:
        other = lax.ppermute(hidden, "blk", [(0, 1), (1, 0)])
        halves = [lax.select(me_blk == 0, hidden, other), lax.select(me_blk == 0, other, hidden)]
    else:
        halves = gather_blk(hidden, n_blk)
    full_hidden = jnp.concatenate(halves, axis=1)
    values = full_hidden.astype(jnp.float32)
    squares = jnp.sum(values * values, axis=1)
    factor = lax.rsqrt(squares / full_width + epsilon)
    normed = (values * factor[:, None] * input_norm_gain[None, :]).astype(jnp.bfloat16)
    normed_part = lax.dynamic_slice_in_dim(normed, me_blk * feature_cols, feature_cols, 1)

    weight_rows = query_weight.shape[0]
    query_cols = query_weight.shape[1]
    pair_cols = keyvalue_weight.shape[1]
    half_rows = weight_rows // 2

    weights = jnp.concatenate([query_weight, keyvalue_weight], axis=1)
    down_rows = adapter_down.size // query_cols
    upq_rows = adapter_up_query.size // query_cols
    upkv_rows = adapter_up_keyvalue.size // query_cols
    quarters = feature_cols // query_cols
    map_rows = adapter_down.size // feature_cols
    half_maps = map_rows // 2
    down_flat = (
        adapter_down.reshape(2, half_maps, quarters, query_cols)
        .transpose(0, 2, 1, 3)
        .reshape(down_rows, query_cols)
    )
    upq_flat = adapter_up_query.reshape(upq_rows, query_cols)
    upkv_flat = adapter_up_keyvalue.reshape(upkv_rows, query_cols)
    dh, uh, vh = down_rows // 2, upq_rows // 2, upkv_rows // 2
    piece_rows = dh + uh + vh
    pad_rows = (-piece_rows) % 8

    def adapter_half(h):
        return jnp.concatenate(
            [
                down_flat[h * dh : (h + 1) * dh],
                upq_flat[h * uh : (h + 1) * uh],
                upkv_flat[h * vh : (h + 1) * vh],
                jnp.zeros((pad_rows, query_cols), jnp.bfloat16),
            ]
        )

    order = ring_order(n_chip)
    inverse = [0] * n_chip
    for i, c in enumerate(order):
        inverse[c] = i
    order_table = jnp.asarray(order, jnp.int32)
    inverse_table = jnp.asarray(inverse, jnp.int32)
    pos = inverse_table[me_chip]
    directions = (1, -1)

    def swap_core(x):
        if n_lo == 1:
            return [x]
        return [x, lax.ppermute(x, "core", [(0, 1), (1, 0)])]

    pair_width = query_cols + pair_cols
    recv = []
    for h, direction in enumerate(directions):
        adapters_padded = jnp.pad(adapter_half(h), ((0, 0), (0, pair_width - query_cols)))
        piece = jnp.concatenate(
            [weights[h * half_rows : (h + 1) * half_rows], adapters_padded], axis=0
        )
        recv.append(ring_gather(piece, n_chip, order, direction))

    total = None
    adapter_steps = [[], []]
    for s in range(n_chip):
        for h, direction in enumerate(directions):
            src_chip = order_table[(pos - s * direction) % n_chip]
            both = swap_core(recv[h][s])
            adapter_steps[h].append(jnp.stack([p[half_rows:, :query_cols] for p in both]))
            for slot, p in enumerate(both):
                src_core = me_core if slot == 0 else n_lo - 1 - me_core
                start = (src_chip * n_lo + src_core) * weight_rows + h * half_rows
                lhs = lax.dynamic_slice_in_dim(normed, start, half_rows, 1)
                part = jnp.dot(lhs, p[:half_rows], preferred_element_type=jnp.float32)
                total = part if total is None else total + part
    adapter_pieces = [jnp.stack(a) for a in adapter_steps]

    picked = prompt_adapter[0]
    prompt_count = picked.shape[0]
    a_chip = picked // n_lo
    a_core = picked % n_lo
    a_slot = (a_core != me_core).astype(jnp.int32)
    per_half = []
    piece_ids = jnp.arange(n_chip * n_lo, dtype=jnp.int32)
    for h, direction in enumerate(directions):
        a_step = ((pos - inverse_table[a_chip]) * direction) % n_chip
        one_hot = (a_step[:, None] * n_lo + a_slot[:, None] == piece_ids[None, :]).astype(
            jnp.bfloat16
        )
        stacked = adapter_pieces[h].reshape((n_chip * n_lo,) + adapter_pieces[h].shape[2:])
        per_half.append(
            jnp.einsum("pk,krc->prc", one_hot, stacked, preferred_element_type=jnp.float32).astype(
                jnp.bfloat16
            )
        )
    up_query_selected = jnp.concatenate(
        [per_half[0][:, dh : dh + uh], per_half[1][:, dh : dh + uh]], axis=1
    ).reshape((prompt_count,) + adapter_up_query.shape[1:])
    up_pair_selected = jnp.concatenate(
        [per_half[0][:, dh + uh : piece_rows], per_half[1][:, dh + uh : piece_rows]], axis=1
    ).reshape((prompt_count,) + adapter_up_keyvalue.shape[1:])

    query_plain = total[:, :query_cols]
    base_pair = total[:, query_cols:]

    lengths = packed_lengths[0]
    member, position, owner, slot_index = layout(lengths, row_number)
    rank_size = adapter_down.shape[2]
    halves_value = []
    for h in range(2):
        value = None
        for q in range(quarters):
            maps = per_half[h][:, q * half_maps : (q + 1) * half_maps]
            term = lax.dot_general(
                normed_part[:, q * query_cols : (q + 1) * query_cols],
                maps.reshape(prompt_count * half_maps, query_cols),
                (((1,), (1,)), ((), ())),
                preferred_element_type=jnp.float32,
            ).reshape(row_number, prompt_count, half_maps)
            value = term if value is None else value + term
        halves_value.append(value)
    partial_value = jnp.concatenate(halves_value, axis=2)
    partial_value = partial_value.reshape(row_number, prompt_count, 3, rank_size)
    masked = jnp.sum(partial_value * member[:, :, None, None], axis=1).reshape(
        row_number, 3 * rank_size
    )
    low_rank = sum_blk(masked, n_blk).reshape(row_number, 3, rank_size).astype(jnp.bfloat16)
    low_float = low_rank.astype(jnp.float32)

    def spread(column):
        return (
            (member[:, :, None] * low_float[:, None, column, :])
            .astype(jnp.bfloat16)
            .reshape(row_number, prompt_count * rank_size)
        )

    up_keyvalue_selected = up_pair_selected.reshape(
        prompt_count, rank_size, KEYVALUE_LOCAL, 2, HEAD_WIDTH
    )
    query_update = jnp.dot(
        spread(0),
        up_query_selected.reshape(prompt_count * rank_size, query_cols),
        preferred_element_type=jnp.float32,
    )
    key_update = jnp.dot(
        spread(1),
        up_keyvalue_selected[:, :, :, 0].reshape(
            prompt_count * rank_size, KEYVALUE_LOCAL * HEAD_WIDTH
        ),
        preferred_element_type=jnp.float32,
    )
    value_update = jnp.dot(
        spread(2),
        up_keyvalue_selected[:, :, :, 1].reshape(
            prompt_count * rank_size, KEYVALUE_LOCAL * HEAD_WIDTH
        ),
        preferred_element_type=jnp.float32,
    )
    cosine_table, sine_table = rope_tables(position, HEAD_WIDTH)
    query_complete = (query_plain + adapter_scale * query_update).reshape(
        row_number, QUERY_LOCAL * KEYVALUE_LOCAL, HEAD_WIDTH
    )
    query_states = apply_rotation(query_complete, cosine_table, sine_table).astype(jnp.bfloat16)
    keyvalue_plain = base_pair.reshape(row_number, KEYVALUE_LOCAL, 2, HEAD_WIDTH)
    key_vectors = apply_rotation(
        keyvalue_plain[:, :, 0]
        + adapter_scale * key_update.reshape(row_number, KEYVALUE_LOCAL, HEAD_WIDTH),
        cosine_table,
        sine_table,
    ).astype(jnp.bfloat16)
    value_vectors = (
        keyvalue_plain[:, :, 1]
        + adapter_scale * value_update.reshape(row_number, KEYVALUE_LOCAL, HEAD_WIDTH)
    ).astype(jnp.bfloat16)
    grouped = query_states.reshape(row_number, KEYVALUE_LOCAL, QUERY_LOCAL, HEAD_WIDTH)
    scores = jnp.einsum(
        "tkgc,skc->kgts", grouped, key_vectors, preferred_element_type=jnp.float32
    ) / math.sqrt(HEAD_WIDTH)
    allowed = (owner[:, None] == owner[None, :]) & (slot_index[None, :] <= slot_index[:, None])
    scores = jnp.where(allowed[None, None], scores, -1e30)
    row_max = jnp.max(scores, axis=-1, keepdims=True)
    exponent = jnp.exp(scores - row_max)
    attend = (exponent / jnp.sum(exponent, axis=-1, keepdims=True)).astype(jnp.bfloat16)
    context = jnp.einsum(
        "kgts,skc->tkgc", attend, value_vectors, preferred_element_type=jnp.float32
    ).astype(jnp.bfloat16)
    return (
        context.reshape(row_number, KEYVALUE_LOCAL * QUERY_LOCAL * HEAD_WIDTH),
        key_vectors.reshape(row_number, KEYVALUE_LOCAL * HEAD_WIDTH),
        value_vectors.reshape(row_number, KEYVALUE_LOCAL * HEAD_WIDTH),
    )


def solution(mesh):
    n_blk = mesh.shape["blk"]
    n_req = mesh.shape["req"]
    n_lo = 2 if n_req % 2 == 0 else 1
    devices = mesh.devices.reshape(n_blk, n_req // n_lo, n_lo)
    split_mesh = Mesh(devices, ("blk", "chip", "core"))
    req = ("chip", "core")
    in_specs = (
        P(req, "blk"),
        P(),
        P(req, "blk"),
        P(req, "blk"),
        P(req, None, None, "blk"),
        P(req, None, "blk"),
        P(req, None, "blk"),
        P(req, None),
        P(req, None),
    )
    out_specs = (P(req, "blk"), P(req, "blk"), P(req, "blk"))
    return jax.shard_map(
        shards, mesh=split_mesh, in_specs=in_specs, out_specs=out_specs, check_vma=False
    )
```

```python
import math

import jax
import jax.numpy as jnp
from jax import lax
from jax.sharding import Mesh
from jax.sharding import PartitionSpec as P

HEAD_WIDTH = 128
QUERY_LOCAL = 8
KEYVALUE_LOCAL = 1


epsilon = 1e-05
adapter_scale = 2.0
rope_base = 10000.0


def apply_rotation(vectors, cosine_table, sine_table):
    half_size = vectors.shape[-1] // 2
    first_half = vectors[..., :half_size]
    second_half = vectors[..., half_size:]
    turned = jnp.concatenate([-second_half, first_half], axis=-1)
    return vectors * cosine_table + turned * sine_table


def layout(lengths, count):
    slot_index = jnp.arange(count, dtype=jnp.int32)
    prompt_ends = jnp.cumsum(lengths)
    prompt_starts = prompt_ends - lengths
    member = (slot_index[:, None] >= prompt_starts[None, :]) & (
        slot_index[:, None] < prompt_ends[None, :]
    )
    position = jnp.sum(jnp.where(member, slot_index[:, None] - prompt_starts[None, :], 0), axis=1)
    owner = jnp.sum((slot_index[:, None] >= prompt_ends[None, :]).astype(jnp.int32), axis=1)
    return (member.astype(jnp.float32), position, owner, slot_index)


def rope_tables(position, head_size):
    frequency = rope_base ** (-(jnp.arange(head_size // 2, dtype=jnp.float32) * 2.0 / head_size))
    angles = position.astype(jnp.float32)[:, None] * frequency[None, :]
    cosine_table = jnp.cos(angles)
    sine_table = jnp.sin(angles)
    return (
        jnp.concatenate([cosine_table, cosine_table], 1)[:, None, :],
        jnp.concatenate([sine_table, sine_table], 1)[:, None, :],
    )


def gather_blk(piece, n_blk):
    me = lax.axis_index("blk")
    received = [piece]
    for shift in range(1, n_blk):
        pairs = [(i, (i + shift) % n_blk) for i in range(n_blk)]
        received.append(lax.ppermute(piece, "blk", pairs))
    ordered = []
    for source in range(n_blk):
        pick = (me - source) % n_blk
        ordered.append(lax.switch(pick, [lambda s=s: received[s] for s in range(n_blk)]))
    return ordered


def sum_blk(piece, n_blk):
    if n_blk == 2:
        return piece + lax.ppermute(piece, "blk", [(0, 1), (1, 0)])
    return lax.psum(piece, "blk")


def ring_order(count):
    if count % 2 == 0 and count > 2:
        return list(range(0, count, 2)) + list(range(count - 1, 0, -2))
    return list(range(count))


def ring_gather(piece, count, order, direction):
    pairs = [(order[i], order[(i + direction) % count]) for i in range(count)]
    received = [piece]
    current = piece
    for _ in range(count - 1):
        current = lax.ppermute(current, "chip", pairs)
        received.append(current)
    return received


def shards(
    hidden,
    input_norm_gain,
    query_weight,
    keyvalue_weight,
    adapter_down,
    adapter_up_query,
    adapter_up_keyvalue,
    packed_lengths,
    prompt_adapter,
):
    n_blk = lax.axis_size("blk")
    n_lo = lax.axis_size("core")
    n_chip = lax.axis_size("chip")
    row_number, feature_cols = hidden.shape
    full_width = feature_cols * n_blk
    me_blk = lax.axis_index("blk")
    me_core = lax.axis_index("core")
    me_chip = lax.axis_index("chip")

    if n_blk == 2:
        other = lax.ppermute(hidden, "blk", [(0, 1), (1, 0)])
        halves = [lax.select(me_blk == 0, hidden, other), lax.select(me_blk == 0, other, hidden)]
    else:
        halves = gather_blk(hidden, n_blk)
    full_hidden = jnp.concatenate(halves, axis=1)
    values = full_hidden.astype(jnp.float32)
    squares = jnp.sum(values * values, axis=1)
    factor = lax.rsqrt(squares / full_width + epsilon)
    normed = (values * factor[:, None] * input_norm_gain[None, :]).astype(jnp.bfloat16)
    normed_part = lax.dynamic_slice_in_dim(normed, me_blk * feature_cols, feature_cols, 1)

    weight_rows = query_weight.shape[0]
    query_cols = query_weight.shape[1]
    pair_cols = keyvalue_weight.shape[1]
    half_rows = weight_rows // 2

    weights = jnp.concatenate([query_weight, keyvalue_weight], axis=1)
    down_rows = adapter_down.size // query_cols
    upq_rows = adapter_up_query.size // query_cols
    upkv_rows = adapter_up_keyvalue.size // query_cols
    down_flat = adapter_down.reshape(down_rows, query_cols)
    upq_flat = adapter_up_query.reshape(upq_rows, query_cols)
    upkv_flat = adapter_up_keyvalue.reshape(upkv_rows, query_cols)
    dh, uh, vh = down_rows // 2, upq_rows // 2, upkv_rows // 2
    piece_rows = dh + uh + vh
    pad_rows = (-piece_rows) % 8

    def adapter_half(h):
        return jnp.concatenate(
            [
                down_flat[h * dh : (h + 1) * dh],
                upq_flat[h * uh : (h + 1) * uh],
                upkv_flat[h * vh : (h + 1) * vh],
                jnp.zeros((pad_rows, query_cols), jnp.bfloat16),
            ]
        )

    order = ring_order(n_chip)
    inverse = [0] * n_chip
    for i, c in enumerate(order):
        inverse[c] = i
    order_table = jnp.asarray(order, jnp.int32)
    inverse_table = jnp.asarray(inverse, jnp.int32)
    pos = inverse_table[me_chip]
    directions = (1, -1)

    def swap_core(x):
        if n_lo == 1:
            return [x]
        return [x, lax.ppermute(x, "core", [(0, 1), (1, 0)])]

    pair_width = query_cols + pair_cols
    recv = []
    for h, direction in enumerate(directions):
        adapters_padded = jnp.pad(adapter_half(h), ((0, 0), (0, pair_width - query_cols)))
        piece = jnp.concatenate(
            [weights[h * half_rows : (h + 1) * half_rows], adapters_padded], axis=0
        )
        recv.append(ring_gather(piece, n_chip, order, direction))

    total = None
    adapter_steps = [[], []]
    for s in range(n_chip):
        for h, direction in enumerate(directions):
            src_chip = order_table[(pos - s * direction) % n_chip]
            both = swap_core(recv[h][s])
            adapter_steps[h].append([p[half_rows:, :query_cols] for p in both])
            for slot, p in enumerate(both):
                src_core = me_core if slot == 0 else n_lo - 1 - me_core
                start = (src_chip * n_lo + src_core) * weight_rows + h * half_rows
                lhs = lax.dynamic_slice_in_dim(normed, start, half_rows, 1)
                part = jnp.dot(lhs, p[:half_rows], preferred_element_type=jnp.float32)
                total = part if total is None else total + part

    picked = prompt_adapter[0]
    prompt_count = picked.shape[0]
    a_chip = picked // n_lo
    a_core = picked % n_lo
    a_slot = (a_core != me_core).astype(jnp.int32)
    per_half = []
    for h, direction in enumerate(directions):
        a_step = ((pos - inverse_table[a_chip]) * direction) % n_chip
        picked_piece = a_step * n_lo + a_slot
        chosen = None
        for s in range(n_chip):
            for slot in range(n_lo):
                weight = (picked_piece == s * n_lo + slot).astype(jnp.float32)[:, None, None]
                term = weight * adapter_steps[h][s][slot].astype(jnp.float32)[None]
                chosen = term if chosen is None else chosen + term
        per_half.append(chosen.astype(jnp.bfloat16))
    down_selected = jnp.concatenate(
        [per_half[0][:, :dh], per_half[1][:, :dh]], axis=1
    ).reshape((prompt_count,) + adapter_down.shape[1:])
    up_query_selected = jnp.concatenate(
        [per_half[0][:, dh : dh + uh], per_half[1][:, dh : dh + uh]], axis=1
    ).reshape((prompt_count,) + adapter_up_query.shape[1:])
    up_pair_selected = jnp.concatenate(
        [per_half[0][:, dh + uh : piece_rows], per_half[1][:, dh + uh : piece_rows]], axis=1
    ).reshape((prompt_count,) + adapter_up_keyvalue.shape[1:])

    query_plain = total[:, :query_cols]
    base_pair = total[:, query_cols:]

    lengths = packed_lengths[0]
    member, position, owner, slot_index = layout(lengths, row_number)
    rank_size = down_selected.shape[2]
    partial_value = lax.dot_general(
        normed_part,
        down_selected.reshape(prompt_count * 3 * rank_size, feature_cols),
        (((1,), (1,)), ((), ())),
        preferred_element_type=jnp.float32,
    )
    partial_value = partial_value.reshape(row_number, prompt_count, 3, rank_size)
    masked = jnp.sum(partial_value * member[:, :, None, None], axis=1).reshape(
        row_number, 3 * rank_size
    )
    low_rank = sum_blk(masked, n_blk).reshape(row_number, 3, rank_size).astype(jnp.bfloat16)
    low_float = low_rank.astype(jnp.float32)

    def spread(column):
        return (
            (member[:, :, None] * low_float[:, None, column, :])
            .astype(jnp.bfloat16)
            .reshape(row_number, prompt_count * rank_size)
        )

    up_keyvalue_selected = up_pair_selected.reshape(
        prompt_count, rank_size, KEYVALUE_LOCAL, 2, HEAD_WIDTH
    )
    query_update = jnp.dot(
        spread(0),
        up_query_selected.reshape(prompt_count * rank_size, query_cols),
        preferred_element_type=jnp.float32,
    )
    key_update = jnp.dot(
        spread(1),
        up_keyvalue_selected[:, :, :, 0].reshape(
            prompt_count * rank_size, KEYVALUE_LOCAL * HEAD_WIDTH
        ),
        preferred_element_type=jnp.float32,
    )
    value_update = jnp.dot(
        spread(2),
        up_keyvalue_selected[:, :, :, 1].reshape(
            prompt_count * rank_size, KEYVALUE_LOCAL * HEAD_WIDTH
        ),
        preferred_element_type=jnp.float32,
    )
    cosine_table, sine_table = rope_tables(position, HEAD_WIDTH)
    query_complete = (query_plain + adapter_scale * query_update).reshape(
        row_number, QUERY_LOCAL * KEYVALUE_LOCAL, HEAD_WIDTH
    )
    query_states = apply_rotation(query_complete, cosine_table, sine_table).astype(jnp.bfloat16)
    keyvalue_plain = base_pair.reshape(row_number, KEYVALUE_LOCAL, 2, HEAD_WIDTH)
    key_vectors = apply_rotation(
        keyvalue_plain[:, :, 0]
        + adapter_scale * key_update.reshape(row_number, KEYVALUE_LOCAL, HEAD_WIDTH),
        cosine_table,
        sine_table,
    ).astype(jnp.bfloat16)
    value_vectors = (
        keyvalue_plain[:, :, 1]
        + adapter_scale * value_update.reshape(row_number, KEYVALUE_LOCAL, HEAD_WIDTH)
    ).astype(jnp.bfloat16)
    grouped = query_states.reshape(row_number, KEYVALUE_LOCAL, QUERY_LOCAL, HEAD_WIDTH)
    scores = jnp.einsum(
        "tkgc,skc->kgts", grouped, key_vectors, preferred_element_type=jnp.float32
    ) / math.sqrt(HEAD_WIDTH)
    allowed = (owner[:, None] == owner[None, :]) & (slot_index[None, :] <= slot_index[:, None])
    scores = jnp.where(allowed[None, None], scores, -1e30)
    row_max = jnp.max(scores, axis=-1, keepdims=True)
    exponent = jnp.exp(scores - row_max)
    attend = (exponent / jnp.sum(exponent, axis=-1, keepdims=True)).astype(jnp.bfloat16)
    context = jnp.einsum(
        "kgts,skc->tkgc", attend, value_vectors, preferred_element_type=jnp.float32
    ).astype(jnp.bfloat16)
    return (
        context.reshape(row_number, KEYVALUE_LOCAL * QUERY_LOCAL * HEAD_WIDTH),
        key_vectors.reshape(row_number, KEYVALUE_LOCAL * HEAD_WIDTH),
        value_vectors.reshape(row_number, KEYVALUE_LOCAL * HEAD_WIDTH),
    )


def solution(mesh):
    n_blk = mesh.shape["blk"]
    n_req = mesh.shape["req"]
    n_lo = 2 if n_req % 2 == 0 else 1
    devices = mesh.devices.reshape(n_blk, n_req // n_lo, n_lo)
    split_mesh = Mesh(devices, ("blk", "chip", "core"))
    req = ("chip", "core")
    in_specs = (
        P(req, "blk"),
        P(),
        P(req, "blk"),
        P(req, "blk"),
        P(req, None, None, "blk"),
        P(req, None, "blk"),
        P(req, None, "blk"),
        P(req, None),
        P(req, None),
    )
    out_specs = (P(req, "blk"), P(req, "blk"), P(req, "blk"))
    return jax.shard_map(
        shards, mesh=split_mesh, in_specs=in_specs, out_specs=out_specs, check_vma=False
    )
```

```python
import math

import jax
import jax.numpy as jnp
from jax import lax
from jax.sharding import Mesh
from jax.sharding import PartitionSpec as P

HEAD_WIDTH = 128
QUERY_LOCAL = 8
KEYVALUE_LOCAL = 1


epsilon = 1e-05
adapter_scale = 2.0
rope_base = 10000.0


def apply_rotation(vectors, cosine_table, sine_table):
    half_size = vectors.shape[-1] // 2
    first_half = vectors[..., :half_size]
    second_half = vectors[..., half_size:]
    turned = jnp.concatenate([-second_half, first_half], axis=-1)
    return vectors * cosine_table + turned * sine_table


def layout(lengths, count):
    slot_index = jnp.arange(count, dtype=jnp.int32)
    prompt_ends = jnp.cumsum(lengths)
    prompt_starts = prompt_ends - lengths
    member = (slot_index[:, None] >= prompt_starts[None, :]) & (
        slot_index[:, None] < prompt_ends[None, :]
    )
    position = jnp.sum(jnp.where(member, slot_index[:, None] - prompt_starts[None, :], 0), axis=1)
    owner = jnp.sum((slot_index[:, None] >= prompt_ends[None, :]).astype(jnp.int32), axis=1)
    return (member.astype(jnp.float32), position, owner, slot_index)


def rope_tables(position, head_size):
    frequency = rope_base ** (-(jnp.arange(head_size // 2, dtype=jnp.float32) * 2.0 / head_size))
    angles = position.astype(jnp.float32)[:, None] * frequency[None, :]
    cosine_table = jnp.cos(angles)
    sine_table = jnp.sin(angles)
    return (
        jnp.concatenate([cosine_table, cosine_table], 1)[:, None, :],
        jnp.concatenate([sine_table, sine_table], 1)[:, None, :],
    )


def gather_blk(piece, n_blk):
    me = lax.axis_index("blk")
    received = [piece]
    for shift in range(1, n_blk):
        pairs = [(i, (i + shift) % n_blk) for i in range(n_blk)]
        received.append(lax.ppermute(piece, "blk", pairs))
    ordered = []
    for source in range(n_blk):
        pick = (me - source) % n_blk
        ordered.append(lax.switch(pick, [lambda s=s: received[s] for s in range(n_blk)]))
    return ordered


def sum_blk(piece, n_blk):
    if n_blk == 2:
        return piece + lax.ppermute(piece, "blk", [(0, 1), (1, 0)])
    return lax.psum(piece, "blk")


def ring_order(count):
    if count % 2 == 0 and count > 2:
        return list(range(0, count, 2)) + list(range(count - 1, 0, -2))
    return list(range(count))


def ring_gather(piece, count, order, direction):
    pairs = [(order[i], order[(i + direction) % count]) for i in range(count)]
    received = [piece]
    current = piece
    for _ in range(count - 1):
        current = lax.ppermute(current, "chip", pairs)
        received.append(current)
    return received


def shards(
    hidden,
    input_norm_gain,
    query_weight,
    keyvalue_weight,
    adapter_down,
    adapter_up_query,
    adapter_up_keyvalue,
    packed_lengths,
    prompt_adapter,
):
    n_blk = lax.axis_size("blk")
    n_lo = lax.axis_size("core")
    n_chip = lax.axis_size("chip")
    row_number, feature_cols = hidden.shape
    full_width = feature_cols * n_blk
    me_blk = lax.axis_index("blk")
    me_core = lax.axis_index("core")
    me_chip = lax.axis_index("chip")

    if n_blk == 2:
        other = lax.ppermute(hidden, "blk", [(0, 1), (1, 0)])
        halves = [lax.select(me_blk == 0, hidden, other), lax.select(me_blk == 0, other, hidden)]
    else:
        halves = gather_blk(hidden, n_blk)
    full_hidden = jnp.concatenate(halves, axis=1)
    values = full_hidden.astype(jnp.float32)
    squares = jnp.sum(values * values, axis=1)
    factor = lax.rsqrt(squares / full_width + epsilon)
    normed = (values * factor[:, None] * input_norm_gain[None, :]).astype(jnp.bfloat16)
    normed_part = lax.dynamic_slice_in_dim(normed, me_blk * feature_cols, feature_cols, 1)

    weight_rows = query_weight.shape[0]
    query_cols = query_weight.shape[1]
    pair_cols = keyvalue_weight.shape[1]
    half_rows = weight_rows // 2

    weights = jnp.concatenate([query_weight, keyvalue_weight], axis=1)
    down_rows = adapter_down.size // query_cols
    upq_rows = adapter_up_query.size // query_cols
    upkv_rows = adapter_up_keyvalue.size // query_cols
    down_flat = adapter_down.reshape(down_rows, query_cols)
    upq_flat = adapter_up_query.reshape(upq_rows, query_cols)
    upkv_flat = adapter_up_keyvalue.reshape(upkv_rows, query_cols)
    dh, uh, vh = down_rows // 2, upq_rows // 2, upkv_rows // 2
    piece_rows = dh + uh + vh
    pad_rows = (-piece_rows) % 8

    def adapter_half(h):
        return jnp.concatenate(
            [
                down_flat[h * dh : (h + 1) * dh],
                upq_flat[h * uh : (h + 1) * uh],
                upkv_flat[h * vh : (h + 1) * vh],
                jnp.zeros((pad_rows, query_cols), jnp.bfloat16),
            ]
        )

    order = ring_order(n_chip)
    inverse = [0] * n_chip
    for i, c in enumerate(order):
        inverse[c] = i
    order_table = jnp.asarray(order, jnp.int32)
    inverse_table = jnp.asarray(inverse, jnp.int32)
    pos = inverse_table[me_chip]
    directions = (1, -1)

    def swap_core(x):
        if n_lo == 1:
            return [x]
        return [x, lax.ppermute(x, "core", [(0, 1), (1, 0)])]

    pair_width = query_cols + pair_cols
    recv = []
    for h, direction in enumerate(directions):
        adapters_padded = jnp.pad(adapter_half(h), ((0, 0), (0, pair_width - query_cols)))
        piece = jnp.concatenate(
            [weights[h * half_rows : (h + 1) * half_rows], adapters_padded], axis=0
        )
        recv.append(ring_gather(piece, n_chip, order, direction))

    total = None
    adapter_steps = [[], []]
    for s in range(n_chip):
        for h, direction in enumerate(directions):
            src_chip = order_table[(pos - s * direction) % n_chip]
            both = swap_core(recv[h][s])
            adapter_steps[h].append([p[half_rows:, :query_cols] for p in both])
            for slot, p in enumerate(both):
                src_core = me_core if slot == 0 else n_lo - 1 - me_core
                start = (src_chip * n_lo + src_core) * weight_rows + h * half_rows
                lhs = lax.dynamic_slice_in_dim(normed, start, half_rows, 1)
                part = jnp.dot(lhs, p[:half_rows], preferred_element_type=jnp.float32)
                total = part if total is None else total + part

    picked = prompt_adapter[0]
    prompt_count = picked.shape[0]
    a_chip = picked // n_lo
    a_core = picked % n_lo
    a_slot = (a_core != me_core).astype(jnp.int32)
    per_half = []
    for h, direction in enumerate(directions):
        a_step = ((pos - inverse_table[a_chip]) * direction) % n_chip
        picked_piece = a_step * n_lo + a_slot
        chosen = None
        for s in range(n_chip):
            for slot in range(n_lo):
                weight = (picked_piece == s * n_lo + slot).astype(jnp.float32)[:, None, None]
                term = weight * adapter_steps[h][s][slot].astype(jnp.float32)[None]
                chosen = term if chosen is None else chosen + term
        per_half.append(chosen.astype(jnp.bfloat16))
    up_query_selected = jnp.concatenate(
        [per_half[0][:, dh : dh + uh], per_half[1][:, dh : dh + uh]], axis=1
    ).reshape((prompt_count,) + adapter_up_query.shape[1:])
    up_pair_selected = jnp.concatenate(
        [per_half[0][:, dh + uh : piece_rows], per_half[1][:, dh + uh : piece_rows]], axis=1
    ).reshape((prompt_count,) + adapter_up_keyvalue.shape[1:])

    query_plain = total[:, :query_cols]
    base_pair = total[:, query_cols:]

    lengths = packed_lengths[0]
    member, position, owner, slot_index = layout(lengths, row_number)
    rank_size = adapter_down.shape[2]
    half_maps = adapter_down.size // feature_cols // 2
    partial_value = jnp.concatenate(
        [
            lax.dot_general(
                normed_part,
                per_half[h][:, :dh].reshape(prompt_count * half_maps, feature_cols),
                (((1,), (1,)), ((), ())),
                preferred_element_type=jnp.float32,
            ).reshape(row_number, prompt_count, half_maps)
            for h in range(2)
        ],
        axis=2,
    )
    partial_value = partial_value.reshape(row_number, prompt_count, 3, rank_size)
    masked = jnp.sum(partial_value * member[:, :, None, None], axis=1).reshape(
        row_number, 3 * rank_size
    )
    low_rank = sum_blk(masked, n_blk).reshape(row_number, 3, rank_size).astype(jnp.bfloat16)
    low_float = low_rank.astype(jnp.float32)

    def spread(column):
        return (
            (member[:, :, None] * low_float[:, None, column, :])
            .astype(jnp.bfloat16)
            .reshape(row_number, prompt_count * rank_size)
        )

    up_keyvalue_selected = up_pair_selected.reshape(
        prompt_count, rank_size, KEYVALUE_LOCAL, 2, HEAD_WIDTH
    )
    query_update = jnp.dot(
        spread(0),
        up_query_selected.reshape(prompt_count * rank_size, query_cols),
        preferred_element_type=jnp.float32,
    )
    key_update = jnp.dot(
        spread(1),
        up_keyvalue_selected[:, :, :, 0].reshape(
            prompt_count * rank_size, KEYVALUE_LOCAL * HEAD_WIDTH
        ),
        preferred_element_type=jnp.float32,
    )
    value_update = jnp.dot(
        spread(2),
        up_keyvalue_selected[:, :, :, 1].reshape(
            prompt_count * rank_size, KEYVALUE_LOCAL * HEAD_WIDTH
        ),
        preferred_element_type=jnp.float32,
    )
    cosine_table, sine_table = rope_tables(position, HEAD_WIDTH)
    query_complete = (query_plain + adapter_scale * query_update).reshape(
        row_number, QUERY_LOCAL * KEYVALUE_LOCAL, HEAD_WIDTH
    )
    query_states = apply_rotation(query_complete, cosine_table, sine_table).astype(jnp.bfloat16)
    keyvalue_plain = base_pair.reshape(row_number, KEYVALUE_LOCAL, 2, HEAD_WIDTH)
    key_vectors = apply_rotation(
        keyvalue_plain[:, :, 0]
        + adapter_scale * key_update.reshape(row_number, KEYVALUE_LOCAL, HEAD_WIDTH),
        cosine_table,
        sine_table,
    ).astype(jnp.bfloat16)
    value_vectors = (
        keyvalue_plain[:, :, 1]
        + adapter_scale * value_update.reshape(row_number, KEYVALUE_LOCAL, HEAD_WIDTH)
    ).astype(jnp.bfloat16)
    grouped = query_states.reshape(row_number, KEYVALUE_LOCAL, QUERY_LOCAL, HEAD_WIDTH)
    scores = jnp.einsum(
        "tkgc,skc->kgts", grouped, key_vectors, preferred_element_type=jnp.float32
    ) / math.sqrt(HEAD_WIDTH)
    allowed = (owner[:, None] == owner[None, :]) & (slot_index[None, :] <= slot_index[:, None])
    scores = jnp.where(allowed[None, None], scores, -1e30)
    row_max = jnp.max(scores, axis=-1, keepdims=True)
    exponent = jnp.exp(scores - row_max)
    attend = (exponent / jnp.sum(exponent, axis=-1, keepdims=True)).astype(jnp.bfloat16)
    context = jnp.einsum(
        "kgts,skc->tkgc", attend, value_vectors, preferred_element_type=jnp.float32
    ).astype(jnp.bfloat16)
    return (
        context.reshape(row_number, KEYVALUE_LOCAL * QUERY_LOCAL * HEAD_WIDTH),
        key_vectors.reshape(row_number, KEYVALUE_LOCAL * HEAD_WIDTH),
        value_vectors.reshape(row_number, KEYVALUE_LOCAL * HEAD_WIDTH),
    )


def solution(mesh):
    n_blk = mesh.shape["blk"]
    n_req = mesh.shape["req"]
    n_lo = 2 if n_req % 2 == 0 else 1
    devices = mesh.devices.reshape(n_blk, n_req // n_lo, n_lo)
    split_mesh = Mesh(devices, ("blk", "chip", "core"))
    req = ("chip", "core")
    in_specs = (
        P(req, "blk"),
        P(),
        P(req, "blk"),
        P(req, "blk"),
        P(req, None, None, "blk"),
        P(req, None, "blk"),
        P(req, None, "blk"),
        P(req, None),
        P(req, None),
    )
    out_specs = (P(req, "blk"), P(req, "blk"), P(req, "blk"))
    return jax.shard_map(
        shards, mesh=split_mesh, in_specs=in_specs, out_specs=out_specs, check_vma=False
    )
```

```python
import math

import jax
import jax.numpy as jnp
from jax import lax
from jax.sharding import Mesh
from jax.sharding import PartitionSpec as P

HEAD_WIDTH = 128
QUERY_LOCAL = 8
KEYVALUE_LOCAL = 1


epsilon = 1e-05
adapter_scale = 2.0
rope_base = 10000.0


def apply_rotation(vectors, cosine_table, sine_table):
    half_size = vectors.shape[-1] // 2
    first_half = vectors[..., :half_size]
    second_half = vectors[..., half_size:]
    turned = jnp.concatenate([-second_half, first_half], axis=-1)
    return vectors * cosine_table + turned * sine_table


def layout(lengths, count):
    slot_index = jnp.arange(count, dtype=jnp.int32)
    prompt_ends = jnp.cumsum(lengths)
    prompt_starts = prompt_ends - lengths
    member = (slot_index[:, None] >= prompt_starts[None, :]) & (
        slot_index[:, None] < prompt_ends[None, :]
    )
    position = jnp.sum(jnp.where(member, slot_index[:, None] - prompt_starts[None, :], 0), axis=1)
    owner = jnp.sum((slot_index[:, None] >= prompt_ends[None, :]).astype(jnp.int32), axis=1)
    return (member.astype(jnp.float32), position, owner, slot_index)


def rope_tables(position, head_size):
    frequency = rope_base ** (-(jnp.arange(head_size // 2, dtype=jnp.float32) * 2.0 / head_size))
    angles = position.astype(jnp.float32)[:, None] * frequency[None, :]
    cosine_table = jnp.cos(angles)
    sine_table = jnp.sin(angles)
    return (
        jnp.concatenate([cosine_table, cosine_table], 1)[:, None, :],
        jnp.concatenate([sine_table, sine_table], 1)[:, None, :],
    )


def gather_blk(piece, n_blk):
    me = lax.axis_index("blk")
    received = [piece]
    for shift in range(1, n_blk):
        pairs = [(i, (i + shift) % n_blk) for i in range(n_blk)]
        received.append(lax.ppermute(piece, "blk", pairs))
    ordered = []
    for source in range(n_blk):
        pick = (me - source) % n_blk
        ordered.append(lax.switch(pick, [lambda s=s: received[s] for s in range(n_blk)]))
    return ordered


def sum_blk(piece, n_blk):
    if n_blk == 2:
        return piece + lax.ppermute(piece, "blk", [(0, 1), (1, 0)])
    return lax.psum(piece, "blk")


def ring_order(count):
    if count % 2 == 0 and count > 2:
        return list(range(0, count, 2)) + list(range(count - 1, 0, -2))
    return list(range(count))


def ring_gather(piece, count, order, direction):
    pairs = [(order[i], order[(i + direction) % count]) for i in range(count)]
    received = [piece]
    current = piece
    for _ in range(count - 1):
        current = lax.ppermute(current, "chip", pairs)
        received.append(current)
    return received


def shards(
    hidden,
    input_norm_gain,
    query_weight,
    keyvalue_weight,
    adapter_down,
    adapter_up_query,
    adapter_up_keyvalue,
    packed_lengths,
    prompt_adapter,
):
    n_blk = lax.axis_size("blk")
    n_lo = lax.axis_size("core")
    n_chip = lax.axis_size("chip")
    row_number, feature_cols = hidden.shape
    full_width = feature_cols * n_blk
    me_blk = lax.axis_index("blk")
    me_core = lax.axis_index("core")
    me_chip = lax.axis_index("chip")

    if n_blk == 2:
        other = lax.ppermute(hidden, "blk", [(0, 1), (1, 0)])
        halves = [lax.select(me_blk == 0, hidden, other), lax.select(me_blk == 0, other, hidden)]
    else:
        halves = gather_blk(hidden, n_blk)
    full_hidden = jnp.concatenate(halves, axis=1)
    values = full_hidden.astype(jnp.float32)
    squares = jnp.sum(values * values, axis=1)
    factor = lax.rsqrt(squares / full_width + epsilon)
    normed = (values * factor[:, None] * input_norm_gain[None, :]).astype(jnp.bfloat16)
    normed_part = lax.dynamic_slice_in_dim(normed, me_blk * feature_cols, feature_cols, 1)

    weight_rows = query_weight.shape[0]
    query_cols = query_weight.shape[1]
    pair_cols = keyvalue_weight.shape[1]
    half_rows = weight_rows // 2

    weights = jnp.concatenate([query_weight, keyvalue_weight], axis=1)
    down_rows = adapter_down.size // query_cols
    upq_rows = adapter_up_query.size // query_cols
    upkv_rows = adapter_up_keyvalue.size // query_cols
    down_flat = adapter_down.reshape(down_rows, query_cols)
    upq_flat = adapter_up_query.reshape(upq_rows, query_cols)
    upkv_flat = adapter_up_keyvalue.reshape(upkv_rows, query_cols)
    dh, uh, vh = down_rows // 2, upq_rows // 2, upkv_rows // 2
    piece_rows = dh + uh + vh
    pad_rows = (-piece_rows) % 8

    def adapter_half(h):
        return jnp.concatenate(
            [
                down_flat[h * dh : (h + 1) * dh],
                upq_flat[h * uh : (h + 1) * uh],
                upkv_flat[h * vh : (h + 1) * vh],
                jnp.zeros((pad_rows, query_cols), jnp.bfloat16),
            ]
        )

    order = ring_order(n_chip)
    inverse = [0] * n_chip
    for i, c in enumerate(order):
        inverse[c] = i
    order_table = jnp.asarray(order, jnp.int32)
    inverse_table = jnp.asarray(inverse, jnp.int32)
    pos = inverse_table[me_chip]
    directions = (1, -1)

    def swap_core(x):
        if n_lo == 1:
            return [x]
        return [x, lax.ppermute(x, "core", [(0, 1), (1, 0)])]

    pair_width = query_cols + pair_cols
    recv = []
    for h, direction in enumerate(directions):
        adapters_padded = jnp.pad(adapter_half(h), ((0, 0), (0, pair_width - query_cols)))
        piece = jnp.concatenate(
            [weights[h * half_rows : (h + 1) * half_rows], adapters_padded], axis=0
        )
        recv.append(ring_gather(piece, n_chip, order, direction))

    total = None
    adapter_steps = [[], []]
    for s in range(n_chip):
        for h, direction in enumerate(directions):
            src_chip = order_table[(pos - s * direction) % n_chip]
            both = swap_core(recv[h][s])
            adapter_steps[h].append([p[half_rows:, :query_cols] for p in both])
            for slot, p in enumerate(both):
                src_core = me_core if slot == 0 else n_lo - 1 - me_core
                start = (src_chip * n_lo + src_core) * weight_rows + h * half_rows
                lhs = lax.dynamic_slice_in_dim(normed, start, half_rows, 1)
                part = jnp.dot(lhs, p[:half_rows], preferred_element_type=jnp.float32)
                total = part if total is None else total + part

    picked = prompt_adapter[0]
    prompt_count = picked.shape[0]
    a_chip = picked // n_lo
    a_core = picked % n_lo
    a_slot = (a_core != me_core).astype(jnp.int32)
    per_half = []
    for h, direction in enumerate(directions):
        a_step = ((pos - inverse_table[a_chip]) * direction) % n_chip
        picked_piece = a_step * n_lo + a_slot
        chosen = None
        for s in range(n_chip):
            for slot in range(n_lo):
                piece = jnp.broadcast_to(
                    adapter_steps[h][s][slot][None], (prompt_count,) + adapter_steps[h][s][slot].shape
                )
                hit = (picked_piece == s * n_lo + slot)[:, None, None]
                chosen = piece if chosen is None else jnp.where(hit, piece, chosen)
        per_half.append(chosen)
    down_selected = jnp.concatenate(
        [per_half[0][:, :dh], per_half[1][:, :dh]], axis=1
    ).reshape((prompt_count,) + adapter_down.shape[1:])
    up_query_selected = jnp.concatenate(
        [per_half[0][:, dh : dh + uh], per_half[1][:, dh : dh + uh]], axis=1
    ).reshape((prompt_count,) + adapter_up_query.shape[1:])
    up_pair_selected = jnp.concatenate(
        [per_half[0][:, dh + uh : piece_rows], per_half[1][:, dh + uh : piece_rows]], axis=1
    ).reshape((prompt_count,) + adapter_up_keyvalue.shape[1:])

    query_plain = total[:, :query_cols]
    base_pair = total[:, query_cols:]

    lengths = packed_lengths[0]
    member, position, owner, slot_index = layout(lengths, row_number)
    rank_size = down_selected.shape[2]
    partial_value = lax.dot_general(
        normed_part,
        down_selected.reshape(prompt_count * 3 * rank_size, feature_cols),
        (((1,), (1,)), ((), ())),
        preferred_element_type=jnp.float32,
    )
    partial_value = partial_value.reshape(row_number, prompt_count, 3, rank_size)
    masked = jnp.sum(partial_value * member[:, :, None, None], axis=1).reshape(
        row_number, 3 * rank_size
    )
    low_rank = sum_blk(masked, n_blk).reshape(row_number, 3, rank_size).astype(jnp.bfloat16)
    low_float = low_rank.astype(jnp.float32)

    def spread(column):
        return (
            (member[:, :, None] * low_float[:, None, column, :])
            .astype(jnp.bfloat16)
            .reshape(row_number, prompt_count * rank_size)
        )

    up_keyvalue_selected = up_pair_selected.reshape(
        prompt_count, rank_size, KEYVALUE_LOCAL, 2, HEAD_WIDTH
    )
    query_update = jnp.dot(
        spread(0),
        up_query_selected.reshape(prompt_count * rank_size, query_cols),
        preferred_element_type=jnp.float32,
    )
    key_update = jnp.dot(
        spread(1),
        up_keyvalue_selected[:, :, :, 0].reshape(
            prompt_count * rank_size, KEYVALUE_LOCAL * HEAD_WIDTH
        ),
        preferred_element_type=jnp.float32,
    )
    value_update = jnp.dot(
        spread(2),
        up_keyvalue_selected[:, :, :, 1].reshape(
            prompt_count * rank_size, KEYVALUE_LOCAL * HEAD_WIDTH
        ),
        preferred_element_type=jnp.float32,
    )
    cosine_table, sine_table = rope_tables(position, HEAD_WIDTH)
    query_complete = (query_plain + adapter_scale * query_update).reshape(
        row_number, QUERY_LOCAL * KEYVALUE_LOCAL, HEAD_WIDTH
    )
    query_states = apply_rotation(query_complete, cosine_table, sine_table).astype(jnp.bfloat16)
    keyvalue_plain = base_pair.reshape(row_number, KEYVALUE_LOCAL, 2, HEAD_WIDTH)
    key_vectors = apply_rotation(
        keyvalue_plain[:, :, 0]
        + adapter_scale * key_update.reshape(row_number, KEYVALUE_LOCAL, HEAD_WIDTH),
        cosine_table,
        sine_table,
    ).astype(jnp.bfloat16)
    value_vectors = (
        keyvalue_plain[:, :, 1]
        + adapter_scale * value_update.reshape(row_number, KEYVALUE_LOCAL, HEAD_WIDTH)
    ).astype(jnp.bfloat16)
    grouped = query_states.reshape(row_number, KEYVALUE_LOCAL, QUERY_LOCAL, HEAD_WIDTH)
    scores = jnp.einsum(
        "tkgc,skc->kgts", grouped, key_vectors, preferred_element_type=jnp.float32
    ) / math.sqrt(HEAD_WIDTH)
    allowed = (owner[:, None] == owner[None, :]) & (slot_index[None, :] <= slot_index[:, None])
    scores = jnp.where(allowed[None, None], scores, -1e30)
    row_max = jnp.max(scores, axis=-1, keepdims=True)
    exponent = jnp.exp(scores - row_max)
    attend = (exponent / jnp.sum(exponent, axis=-1, keepdims=True)).astype(jnp.bfloat16)
    context = jnp.einsum(
        "kgts,skc->tkgc", attend, value_vectors, preferred_element_type=jnp.float32
    ).astype(jnp.bfloat16)
    return (
        context.reshape(row_number, KEYVALUE_LOCAL * QUERY_LOCAL * HEAD_WIDTH),
        key_vectors.reshape(row_number, KEYVALUE_LOCAL * HEAD_WIDTH),
        value_vectors.reshape(row_number, KEYVALUE_LOCAL * HEAD_WIDTH),
    )


def solution(mesh):
    n_blk = mesh.shape["blk"]
    n_req = mesh.shape["req"]
    n_lo = 2 if n_req % 2 == 0 else 1
    devices = mesh.devices.reshape(n_blk, n_req // n_lo, n_lo)
    split_mesh = Mesh(devices, ("blk", "chip", "core"))
    req = ("chip", "core")
    in_specs = (
        P(req, "blk"),
        P(),
        P(req, "blk"),
        P(req, "blk"),
        P(req, None, None, "blk"),
        P(req, None, "blk"),
        P(req, None, "blk"),
        P(req, None),
        P(req, None),
    )
    out_specs = (P(req, "blk"), P(req, "blk"), P(req, "blk"))
    return jax.shard_map(
        shards, mesh=split_mesh, in_specs=in_specs, out_specs=out_specs, check_vma=False
    )
```
